32 devices in a mesh: layer: 2 (over x), gx: 8 (over z, core), gy: 2 (over y).
Axes of the slice: x: 2, y: 2, z: 4, core: 2. Of those that a mesh axis runs over, the one named last changes fastest.
Arguments:
- prev_vec: float32 [2, 16, 8, 32, 128], P('layer', 'gx', 'gy'), may hold values from -6 to 6
- cur_vec: float32 [2, 16, 8, 32, 128], P('layer', 'gx', 'gy'), may hold values from -6 to 6
- displace: float32 [2, 16, 8, 2, 128], P('layer', 'gx', 'gy'), may hold values from -0.15 to 0.15
- potential: float32 [2, 16, 8, 128], P('layer', 'gx', 'gy'), may hold values from -1.5 to 1.5
Outputs:
- first_term: float32 [2, 16, 8, 32, 128], P('layer', 'gx', 'gy')
- second_term: float32 [2, 16, 8, 32, 128], P('layer', 'gx', 'gy')
The draws below stay inside these ranges and needn't reach their ends.
All inputs are finite; a program needn't handle non-finite values.
Results may differ from the reference program's by a relative error of at most 0.0003.
Values sent between devices are 32-bit elements; how exact they have to be, the bound alone decides.
No kernel may reach another device: no remote copies, remote signals or barrier semaphores. Data moves between devices by JAX's collectives and lax.ppermute only.
A program may use at most 64 MiB of HBM per device.

```python
import math
import jax
import jax.numpy as jnp
from jax import lax

ORB = 128
VECS = 32
PATCH_X = 14
PATCH_Y = 4
NBX = 16
NBY = 8


def shard_levels(key, dims, cuts, least, top_value):
    gain, own = 1.0, jax.random.fold_in(key, 6)
    for dim, blocks in cuts:
        steps = jnp.exp(jax.random.uniform(jax.random.fold_in(own, dim), (blocks,), jnp.float32, least / len(cuts), top_value / len(cuts)))
        gain = gain * jnp.repeat(steps, dims[dim] // blocks).reshape([-1 if axis == dim else 1 for axis in range(len(dims))])
    return gain


def bell_draw(stream_key, shape, width, reach, cuts=(), kind=jnp.bfloat16):
    loudness = shard_levels(stream_key, shape, cuts, -0.22, 0.18) if cuts else 1.0
    entries = jax.random.normal(stream_key, shape, jnp.float32) * width * loudness
    return jnp.minimum(jnp.maximum(entries, -reach), reach).astype(kind)


def setup_inputs(seed: int = 0) -> dict:
    key_of = jax.random.split(jax.random.key(seed), 5)
    prev_vec = bell_draw(key_of[0], (2, NBX, NBY, VECS, ORB), 1.0, 6.0, ((0, 2), (1, 8), (2, 2)), jnp.float32)
    cur_vec = bell_draw(key_of[1], (2, NBX, NBY, VECS, ORB), 1.0, 6.0, ((0, 2), (1, 8), (2, 2)), jnp.float32)
    displace = jnp.clip(jax.random.uniform(key_of[2], (2, NBX, NBY, 2, ORB), jnp.float32, -0.15, 0.15) * shard_levels(key_of[2], (2, NBX, NBY, 2, ORB), ((0, 2), (1, 8), (2, 2)), -0.4, 0.0), -0.15, 0.15)
    potential = jnp.clip(jax.random.uniform(key_of[3], (2, NBX, NBY, ORB), jnp.float32, -1.5, 1.5) * shard_levels(key_of[3], (2, NBX, NBY, ORB), ((0, 2), (1, 8), (2, 2)), -0.4, 0.0), -1.5, 1.5)
    return {"prev_vec": prev_vec, "cur_vec": cur_vec, "displace": displace, "potential": potential}


v_pi = -2.7
v_sigma = 0.48
decay_len = 0.319
layer_gap = 3.35 / 1.42
cut_radius = 3.5
hop_scale = 12.0
twist_angle = 1.05 * math.pi / 180.0
root_three = math.sqrt(3.0)
cell_w = 4.0 * root_three
cell_h = 24.0

def lattice(cos_vals, sin_vals):
    orbital = jnp.arange(128, dtype=jnp.int32)
    sublattice = orbital % 4
    unit_cell = orbital // 4
    column_at = (unit_cell // 8).astype(jnp.float32)
    row_at = (unit_cell % 8).astype(jnp.float32)
    inner_x = jnp.where((sublattice == 1) | (sublattice == 2), root_three / 2.0, 0.0)
    inner_y = jnp.where(sublattice == 1, 0.5, jnp.where(sublattice == 2, 1.5, jnp.where(sublattice == 3, 2.0, 0.0)))
    pos_x = column_at * root_three + inner_x - cell_w / 2.0
    pos_y = row_at * 3.0 + inner_y - cell_h / 2.0
    rot_x = cos_vals[:, None] * pos_x - sin_vals[:, None] * pos_y
    rot_y = sin_vals[:, None] * pos_x + cos_vals[:, None] * pos_y
    return jnp.stack([rot_x, rot_y], axis=1).astype(jnp.float32)

def twist_offsets(cos_vals, sin_vals, row_ids, col_ids):
    along_x = cell_w * ((row_ids % PATCH_X).astype(jnp.float32) - (PATCH_X - 1) / 2.0)
    along_y = cell_h * ((col_ids % PATCH_Y).astype(jnp.float32) - (PATCH_Y - 1) / 2.0)
    cos_less = (cos_vals - 1.0)[:, None, None]
    sin_cast = sin_vals[:, None, None]
    shift_x = cos_less * along_x[None, :, None] - sin_cast * along_y[None, None, :]
    shift_y = sin_cast * along_x[None, :, None] + cos_less * along_y[None, None, :]
    return jnp.stack([shift_x, shift_y], axis=-1)[..., None]

def taper(dist_sq):
    scaled = dist_sq / (cut_radius * cut_radius)
    return jnp.maximum(1.0 - scaled * scaled, 0.0)

def plane_block(own_pos, near_pos, shift_x, shift_y, diagonal_zero):
    delta_x = own_pos[..., 0, :, None] - near_pos[..., 0, None, :] - shift_x
    delta_y = own_pos[..., 1, :, None] - near_pos[..., 1, None, :] - shift_y
    dist_sq = delta_x * delta_x + delta_y * delta_y
    spread = jnp.sqrt(dist_sq)
    hopping = v_pi * jnp.exp(-(spread - 1.0) / decay_len) * taper(dist_sq)
    if diagonal_zero:
        orbital = jnp.arange(128, dtype=jnp.int32)
        hopping = jnp.where(orbital[:, None] == orbital[None, :], 0.0, hopping)
    return hopping

def inter_block(own_pos, near_pos, shift_x, shift_y):
    delta_x = own_pos[..., 0, :, None] - near_pos[..., 0, None, :] - shift_x
    delta_y = own_pos[..., 1, :, None] - near_pos[..., 1, None, :] - shift_y
    dist_sq = delta_x * delta_x + delta_y * delta_y + layer_gap * layer_gap
    spread = jnp.sqrt(dist_sq)
    cosine_sq = layer_gap * layer_gap / dist_sq
    bonds = v_pi * jnp.exp(-(spread - 1.0) / decay_len) * (1.0 - cosine_sq) + v_sigma * jnp.exp(-(spread - layer_gap) / decay_len) * cosine_sq
    return bonds * taper(dist_sq)

def reference(prev_vec, cur_vec, displace, potential):
    cos_vals = jnp.array([1.0, math.cos(twist_angle)], dtype=jnp.float32)
    sin_vals = jnp.array([0.0, math.sin(twist_angle)], dtype=jnp.float32)
    places = displace + lattice(cos_vals, sin_vals)[:, None, None]
    row_count = places.shape[1]
    col_count = places.shape[2]
    twisted = places + twist_offsets(cos_vals, sin_vals, jnp.arange(row_count, dtype=jnp.int32), jnp.arange(col_count, dtype=jnp.int32))

    def apply_layer(vectors, layer_id):
        other_layer = 1 - layer_id
        cos_l = math.cos(twist_angle * layer_id)
        sin_l = math.sin(twist_angle * layer_id)

        def row_terms(row_id):
            own_pos = places[layer_id, row_id]
            own_twist = twisted[layer_id, row_id]
            summed = jnp.zeros((col_count, vectors.shape[3], 128), jnp.float32)
            for step_x in (-1, 0, 1):
                near_row = (row_id + step_x) % row_count
                row_pos = places[layer_id, near_row]
                row_vec = vectors[layer_id, near_row]
                far_pos = twisted[other_layer, near_row]
                far_vec = vectors[other_layer, near_row]
                for step_y in (-1, 0, 1):
                    near_pos = jnp.roll(row_pos, -step_y, axis=0)
                    near_vec = jnp.roll(row_vec, -step_y, axis=0)
                    shift_x = cos_l * step_x * cell_w - sin_l * step_y * cell_h
                    shift_y = sin_l * step_x * cell_w + cos_l * step_y * cell_h
                    hop_block = plane_block(own_pos, near_pos, shift_x, shift_y, step_x == 0 and step_y == 0)
                    summed = summed + jnp.einsum('ycq,ypq->ycp', near_vec, hop_block, precision=lax.Precision.HIGHEST)
                    cross_block = inter_block(own_twist, jnp.roll(far_pos, -step_y, axis=0), step_x * cell_w, step_y * cell_h)
                    summed = summed + jnp.einsum('ycq,ypq->ycp', jnp.roll(far_vec, -step_y, axis=0), cross_block, precision=lax.Precision.HIGHEST)
            summed = summed + potential[layer_id, row_id][:, None, :] * vectors[layer_id, row_id]
            return summed / hop_scale
        return lax.map(row_terms, jnp.arange(row_count, dtype=jnp.int32))

    def apply_hops(vectors):
        return jnp.stack([apply_layer(vectors, 0), apply_layer(vectors, 1)])
    first_term = 2.0 * apply_hops(cur_vec) - prev_vec
    second_term = 2.0 * apply_hops(first_term) - cur_vec
    return (first_term, second_term)
```

```python
import math

import jax
import jax.numpy as jnp
import numpy as np
from jax import lax
from jax.sharding import PartitionSpec as P

PATCH_X = 14
PATCH_Y = 4


v_pi = -2.7
v_sigma = 0.48
decay_len = 0.319
layer_gap = 3.35 / 1.42
cut_radius = 3.5
hop_scale = 12.0
twist_angle = 1.05 * math.pi / 180.0
root_three = math.sqrt(3.0)
cell_w = 4.0 * root_three
cell_h = 24.0
sigma_gain = v_sigma * math.exp((layer_gap - 1.0) / decay_len)
HI = lax.Precision.HIGHEST
OFFSETS = [(a, b) for a in (-1, 0, 1) for b in (-1, 0, 1)]


def _base_np():
    orbital = np.arange(128)
    sub = orbital % 4
    cell = orbital // 4
    inner_x = np.where((sub == 1) | (sub == 2), root_three / 2.0, 0.0)
    inner_y = np.select([sub == 1, sub == 2, sub == 3], [0.5, 1.5, 2.0], 0.0)
    return np.stack([(cell // 8) * root_three + inner_x - cell_w / 2.0, (cell % 8) * 3.0 + inner_y - cell_h / 2.0])


def _reach_sets():
    base = _base_np()
    c, s = math.cos(twist_angle), math.sin(twist_angle)
    rot = np.array([[c, -s], [s, c]])
    margin = 0.5
    plane_r = cut_radius + margin
    inter_r = math.sqrt(cut_radius**2 - layer_gap**2) + margin
    twists = [
        np.array([[cell_w * (i - (PATCH_X - 1) / 2.0)], [cell_h * (j - (PATCH_Y - 1) / 2.0)]])
        for i in range(PATCH_X)
        for j in range(PATCH_Y)
    ]
    sets = {}
    for a, b in OFFSETS:
        shift = np.array([[a * cell_w], [b * cell_h]])
        gap = base[:, :, None] - base[:, None, :] - shift[:, :, None]
        mask = np.sqrt((gap**2).sum(0)) < plane_r
        for e in twists:
            turned = rot @ base + (rot - np.eye(2)) @ e
            for own, near in ((base, turned), (turned, base)):
                gap = own[:, :, None] - near[:, None, :] - shift[:, :, None]
                mask |= np.sqrt((gap**2).sum(0)) < inter_r
        sets[(a, b)] = (np.nonzero(mask.any(1))[0], np.nonzero(mask.any(0))[0])
    return sets


REACH = _reach_sets()


def _one_hot(idx):
    table = np.zeros((128, len(idx)), np.float32)
    table[idx, np.arange(len(idx))] = 1.0
    return table


def pick(x, idx):
    if len(idx) == x.shape[-1]:
        return x
    if np.all(np.diff(idx) == 1):
        return x[..., idx[0] : idx[0] + len(idx)]
    return jnp.einsum("...q,qk->...k", x, _one_hot(idx), precision=HI)


def extended_2(value, sides, width):
    for axis, dim in sides:
        devices, length = (lax.axis_size(axis), value.shape[dim])
        up = [(i, (i + 1) % devices) for i in range(devices)]
        down = [(j, i) for i, j in up]
        last = lax.slice_in_dim(value, length - width, length, axis=dim)
        first = lax.slice_in_dim(value, 0, width, axis=dim)
        before = lax.ppermute(last, axis, up)
        after = lax.ppermute(first, axis, down)
        value = jnp.concatenate([before, value, after], axis=dim)
    return value


def partner_2(value, axis, distance):
    return lax.ppermute(value, axis, [(i, i ^ 1 << distance) for i in range(lax.axis_size(axis))])


def lattice(cos_vals, sin_vals):
    base = jnp.asarray(_base_np(), jnp.float32)
    rot_x = cos_vals[:, None] * base[0] - sin_vals[:, None] * base[1]
    rot_y = sin_vals[:, None] * base[0] + cos_vals[:, None] * base[1]
    return jnp.stack([rot_x, rot_y], axis=1)


def twist_offsets(cos_vals, sin_vals, row_ids, col_ids):
    along_x = cell_w * ((row_ids % PATCH_X).astype(jnp.float32) - (PATCH_X - 1) / 2.0)
    along_y = cell_h * ((col_ids % PATCH_Y).astype(jnp.float32) - (PATCH_Y - 1) / 2.0)
    cos_less = (cos_vals - 1.0)[:, None, None]
    sin_cast = sin_vals[:, None, None]
    shift_x = cos_less * along_x[None, :, None] - sin_cast * along_y[None, None, :]
    shift_y = sin_cast * along_x[None, :, None] + cos_less * along_y[None, None, :]
    return jnp.stack([shift_x, shift_y], axis=-1)[..., None]


def taper(dist_sq):
    scaled = dist_sq / (cut_radius * cut_radius)
    return jnp.maximum(1.0 - scaled * scaled, 0.0)


def plane_block(own_pos, near_pos, shift_x, shift_y, self_rows):
    delta_x = own_pos[..., 0, :, None] - near_pos[..., 0, None, :] - shift_x
    delta_y = own_pos[..., 1, :, None] - near_pos[..., 1, None, :] - shift_y
    dist_sq = delta_x * delta_x + delta_y * delta_y
    spread = jnp.sqrt(dist_sq)
    hopping = v_pi * jnp.exp(-(spread - 1.0) / decay_len) * taper(dist_sq)
    if self_rows:
        orbital = jnp.arange(128, dtype=jnp.int32)
        hopping = jnp.where(orbital[:, None] == orbital[None, :], 0.0, hopping)
    return hopping


def inter_block(own_pos, near_pos, shift_x, shift_y):
    delta_x = own_pos[..., 0, :, None] - near_pos[..., 0, None, :] - shift_x
    delta_y = own_pos[..., 1, :, None] - near_pos[..., 1, None, :] - shift_y
    dist_sq = delta_x * delta_x + delta_y * delta_y + layer_gap * layer_gap
    spread = jnp.sqrt(dist_sq)
    cosine_sq = layer_gap * layer_gap / dist_sq
    decay = jnp.exp(-(spread - 1.0) / decay_len)
    bonds = decay * (v_pi * (1.0 - cosine_sq) + sigma_gain * cosine_sq)
    return bonds * taper(dist_sq)


def body(prev_vec, cur_vec, displace, potential):
    layer_id = lax.axis_index("layer")
    tile_x = displace.shape[1]
    tile_y = displace.shape[2]
    cos_twist = math.cos(twist_angle)
    sin_twist = math.sin(twist_angle)
    partner = partner_2(displace, "layer", 0)
    both_disp = jnp.concatenate([displace, partner], axis=0)
    layer_up = layer_id == 1
    cos_vals = jnp.stack(
        [jnp.where(layer_up, cos_twist, 1.0), jnp.where(layer_up, 1.0, cos_twist)]
    ).astype(jnp.float32)
    sin_vals = jnp.stack(
        [jnp.where(layer_up, sin_twist, 0.0), jnp.where(layer_up, 0.0, sin_twist)]
    ).astype(jnp.float32)
    ext_disp = extended_2(both_disp, (("gx", 1), ("gy", 2)), 1)
    places = ext_disp + lattice(cos_vals, sin_vals)[:, None, None]
    row_count = tile_x * lax.axis_size("gx")
    col_count = tile_y * lax.axis_size("gy")
    row_ids = (
        lax.axis_index("gx") * tile_x + jnp.arange(tile_x + 2, dtype=jnp.int32) - 1 + row_count
    ) % row_count
    col_ids = (
        lax.axis_index("gy") * tile_y + jnp.arange(tile_y + 2, dtype=jnp.int32) - 1 + col_count
    ) % col_count
    twisted = places + twist_offsets(cos_vals, sin_vals, row_ids, col_ids)

    def own_view(value, a, b):
        return value[:, 1 + a : 1 + a + tile_x, 1 + b : 1 + b + tile_y]

    own_pos = own_view(places[:1], 0, 0)[0]
    own_twist = own_view(twisted[:1], 0, 0)[0]
    cos_own = cos_vals[0]
    sin_own = sin_vals[0]
    blocks = []
    for a, b in OFFSETS:
        rows, cols = REACH[(a, b)]
        shift_x = cos_own * (a * cell_w) - sin_own * (b * cell_h)
        shift_y = sin_own * (a * cell_w) + cos_own * (b * cell_h)
        near_pos = pick(own_view(places[:1], a, b)[0], cols)
        near_twist = pick(own_view(twisted[1:], a, b)[0], cols)
        plane = plane_block(pick(own_pos, rows), near_pos, shift_x, shift_y, a == 0 and b == 0)
        inter = inter_block(pick(own_twist, rows), near_twist, a * cell_w, b * cell_h)
        blocks.append((plane, inter))

    spread_rows = np.concatenate([REACH[o][0] for o in OFFSETS if len(REACH[o][0]) < 128])
    scatter = np.zeros((len(spread_rows), 128), np.float32)
    scatter[np.arange(len(spread_rows)), spread_rows] = 1.0

    def hop_terms(vectors):
        stacked = jnp.concatenate([vectors, partner_2(vectors, "layer", 0)], axis=0)
        extended = extended_2(stacked, (("gx", 1), ("gy", 2)), 1)
        full = potential[0][..., None, :] * vectors[0]
        parts = []
        for (a, b), (plane, inter) in zip(OFFSETS, blocks):
            rows, cols = REACH[(a, b)]
            near = pick(own_view(extended, a, b), cols)
            summed = jnp.einsum("xycq,xypq->xycp", near[0], plane, precision=HI)
            summed = summed + jnp.einsum("xycq,xypq->xycp", near[1], inter, precision=HI)
            if len(rows) == 128:
                full = full + summed
            else:
                parts.append(summed)
        full = full + jnp.einsum(
            "xycp,pn->xycn", jnp.concatenate(parts, axis=-1), scatter, precision=HI
        )
        return (full / hop_scale)[None]

    first_term = 2.0 * hop_terms(cur_vec) - prev_vec
    second_term = 2.0 * hop_terms(first_term) - cur_vec
    return (first_term, second_term)


def solution(mesh):
    in_specs = (
        P("layer", "gx", "gy", None, None),
        P("layer", "gx", "gy", None, None),
        P("layer", "gx", "gy", None, None),
        P("layer", "gx", "gy", None),
    )
    out_specs = (P("layer", "gx", "gy", None, None), P("layer", "gx", "gy", None, None))
    return jax.shard_map(body, mesh=mesh, in_specs=in_specs, out_specs=out_specs, check_vma=False)
```

```python
import math

import jax
import jax.numpy as jnp
import numpy as np
from jax import lax
from jax.sharding import PartitionSpec as P

PATCH_X = 14
PATCH_Y = 4


v_pi = -2.7
v_sigma = 0.48
decay_len = 0.319
layer_gap = 3.35 / 1.42
cut_radius = 3.5
hop_scale = 12.0
twist_angle = 1.05 * math.pi / 180.0
root_three = math.sqrt(3.0)
cell_w = 4.0 * root_three
cell_h = 24.0
sigma_gain = v_sigma * math.exp((layer_gap - 1.0) / decay_len)
HI = lax.Precision.HIGHEST
OFFSETS = [(a, b) for a in (-1, 0, 1) for b in (-1, 0, 1)]


def _base_np():
    orbital = np.arange(128)
    sub = orbital % 4
    cell = orbital // 4
    inner_x = np.where((sub == 1) | (sub == 2), root_three / 2.0, 0.0)
    inner_y = np.select([sub == 1, sub == 2, sub == 3], [0.5, 1.5, 2.0], 0.0)
    return np.stack([(cell // 8) * root_three + inner_x - cell_w / 2.0, (cell % 8) * 3.0 + inner_y - cell_h / 2.0])


def _reach_sets():
    base = _base_np()
    c, s = math.cos(twist_angle), math.sin(twist_angle)
    rot = np.array([[c, -s], [s, c]])
    margin = 0.5
    plane_r = cut_radius + margin
    inter_r = math.sqrt(cut_radius**2 - layer_gap**2) + margin
    twists = [
        np.array([[cell_w * (i - (PATCH_X - 1) / 2.0)], [cell_h * (j - (PATCH_Y - 1) / 2.0)]])
        for i in range(PATCH_X)
        for j in range(PATCH_Y)
    ]
    sets = {}
    for a, b in OFFSETS:
        shift = np.array([[a * cell_w], [b * cell_h]])
        gap = base[:, :, None] - base[:, None, :] - shift[:, :, None]
        mask = np.sqrt((gap**2).sum(0)) < plane_r
        for e in twists:
            turned = rot @ base + (rot - np.eye(2)) @ e
            for own, near in ((base, turned), (turned, base)):
                gap = own[:, :, None] - near[:, None, :] - shift[:, :, None]
                mask |= np.sqrt((gap**2).sum(0)) < inter_r
        sets[(a, b)] = (np.nonzero(mask.any(1))[0], np.nonzero(mask.any(0))[0])
    return sets


REACH = _reach_sets()


def _one_hot(idx):
    table = np.zeros((128, len(idx)), np.float32)
    table[idx, np.arange(len(idx))] = 1.0
    return table


def pick(x, idx):
    if len(idx) == x.shape[-1]:
        return x
    if np.all(np.diff(idx) == 1):
        return x[..., idx[0] : idx[0] + len(idx)]
    return jnp.einsum("...q,qk->...k", x, _one_hot(idx), precision=HI)


def extended_2(value, sides, width):
    for axis, dim in sides:
        devices, length = (lax.axis_size(axis), value.shape[dim])
        up = [(i, (i + 1) % devices) for i in range(devices)]
        down = [(j, i) for i, j in up]
        last = lax.slice_in_dim(value, length - width, length, axis=dim)
        first = lax.slice_in_dim(value, 0, width, axis=dim)
        if devices == 2:
            both = lax.ppermute(jnp.concatenate([last, first], axis=dim), axis, up)
            before = lax.slice_in_dim(both, 0, width, axis=dim)
            after = lax.slice_in_dim(both, width, 2 * width, axis=dim)
        else:
            before = lax.ppermute(last, axis, up)
            after = lax.ppermute(first, axis, down)
        value = jnp.concatenate([before, value, after], axis=dim)
    return value


def partner_2(value, axis, distance):
    return lax.ppermute(value, axis, [(i, i ^ 1 << distance) for i in range(lax.axis_size(axis))])


def lattice(cos_vals, sin_vals):
    base = jnp.asarray(_base_np(), jnp.float32)
    rot_x = cos_vals[:, None] * base[0] - sin_vals[:, None] * base[1]
    rot_y = sin_vals[:, None] * base[0] + cos_vals[:, None] * base[1]
    return jnp.stack([rot_x, rot_y], axis=1)


def twist_offsets(cos_vals, sin_vals, row_ids, col_ids):
    along_x = cell_w * ((row_ids % PATCH_X).astype(jnp.float32) - (PATCH_X - 1) / 2.0)
    along_y = cell_h * ((col_ids % PATCH_Y).astype(jnp.float32) - (PATCH_Y - 1) / 2.0)
    cos_less = (cos_vals - 1.0)[:, None, None]
    sin_cast = sin_vals[:, None, None]
    shift_x = cos_less * along_x[None, :, None] - sin_cast * along_y[None, None, :]
    shift_y = sin_cast * along_x[None, :, None] + cos_less * along_y[None, None, :]
    return jnp.stack([shift_x, shift_y], axis=-1)[..., None]


def taper(dist_sq):
    scaled = dist_sq / (cut_radius * cut_radius)
    return jnp.maximum(1.0 - scaled * scaled, 0.0)


def plane_block(own_pos, near_pos, shift_x, shift_y, self_rows):
    delta_x = own_pos[..., 0, :, None] - near_pos[..., 0, None, :] - shift_x
    delta_y = own_pos[..., 1, :, None] - near_pos[..., 1, None, :] - shift_y
    dist_sq = delta_x * delta_x + delta_y * delta_y
    spread = jnp.sqrt(dist_sq)
    hopping = v_pi * jnp.exp(-(spread - 1.0) / decay_len) * taper(dist_sq)
    if self_rows:
        orbital = jnp.arange(128, dtype=jnp.int32)
        hopping = jnp.where(orbital[:, None] == orbital[None, :], 0.0, hopping)
    return hopping


def inter_block(own_pos, near_pos, shift_x, shift_y):
    delta_x = own_pos[..., 0, :, None] - near_pos[..., 0, None, :] - shift_x
    delta_y = own_pos[..., 1, :, None] - near_pos[..., 1, None, :] - shift_y
    dist_sq = delta_x * delta_x + delta_y * delta_y + layer_gap * layer_gap
    spread = jnp.sqrt(dist_sq)
    cosine_sq = layer_gap * layer_gap / dist_sq
    decay = jnp.exp(-(spread - 1.0) / decay_len)
    bonds = decay * (v_pi * (1.0 - cosine_sq) + sigma_gain * cosine_sq)
    return bonds * taper(dist_sq)


def exchange(value):
    stacked = jnp.concatenate([value, partner_2(value, "layer", 0)], axis=0)
    return extended_2(stacked, (("gx", 1), ("gy", 2)), 1)


def body(prev_vec, cur_vec, displace, potential):
    layer_id = lax.axis_index("layer")
    tile_x = displace.shape[1]
    tile_y = displace.shape[2]
    cos_twist = math.cos(twist_angle)
    sin_twist = math.sin(twist_angle)
    packed = exchange(jnp.concatenate([cur_vec, displace], axis=-2))
    vec_ext = packed[..., : cur_vec.shape[-2], :]
    ext_disp = packed[..., cur_vec.shape[-2] :, :]
    layer_up = layer_id == 1
    cos_vals = jnp.stack(
        [jnp.where(layer_up, cos_twist, 1.0), jnp.where(layer_up, 1.0, cos_twist)]
    ).astype(jnp.float32)
    sin_vals = jnp.stack(
        [jnp.where(layer_up, sin_twist, 0.0), jnp.where(layer_up, 0.0, sin_twist)]
    ).astype(jnp.float32)
    places = ext_disp + lattice(cos_vals, sin_vals)[:, None, None]
    row_count = tile_x * lax.axis_size("gx")
    col_count = tile_y * lax.axis_size("gy")
    row_ids = (
        lax.axis_index("gx") * tile_x + jnp.arange(tile_x + 2, dtype=jnp.int32) - 1 + row_count
    ) % row_count
    col_ids = (
        lax.axis_index("gy") * tile_y + jnp.arange(tile_y + 2, dtype=jnp.int32) - 1 + col_count
    ) % col_count
    turn = twist_offsets(cos_vals, sin_vals, row_ids, col_ids)
    twisted = places + turn

    def own_view(value, a, b):
        return value[:, 1 + a : 1 + a + tile_x, 1 + b : 1 + b + tile_y]

    own_pos = own_view(places[:1], 0, 0)[0]
    own_shift = own_view(turn[:1], 0, 0)[0]
    cos_own = cos_vals[0]
    sin_own = sin_vals[0]
    narrow = [o for o in OFFSETS if len(REACH[o][0]) < 64]
    narrow_rows = np.concatenate([REACH[o][0] for o in narrow])
    picked = jnp.einsum("...q,qk->...k", own_pos, _one_hot(narrow_rows), precision=HI)
    blocks = {}
    columns = {}
    at = 0
    for a, b in OFFSETS:
        rows, cols = REACH[(a, b)]
        if len(rows) < 64:
            own_rows = picked[..., at : at + len(rows)]
            at += len(rows)
            cols = np.arange(128)
        else:
            own_rows = pick(own_pos, rows)
        shift_x = cos_own * (a * cell_w) - sin_own * (b * cell_h)
        shift_y = sin_own * (a * cell_w) + cos_own * (b * cell_h)
        near_pos = pick(own_view(places[:1], a, b)[0], cols)
        near_twist = pick(own_view(twisted[1:], a, b)[0], cols)
        plane = plane_block(own_rows, near_pos, shift_x, shift_y, a == 0 and b == 0)
        inter = inter_block(own_rows + own_shift, near_twist, a * cell_w, b * cell_h)
        blocks[(a, b)] = (plane, inter)
        columns[(a, b)] = cols
    blocks = lax.optimization_barrier(blocks)

    scatter = np.zeros((len(narrow_rows), 128), np.float32)
    scatter[np.arange(len(narrow_rows)), narrow_rows] = 1.0

    def hop_terms(vectors, extended):
        full = potential[0][..., None, :] * vectors[0]
        parts = {}
        for a, b in OFFSETS:
            plane, inter = blocks[(a, b)]
            near = pick(own_view(extended, a, b), columns[(a, b)])
            summed = jnp.einsum("xycq,xypq->xycp", near[0], plane, precision=HI)
            parts[(a, b)] = summed + jnp.einsum("xycq,xypq->xycp", near[1], inter, precision=HI)
        full = full + parts[(0, 0)]
        full = full + jnp.concatenate([parts[(-1, 0)], parts[(1, 0)]], axis=-1)
        full = full + jnp.einsum(
            "xycp,pn->xycn", jnp.concatenate([parts[o] for o in narrow], axis=-1), scatter, precision=HI
        )
        return (full / hop_scale)[None]

    first_term = 2.0 * hop_terms(cur_vec, vec_ext) - prev_vec
    second_term = 2.0 * hop_terms(first_term, exchange(first_term)) - cur_vec
    return (first_term, second_term)


def solution(mesh):
    in_specs = (
        P("layer", "gx", "gy", None, None),
        P("layer", "gx", "gy", None, None),
        P("layer", "gx", "gy", None, None),
        P("layer", "gx", "gy", None),
    )
    out_specs = (P("layer", "gx", "gy", None, None), P("layer", "gx", "gy", None, None))
    return jax.shard_map(body, mesh=mesh, in_specs=in_specs, out_specs=out_specs, check_vma=False)
```

```python
import math

import jax
import jax.numpy as jnp
import numpy as np
from jax import lax
from jax.sharding import PartitionSpec as P

PATCH_X = 14
PATCH_Y = 4


v_pi = -2.7
v_sigma = 0.48
decay_len = 0.319
layer_gap = 3.35 / 1.42
cut_radius = 3.5
hop_scale = 12.0
twist_angle = 1.05 * math.pi / 180.0
root_three = math.sqrt(3.0)
cell_w = 4.0 * root_three
cell_h = 24.0
sigma_gain = v_sigma * math.exp((layer_gap - 1.0) / decay_len)
HI = lax.Precision.HIGHEST
OFFSETS = [(a, b) for a in (-1, 0, 1) for b in (-1, 0, 1)]


def _base_np():
    orbital = np.arange(128)
    sub = orbital % 4
    cell = orbital // 4
    inner_x = np.where((sub == 1) | (sub == 2), root_three / 2.0, 0.0)
    inner_y = np.select([sub == 1, sub == 2, sub == 3], [0.5, 1.5, 2.0], 0.0)
    return np.stack([(cell // 8) * root_three + inner_x - cell_w / 2.0, (cell % 8) * 3.0 + inner_y - cell_h / 2.0])


def _reach_sets():
    base = _base_np()
    c, s = math.cos(twist_angle), math.sin(twist_angle)
    rot = np.array([[c, -s], [s, c]])
    margin = 0.5
    plane_r = cut_radius + margin
    inter_r = math.sqrt(cut_radius**2 - layer_gap**2) + margin
    twists = [
        np.array([[cell_w * (i - (PATCH_X - 1) / 2.0)], [cell_h * (j - (PATCH_Y - 1) / 2.0)]])
        for i in range(PATCH_X)
        for j in range(PATCH_Y)
    ]
    sets = {}
    for a, b in OFFSETS:
        shift = np.array([[a * cell_w], [b * cell_h]])
        gap = base[:, :, None] - base[:, None, :] - shift[:, :, None]
        mask = np.sqrt((gap**2).sum(0)) < plane_r
        for e in twists:
            turned = rot @ base + (rot - np.eye(2)) @ e
            for own, near in ((base, turned), (turned, base)):
                gap = own[:, :, None] - near[:, None, :] - shift[:, :, None]
                mask |= np.sqrt((gap**2).sum(0)) < inter_r
        sets[(a, b)] = (np.nonzero(mask.any(1))[0], np.nonzero(mask.any(0))[0])
    return sets


REACH = _reach_sets()


def _one_hot(idx):
    table = np.zeros((128, len(idx)), np.float32)
    table[idx, np.arange(len(idx))] = 1.0
    return table


def pick(x, idx):
    if len(idx) == x.shape[-1]:
        return x
    if np.all(np.diff(idx) == 1):
        return x[..., idx[0] : idx[0] + len(idx)]
    return jnp.einsum("...q,qk->...k", x, _one_hot(idx), precision=HI)


def extended_2(value, sides, width):
    for axis, dim in sides:
        devices, length = (lax.axis_size(axis), value.shape[dim])
        up = [(i, (i + 1) % devices) for i in range(devices)]
        down = [(j, i) for i, j in up]
        last = lax.slice_in_dim(value, length - width, length, axis=dim)
        first = lax.slice_in_dim(value, 0, width, axis=dim)
        if devices == 2:
            both = lax.ppermute(jnp.concatenate([last, first], axis=dim), axis, up)
            before = lax.slice_in_dim(both, 0, width, axis=dim)
            after = lax.slice_in_dim(both, width, 2 * width, axis=dim)
        else:
            before = lax.ppermute(last, axis, up)
            after = lax.ppermute(first, axis, down)
        value = jnp.concatenate([before, value, after], axis=dim)
    return value


def partner_2(value, axis, distance):
    return lax.ppermute(value, axis, [(i, i ^ 1 << distance) for i in range(lax.axis_size(axis))])


def lattice(cos_vals, sin_vals):
    base = jnp.asarray(_base_np(), jnp.float32)
    rot_x = cos_vals[:, None] * base[0] - sin_vals[:, None] * base[1]
    rot_y = sin_vals[:, None] * base[0] + cos_vals[:, None] * base[1]
    return jnp.stack([rot_x, rot_y], axis=1)


def twist_offsets(cos_vals, sin_vals, row_ids, col_ids):
    along_x = cell_w * ((row_ids % PATCH_X).astype(jnp.float32) - (PATCH_X - 1) / 2.0)
    along_y = cell_h * ((col_ids % PATCH_Y).astype(jnp.float32) - (PATCH_Y - 1) / 2.0)
    cos_less = (cos_vals - 1.0)[:, None, None]
    sin_cast = sin_vals[:, None, None]
    shift_x = cos_less * along_x[None, :, None] - sin_cast * along_y[None, None, :]
    shift_y = sin_cast * along_x[None, :, None] + cos_less * along_y[None, None, :]
    return jnp.stack([shift_x, shift_y], axis=-1)[..., None]


def taper(dist_sq):
    scaled = dist_sq / (cut_radius * cut_radius)
    return jnp.maximum(1.0 - scaled * scaled, 0.0)


def plane_block(own_pos, near_pos, shift_x, shift_y, self_rows):
    delta_x = own_pos[..., 0, :, None] - near_pos[..., 0, None, :] - shift_x
    delta_y = own_pos[..., 1, :, None] - near_pos[..., 1, None, :] - shift_y
    dist_sq = delta_x * delta_x + delta_y * delta_y
    spread = jnp.sqrt(dist_sq)
    hopping = v_pi * jnp.exp(-(spread - 1.0) / decay_len) * taper(dist_sq)
    if self_rows:
        orbital = jnp.arange(128, dtype=jnp.int32)
        hopping = jnp.where(orbital[:, None] == orbital[None, :], 0.0, hopping)
    return hopping


def inter_block(own_pos, near_pos, shift_x, shift_y):
    delta_x = own_pos[..., 0, :, None] - near_pos[..., 0, None, :] - shift_x
    delta_y = own_pos[..., 1, :, None] - near_pos[..., 1, None, :] - shift_y
    dist_sq = delta_x * delta_x + delta_y * delta_y + layer_gap * layer_gap
    spread = jnp.sqrt(dist_sq)
    cosine_sq = layer_gap * layer_gap / dist_sq
    decay = jnp.exp(-(spread - 1.0) / decay_len)
    bonds = decay * (v_pi * (1.0 - cosine_sq) + sigma_gain * cosine_sq)
    return bonds * taper(dist_sq)


def _halo_options(n):
    if n == 1:
        return [(0, ("last", "all", "first"))]
    if n == 2:
        return [(0, ("all",)), (1, ("last", "first"))]
    return [(-1, ("last",)), (0, ("all",)), (1, ("first",))]


def _region(value, kind, axis):
    length = value.shape[axis]
    if kind == "last":
        return lax.slice_in_dim(value, length - 1, length, axis=axis)
    if kind == "first":
        return lax.slice_in_dim(value, 0, 1, axis=axis)
    return value


def exchange(value):
    axes = ("layer", "gx", "gy")
    sizes = [lax.axis_size(a) for a in axes]
    tile = {1: value.shape[1], 2: value.shape[2]}
    pieces = {}
    for layer_step in (0, 1):
        for step_x, kinds_x in _halo_options(sizes[1]):
            along_x = jnp.concatenate([_region(value, r, 1) for r in kinds_x], axis=1)
            for step_y, kinds_y in _halo_options(sizes[2]):
                part = jnp.concatenate([_region(along_x, r, 2) for r in kinds_y], axis=2)
                if (layer_step, step_x, step_y) != (0, 0, 0):
                    pairs = []
                    for l in range(sizes[0]):
                        for x in range(sizes[1]):
                            for y in range(sizes[2]):
                                src = (l * sizes[1] + x) * sizes[2] + y
                                dst_l = (l - layer_step) % sizes[0]
                                dst_x = (x - step_x) % sizes[1]
                                dst_y = (y - step_y) % sizes[2]
                                pairs.append((src, (dst_l * sizes[1] + dst_x) * sizes[2] + dst_y))
                    part = lax.ppermute(part, axes, pairs)
                at_x = 0
                for rx in kinds_x:
                    wide_x = tile[1] if rx == "all" else 1
                    at_y = 0
                    for ry in kinds_y:
                        wide_y = tile[2] if ry == "all" else 1
                        pieces[(layer_step, rx, ry)] = part[:, at_x : at_x + wide_x, at_y : at_y + wide_y]
                        at_y += wide_y
                    at_x += wide_x
    order = ("last", "all", "first")
    layers = []
    for layer_step in (0, 1):
        rows = [
            jnp.concatenate([pieces[(layer_step, rx, ry)] for ry in order], axis=2) for rx in order
        ]
        layers.append(jnp.concatenate(rows, axis=1))
    return jnp.concatenate(layers, axis=0)


def body(prev_vec, cur_vec, displace, potential):
    layer_id = lax.axis_index("layer")
    tile_x = displace.shape[1]
    tile_y = displace.shape[2]
    cos_twist = math.cos(twist_angle)
    sin_twist = math.sin(twist_angle)
    packed = exchange(jnp.concatenate([cur_vec, displace], axis=-2))
    vec_ext = packed[..., : cur_vec.shape[-2], :]
    ext_disp = packed[..., cur_vec.shape[-2] :, :]
    layer_up = layer_id == 1
    cos_vals = jnp.stack(
        [jnp.where(layer_up, cos_twist, 1.0), jnp.where(layer_up, 1.0, cos_twist)]
    ).astype(jnp.float32)
    sin_vals = jnp.stack(
        [jnp.where(layer_up, sin_twist, 0.0), jnp.where(layer_up, 0.0, sin_twist)]
    ).astype(jnp.float32)
    places = ext_disp + lattice(cos_vals, sin_vals)[:, None, None]
    row_count = tile_x * lax.axis_size("gx")
    col_count = tile_y * lax.axis_size("gy")
    row_ids = (
        lax.axis_index("gx") * tile_x + jnp.arange(tile_x + 2, dtype=jnp.int32) - 1 + row_count
    ) % row_count
    col_ids = (
        lax.axis_index("gy") * tile_y + jnp.arange(tile_y + 2, dtype=jnp.int32) - 1 + col_count
    ) % col_count
    turn = twist_offsets(cos_vals, sin_vals, row_ids, col_ids)
    twisted = places + turn

    def own_view(value, a, b):
        return value[:, 1 + a : 1 + a + tile_x, 1 + b : 1 + b + tile_y]

    own_pos = own_view(places[:1], 0, 0)[0]
    own_shift = own_view(turn[:1], 0, 0)[0]
    cos_own = cos_vals[0]
    sin_own = sin_vals[0]
    narrow = [o for o in OFFSETS if len(REACH[o][0]) < 64]
    narrow_rows = np.concatenate([REACH[o][0] for o in narrow])
    picked = jnp.einsum("...q,qk->...k", own_pos, _one_hot(narrow_rows), precision=HI)
    blocks = {}
    columns = {}
    at = 0
    for a, b in OFFSETS:
        rows, cols = REACH[(a, b)]
        if len(rows) < 64:
            own_rows = picked[..., at : at + len(rows)]
            at += len(rows)
            cols = np.arange(128)
        else:
            own_rows = pick(own_pos, rows)
        shift_x = cos_own * (a * cell_w) - sin_own * (b * cell_h)
        shift_y = sin_own * (a * cell_w) + cos_own * (b * cell_h)
        near_pos = pick(own_view(places[:1], a, b)[0], cols)
        near_twist = pick(own_view(twisted[1:], a, b)[0], cols)
        plane = plane_block(own_rows, near_pos, shift_x, shift_y, a == 0 and b == 0)
        inter = inter_block(own_rows + own_shift, near_twist, a * cell_w, b * cell_h)
        blocks[(a, b)] = (plane, inter)
        columns[(a, b)] = cols
    blocks = lax.optimization_barrier(blocks)

    scatter = np.zeros((len(narrow_rows), 128), np.float32)
    scatter[np.arange(len(narrow_rows)), narrow_rows] = 1.0

    def hop_terms(vectors, extended):
        full = potential[0][..., None, :] * vectors[0]
        parts = {}
        for a, b in OFFSETS:
            plane, inter = blocks[(a, b)]
            near = pick(own_view(extended, a, b), columns[(a, b)])
            summed = jnp.einsum("xycq,xypq->xycp", near[0], plane, precision=HI)
            parts[(a, b)] = summed + jnp.einsum("xycq,xypq->xycp", near[1], inter, precision=HI)
        full = full + parts[(0, 0)]
        full = full + jnp.concatenate([parts[(-1, 0)], parts[(1, 0)]], axis=-1)
        full = full + jnp.einsum(
            "xycp,pn->xycn", jnp.concatenate([parts[o] for o in narrow], axis=-1), scatter, precision=HI
        )
        return (full / hop_scale)[None]

    first_term = 2.0 * hop_terms(cur_vec, vec_ext) - prev_vec
    second_term = 2.0 * hop_terms(first_term, exchange(first_term)) - cur_vec
    return (first_term, second_term)


def solution(mesh):
    in_specs = (
        P("layer", "gx", "gy", None, None),
        P("layer", "gx", "gy", None, None),
        P("layer", "gx", "gy", None, None),
        P("layer", "gx", "gy", None),
    )
    out_specs = (P("layer", "gx", "gy", None, None), P("layer", "gx", "gy", None, None))
    return jax.shard_map(body, mesh=mesh, in_specs=in_specs, out_specs=out_specs, check_vma=False)
```

```python
import math

import jax
import jax.numpy as jnp
import numpy as np
from jax import lax
from jax.sharding import PartitionSpec as P

PATCH_X = 14
PATCH_Y = 4


v_pi = -2.7
v_sigma = 0.48
decay_len = 0.319
layer_gap = 3.35 / 1.42
cut_radius = 3.5
hop_scale = 12.0
twist_angle = 1.05 * math.pi / 180.0
root_three = math.sqrt(3.0)
cell_w = 4.0 * root_three
cell_h = 24.0
sigma_gain = v_sigma * math.exp((layer_gap - 1.0) / decay_len)
HI = lax.Precision.HIGHEST
MID = lax.Precision.HIGH
OFFSETS = [(a, b) for a in (-1, 0, 1) for b in (-1, 0, 1)]


def _base_np():
    orbital = np.arange(128)
    sub = orbital % 4
    cell = orbital // 4
    inner_x = np.where((sub == 1) | (sub == 2), root_three / 2.0, 0.0)
    inner_y = np.select([sub == 1, sub == 2, sub == 3], [0.5, 1.5, 2.0], 0.0)
    return np.stack([(cell // 8) * root_three + inner_x - cell_w / 2.0, (cell % 8) * 3.0 + inner_y - cell_h / 2.0])


def _reach_sets():
    base = _base_np()
    c, s = math.cos(twist_angle), math.sin(twist_angle)
    rot = np.array([[c, -s], [s, c]])
    margin = 0.5
    plane_r = cut_radius + margin
    inter_r = math.sqrt(cut_radius**2 - layer_gap**2) + margin
    twists = [
        np.array([[cell_w * (i - (PATCH_X - 1) / 2.0)], [cell_h * (j - (PATCH_Y - 1) / 2.0)]])
        for i in range(PATCH_X)
        for j in range(PATCH_Y)
    ]
    sets = {}
    for a, b in OFFSETS:
        shift = np.array([[a * cell_w], [b * cell_h]])
        gap = base[:, :, None] - base[:, None, :] - shift[:, :, None]
        mask = np.sqrt((gap**2).sum(0)) < plane_r
        for e in twists:
            turned = rot @ base + (rot - np.eye(2)) @ e
            for own, near in ((base, turned), (turned, base)):
                gap = own[:, :, None] - near[:, None, :] - shift[:, :, None]
                mask |= np.sqrt((gap**2).sum(0)) < inter_r
        sets[(a, b)] = (np.nonzero(mask.any(1))[0], np.nonzero(mask.any(0))[0])
    return sets


REACH = _reach_sets()


def _one_hot(idx):
    table = np.zeros((128, len(idx)), np.float32)
    table[idx, np.arange(len(idx))] = 1.0
    return table


def pick(x, idx):
    if len(idx) == x.shape[-1]:
        return x
    if np.all(np.diff(idx) == 1):
        return x[..., idx[0] : idx[0] + len(idx)]
    return jnp.einsum("...q,qk->...k", x, _one_hot(idx), precision=HI)


def extended_2(value, sides, width):
    for axis, dim in sides:
        devices, length = (lax.axis_size(axis), value.shape[dim])
        up = [(i, (i + 1) % devices) for i in range(devices)]
        down = [(j, i) for i, j in up]
        last = lax.slice_in_dim(value, length - width, length, axis=dim)
        first = lax.slice_in_dim(value, 0, width, axis=dim)
        if devices == 2:
            both = lax.ppermute(jnp.concatenate([last, first], axis=dim), axis, up)
            before = lax.slice_in_dim(both, 0, width, axis=dim)
            after = lax.slice_in_dim(both, width, 2 * width, axis=dim)
        else:
            before = lax.ppermute(last, axis, up)
            after = lax.ppermute(first, axis, down)
        value = jnp.concatenate([before, value, after], axis=dim)
    return value


def partner_2(value, axis, distance):
    return lax.ppermute(value, axis, [(i, i ^ 1 << distance) for i in range(lax.axis_size(axis))])


def lattice(cos_vals, sin_vals):
    base = jnp.asarray(_base_np(), jnp.float32)
    rot_x = cos_vals[:, None] * base[0] - sin_vals[:, None] * base[1]
    rot_y = sin_vals[:, None] * base[0] + cos_vals[:, None] * base[1]
    return jnp.stack([rot_x, rot_y], axis=1)


def twist_offsets(cos_vals, sin_vals, row_ids, col_ids):
    along_x = cell_w * ((row_ids % PATCH_X).astype(jnp.float32) - (PATCH_X - 1) / 2.0)
    along_y = cell_h * ((col_ids % PATCH_Y).astype(jnp.float32) - (PATCH_Y - 1) / 2.0)
    cos_less = (cos_vals - 1.0)[:, None, None]
    sin_cast = sin_vals[:, None, None]
    shift_x = cos_less * along_x[None, :, None] - sin_cast * along_y[None, None, :]
    shift_y = sin_cast * along_x[None, :, None] + cos_less * along_y[None, None, :]
    return jnp.stack([shift_x, shift_y], axis=-1)[..., None]


def taper(dist_sq):
    scaled = dist_sq / (cut_radius * cut_radius)
    return jnp.maximum(1.0 - scaled * scaled, 0.0)


def plane_block(own_pos, near_pos, shift_x, shift_y, self_rows):
    delta_x = own_pos[..., 0, :, None] - near_pos[..., 0, None, :] - shift_x
    delta_y = own_pos[..., 1, :, None] - near_pos[..., 1, None, :] - shift_y
    dist_sq = delta_x * delta_x + delta_y * delta_y
    spread = jnp.sqrt(dist_sq)
    hopping = v_pi * jnp.exp(-(spread - 1.0) / decay_len) * taper(dist_sq)
    if self_rows:
        orbital = jnp.arange(128, dtype=jnp.int32)
        hopping = jnp.where(orbital[:, None] == orbital[None, :], 0.0, hopping)
    return hopping


def inter_block(own_pos, near_pos, shift_x, shift_y):
    delta_x = own_pos[..., 0, :, None] - near_pos[..., 0, None, :] - shift_x
    delta_y = own_pos[..., 1, :, None] - near_pos[..., 1, None, :] - shift_y
    dist_sq = delta_x * delta_x + delta_y * delta_y + layer_gap * layer_gap
    spread = jnp.sqrt(dist_sq)
    cosine_sq = layer_gap * layer_gap / dist_sq
    decay = jnp.exp(-(spread - 1.0) / decay_len)
    bonds = decay * (v_pi * (1.0 - cosine_sq) + sigma_gain * cosine_sq)
    return bonds * taper(dist_sq)


def _halo_options(n):
    if n == 1:
        return [(0, ("last", "all", "first"))]
    if n == 2:
        return [(0, ("all",)), (1, ("last", "first"))]
    return [(-1, ("last",)), (0, ("all",)), (1, ("first",))]


def _region(value, kind, axis):
    length = value.shape[axis]
    if kind == "last":
        return lax.slice_in_dim(value, length - 1, length, axis=axis)
    if kind == "first":
        return lax.slice_in_dim(value, 0, 1, axis=axis)
    return value


def exchange(value):
    axes = ("layer", "gx", "gy")
    sizes = [lax.axis_size(a) for a in axes]
    tile = {1: value.shape[1], 2: value.shape[2]}
    pieces = {}
    for layer_step in (0, 1):
        for step_x, kinds_x in _halo_options(sizes[1]):
            along_x = jnp.concatenate([_region(value, r, 1) for r in kinds_x], axis=1)
            for step_y, kinds_y in _halo_options(sizes[2]):
                part = jnp.concatenate([_region(along_x, r, 2) for r in kinds_y], axis=2)
                if (layer_step, step_x, step_y) != (0, 0, 0):
                    pairs = []
                    for l in range(sizes[0]):
                        for x in range(sizes[1]):
                            for y in range(sizes[2]):
                                src = (l * sizes[1] + x) * sizes[2] + y
                                dst_l = (l - layer_step) % sizes[0]
                                dst_x = (x - step_x) % sizes[1]
                                dst_y = (y - step_y) % sizes[2]
                                pairs.append((src, (dst_l * sizes[1] + dst_x) * sizes[2] + dst_y))
                    part = lax.ppermute(part, axes, pairs)
                at_x = 0
                for rx in kinds_x:
                    wide_x = tile[1] if rx == "all" else 1
                    at_y = 0
                    for ry in kinds_y:
                        wide_y = tile[2] if ry == "all" else 1
                        pieces[(layer_step, rx, ry)] = part[:, at_x : at_x + wide_x, at_y : at_y + wide_y]
                        at_y += wide_y
                    at_x += wide_x
    order = ("last", "all", "first")
    layers = []
    for layer_step in (0, 1):
        rows = [
            jnp.concatenate([pieces[(layer_step, rx, ry)] for ry in order], axis=2) for rx in order
        ]
        layers.append(jnp.concatenate(rows, axis=1))
    return jnp.concatenate(layers, axis=0)


def body(prev_vec, cur_vec, displace, potential):
    layer_id = lax.axis_index("layer")
    tile_x = displace.shape[1]
    tile_y = displace.shape[2]
    cos_twist = math.cos(twist_angle)
    sin_twist = math.sin(twist_angle)
    packed = exchange(jnp.concatenate([cur_vec, displace], axis=-2))
    vec_ext = packed[..., : cur_vec.shape[-2], :]
    ext_disp = packed[..., cur_vec.shape[-2] :, :]
    layer_up = layer_id == 1
    cos_vals = jnp.stack(
        [jnp.where(layer_up, cos_twist, 1.0), jnp.where(layer_up, 1.0, cos_twist)]
    ).astype(jnp.float32)
    sin_vals = jnp.stack(
        [jnp.where(layer_up, sin_twist, 0.0), jnp.where(layer_up, 0.0, sin_twist)]
    ).astype(jnp.float32)
    places = ext_disp + lattice(cos_vals, sin_vals)[:, None, None]
    row_count = tile_x * lax.axis_size("gx")
    col_count = tile_y * lax.axis_size("gy")
    row_ids = (
        lax.axis_index("gx") * tile_x + jnp.arange(tile_x + 2, dtype=jnp.int32) - 1 + row_count
    ) % row_count
    col_ids = (
        lax.axis_index("gy") * tile_y + jnp.arange(tile_y + 2, dtype=jnp.int32) - 1 + col_count
    ) % col_count
    turn = twist_offsets(cos_vals, sin_vals, row_ids, col_ids)
    twisted = places + turn

    def own_view(value, a, b):
        return value[:, 1 + a : 1 + a + tile_x, 1 + b : 1 + b + tile_y]

    own_pos = own_view(places[:1], 0, 0)[0]
    own_shift = own_view(turn[:1], 0, 0)[0]
    cos_own = cos_vals[0]
    sin_own = sin_vals[0]
    narrow = [o for o in OFFSETS if len(REACH[o][0]) < 64]
    narrow_rows = np.concatenate([REACH[o][0] for o in narrow])
    picked = jnp.einsum("...q,qk->...k", own_pos, _one_hot(narrow_rows), precision=HI)
    blocks = {}
    columns = {}
    at = 0
    for a, b in OFFSETS:
        rows, cols = REACH[(a, b)]
        if len(rows) < 64:
            own_rows = picked[..., at : at + len(rows)]
            at += len(rows)
            cols = np.arange(128)
        else:
            own_rows = pick(own_pos, rows)
        shift_x = cos_own * (a * cell_w) - sin_own * (b * cell_h)
        shift_y = sin_own * (a * cell_w) + cos_own * (b * cell_h)
        near_pos = pick(own_view(places[:1], a, b)[0], cols)
        near_twist = pick(own_view(twisted[1:], a, b)[0], cols)
        plane = plane_block(own_rows, near_pos, shift_x, shift_y, a == 0 and b == 0)
        inter = inter_block(own_rows + own_shift, near_twist, a * cell_w, b * cell_h)
        blocks[(a, b)] = (plane, inter)
        columns[(a, b)] = cols
    blocks = lax.optimization_barrier(blocks)

    scatter = np.zeros((len(narrow_rows), 128), np.float32)
    scatter[np.arange(len(narrow_rows)), narrow_rows] = 1.0

    def hop_terms(vectors, extended):
        full = potential[0][..., None, :] * vectors[0]
        parts = {}
        for a, b in OFFSETS:
            plane, inter = blocks[(a, b)]
            near = pick(own_view(extended, a, b), columns[(a, b)])
            summed = jnp.einsum("xycq,xypq->xycp", near[0], plane, precision=MID)
            parts[(a, b)] = summed + jnp.einsum("xycq,xypq->xycp", near[1], inter, precision=MID)
        full = full + parts[(0, 0)]
        full = full + jnp.concatenate([parts[(-1, 0)], parts[(1, 0)]], axis=-1)
        full = full + jnp.einsum(
            "xycp,pn->xycn", jnp.concatenate([parts[o] for o in narrow], axis=-1), scatter, precision=MID
        )
        return (full / hop_scale)[None]

    first_term = 2.0 * hop_terms(cur_vec, vec_ext) - prev_vec
    second_term = 2.0 * hop_terms(first_term, exchange(first_term)) - cur_vec
    return (first_term, second_term)


def solution(mesh):
    in_specs = (
        P("layer", "gx", "gy", None, None),
        P("layer", "gx", "gy", None, None),
        P("layer", "gx", "gy", None, None),
        P("layer", "gx", "gy", None),
    )
    out_specs = (P("layer", "gx", "gy", None, None), P("layer", "gx", "gy", None, None))
    return jax.shard_map(body, mesh=mesh, in_specs=in_specs, out_specs=out_specs, check_vma=False)
```

```python
import math

import jax
import jax.numpy as jnp
import numpy as np
from jax import lax
from jax.sharding import PartitionSpec as P

PATCH_X = 14
PATCH_Y = 4


v_pi = -2.7
v_sigma = 0.48
decay_len = 0.319
layer_gap = 3.35 / 1.42
cut_radius = 3.5
hop_scale = 12.0
twist_angle = 1.05 * math.pi / 180.0
root_three = math.sqrt(3.0)
cell_w = 4.0 * root_three
cell_h = 24.0
sigma_gain = v_sigma * math.exp((layer_gap - 1.0) / decay_len)
HI = lax.Precision.HIGHEST
MID = lax.Precision.HIGH
OFFSETS = [(a, b) for a in (-1, 0, 1) for b in (-1, 0, 1)]


def _base_np():
    orbital = np.arange(128)
    sub = orbital % 4
    cell = orbital // 4
    inner_x = np.where((sub == 1) | (sub == 2), root_three / 2.0, 0.0)
    inner_y = np.select([sub == 1, sub == 2, sub == 3], [0.5, 1.5, 2.0], 0.0)
    return np.stack([(cell // 8) * root_three + inner_x - cell_w / 2.0, (cell % 8) * 3.0 + inner_y - cell_h / 2.0])


def _reach_sets():
    base = _base_np()
    c, s = math.cos(twist_angle), math.sin(twist_angle)
    rot = np.array([[c, -s], [s, c]])
    margin = 0.5
    plane_r = cut_radius + margin
    inter_r = math.sqrt(cut_radius**2 - layer_gap**2) + margin
    twists = [
        np.array([[cell_w * (i - (PATCH_X - 1) / 2.0)], [cell_h * (j - (PATCH_Y - 1) / 2.0)]])
        for i in range(PATCH_X)
        for j in range(PATCH_Y)
    ]
    sets = {}
    for a, b in OFFSETS:
        shift = np.array([[a * cell_w], [b * cell_h]])
        gap = base[:, :, None] - base[:, None, :] - shift[:, :, None]
        mask = np.sqrt((gap**2).sum(0)) < plane_r
        for e in twists:
            turned = rot @ base + (rot - np.eye(2)) @ e
            for own, near in ((base, turned), (turned, base)):
                gap = own[:, :, None] - near[:, None, :] - shift[:, :, None]
                mask |= np.sqrt((gap**2).sum(0)) < inter_r
        sets[(a, b)] = (np.nonzero(mask.any(1))[0], np.nonzero(mask.any(0))[0])
    return sets


REACH = _reach_sets()


def _one_hot(idx):
    table = np.zeros((128, len(idx)), np.float32)
    table[idx, np.arange(len(idx))] = 1.0
    return table


def pick(x, idx):
    if len(idx) == x.shape[-1]:
        return x
    if np.all(np.diff(idx) == 1):
        return x[..., idx[0] : idx[0] + len(idx)]
    return jnp.einsum("...q,qk->...k", x, _one_hot(idx), precision=HI)


def extended_2(value, sides, width):
    for axis, dim in sides:
        devices, length = (lax.axis_size(axis), value.shape[dim])
        up = [(i, (i + 1) % devices) for i in range(devices)]
        down = [(j, i) for i, j in up]
        last = lax.slice_in_dim(value, length - width, length, axis=dim)
        first = lax.slice_in_dim(value, 0, width, axis=dim)
        if devices == 2:
            both = lax.ppermute(jnp.concatenate([last, first], axis=dim), axis, up)
            before = lax.slice_in_dim(both, 0, width, axis=dim)
            after = lax.slice_in_dim(both, width, 2 * width, axis=dim)
        else:
            before = lax.ppermute(last, axis, up)
            after = lax.ppermute(first, axis, down)
        value = jnp.concatenate([before, value, after], axis=dim)
    return value


def partner_2(value, axis, distance):
    return lax.ppermute(value, axis, [(i, i ^ 1 << distance) for i in range(lax.axis_size(axis))])


def lattice(cos_vals, sin_vals):
    base = jnp.asarray(_base_np(), jnp.float32)
    rot_x = cos_vals[:, None] * base[0] - sin_vals[:, None] * base[1]
    rot_y = sin_vals[:, None] * base[0] + cos_vals[:, None] * base[1]
    return jnp.stack([rot_x, rot_y], axis=1)


def twist_offsets(cos_vals, sin_vals, row_ids, col_ids):
    along_x = cell_w * ((row_ids % PATCH_X).astype(jnp.float32) - (PATCH_X - 1) / 2.0)
    along_y = cell_h * ((col_ids % PATCH_Y).astype(jnp.float32) - (PATCH_Y - 1) / 2.0)
    cos_less = (cos_vals - 1.0)[:, None, None]
    sin_cast = sin_vals[:, None, None]
    shift_x = cos_less * along_x[None, :, None] - sin_cast * along_y[None, None, :]
    shift_y = sin_cast * along_x[None, :, None] + cos_less * along_y[None, None, :]
    return jnp.stack([shift_x, shift_y], axis=-1)[..., None]


def taper(dist_sq):
    scaled = dist_sq / (cut_radius * cut_radius)
    return jnp.maximum(1.0 - scaled * scaled, 0.0)


def plane_block(own_pos, near_pos, shift_x, shift_y, self_rows):
    delta_x = own_pos[..., 0, :, None] - near_pos[..., 0, None, :] - shift_x
    delta_y = own_pos[..., 1, :, None] - near_pos[..., 1, None, :] - shift_y
    dist_sq = delta_x * delta_x + delta_y * delta_y
    spread = jnp.sqrt(dist_sq)
    hopping = v_pi * jnp.exp(-(spread - 1.0) / decay_len) * taper(dist_sq)
    if self_rows:
        orbital = jnp.arange(128, dtype=jnp.int32)
        hopping = jnp.where(orbital[:, None] == orbital[None, :], 0.0, hopping)
    return hopping


def inter_block(own_pos, near_pos, shift_x, shift_y):
    delta_x = own_pos[..., 0, :, None] - near_pos[..., 0, None, :] - shift_x
    delta_y = own_pos[..., 1, :, None] - near_pos[..., 1, None, :] - shift_y
    dist_sq = delta_x * delta_x + delta_y * delta_y + layer_gap * layer_gap
    spread = jnp.sqrt(dist_sq)
    cosine_sq = layer_gap * layer_gap / dist_sq
    decay = jnp.exp(-(spread - 1.0) / decay_len)
    bonds = decay * (v_pi * (1.0 - cosine_sq) + sigma_gain * cosine_sq)
    return bonds * taper(dist_sq)


def exchange(value):
    stacked = jnp.concatenate([value, partner_2(value, "layer", 0)], axis=0)
    return extended_2(stacked, (("gx", 1), ("gy", 2)), 1)


def body(prev_vec, cur_vec, displace, potential):
    layer_id = lax.axis_index("layer")
    tile_x = displace.shape[1]
    tile_y = displace.shape[2]
    cos_twist = math.cos(twist_angle)
    sin_twist = math.sin(twist_angle)
    packed = exchange(jnp.concatenate([cur_vec, displace], axis=-2))
    vec_ext = packed[..., : cur_vec.shape[-2], :]
    ext_disp = packed[..., cur_vec.shape[-2] :, :]
    layer_up = layer_id == 1
    cos_vals = jnp.stack(
        [jnp.where(layer_up, cos_twist, 1.0), jnp.where(layer_up, 1.0, cos_twist)]
    ).astype(jnp.float32)
    sin_vals = jnp.stack(
        [jnp.where(layer_up, sin_twist, 0.0), jnp.where(layer_up, 0.0, sin_twist)]
    ).astype(jnp.float32)
    places = ext_disp + lattice(cos_vals, sin_vals)[:, None, None]
    row_count = tile_x * lax.axis_size("gx")
    col_count = tile_y * lax.axis_size("gy")
    row_ids = (
        lax.axis_index("gx") * tile_x + jnp.arange(tile_x + 2, dtype=jnp.int32) - 1 + row_count
    ) % row_count
    col_ids = (
        lax.axis_index("gy") * tile_y + jnp.arange(tile_y + 2, dtype=jnp.int32) - 1 + col_count
    ) % col_count
    turn = twist_offsets(cos_vals, sin_vals, row_ids, col_ids)
    twisted = places + turn

    def own_view(value, a, b):
        return value[:, 1 + a : 1 + a + tile_x, 1 + b : 1 + b + tile_y]

    own_pos = own_view(places[:1], 0, 0)[0]
    own_shift = own_view(turn[:1], 0, 0)[0]
    cos_own = cos_vals[0]
    sin_own = sin_vals[0]
    narrow = [o for o in OFFSETS if len(REACH[o][0]) < 64]
    narrow_rows = np.concatenate([REACH[o][0] for o in narrow])
    picked = jnp.einsum("...q,qk->...k", own_pos, _one_hot(narrow_rows), precision=HI)
    blocks = {}
    columns = {}
    at = 0
    for a, b in OFFSETS:
        rows, cols = REACH[(a, b)]
        if len(rows) < 64:
            own_rows = picked[..., at : at + len(rows)]
            at += len(rows)
            cols = np.arange(128)
        else:
            own_rows = pick(own_pos, rows)
        shift_x = cos_own * (a * cell_w) - sin_own * (b * cell_h)
        shift_y = sin_own * (a * cell_w) + cos_own * (b * cell_h)
        near_pos = pick(own_view(places[:1], a, b)[0], cols)
        near_twist = pick(own_view(twisted[1:], a, b)[0], cols)
        plane = plane_block(own_rows, near_pos, shift_x, shift_y, a == 0 and b == 0)
        inter = inter_block(own_rows + own_shift, near_twist, a * cell_w, b * cell_h)
        blocks[(a, b)] = (plane, inter)
        columns[(a, b)] = cols
    blocks = lax.optimization_barrier(blocks)

    scatter = np.zeros((len(narrow_rows), 128), np.float32)
    scatter[np.arange(len(narrow_rows)), narrow_rows] = 1.0

    def hop_terms(vectors, extended):
        full = potential[0][..., None, :] * vectors[0]
        parts = {}
        for a, b in OFFSETS:
            plane, inter = blocks[(a, b)]
            near = pick(own_view(extended, a, b), columns[(a, b)])
            summed = jnp.einsum("xycq,xypq->xycp", near[0], plane, precision=MID)
            parts[(a, b)] = summed + jnp.einsum("xycq,xypq->xycp", near[1], inter, precision=MID)
        full = full + parts[(0, 0)]
        full = full + jnp.concatenate([parts[(-1, 0)], parts[(1, 0)]], axis=-1)
        full = full + jnp.einsum(
            "xycp,pn->xycn", jnp.concatenate([parts[o] for o in narrow], axis=-1), scatter, precision=MID
        )
        return (full / hop_scale)[None]

    first_term = 2.0 * hop_terms(cur_vec, vec_ext) - prev_vec
    second_term = 2.0 * hop_terms(first_term, exchange(first_term)) - cur_vec
    return (first_term, second_term)


def solution(mesh):
    in_specs = (
        P("layer", "gx", "gy", None, None),
        P("layer", "gx", "gy", None, None),
        P("layer", "gx", "gy", None, None),
        P("layer", "gx", "gy", None),
    )
    out_specs = (P("layer", "gx", "gy", None, None), P("layer", "gx", "gy", None, None))
    return jax.shard_map(body, mesh=mesh, in_specs=in_specs, out_specs=out_specs, check_vma=False)
```

```python
import math

import jax
import jax.numpy as jnp
import numpy as np
from jax import lax
from jax.sharding import PartitionSpec as P

PATCH_X = 14
PATCH_Y = 4


v_pi = -2.7
v_sigma = 0.48
decay_len = 0.319
layer_gap = 3.35 / 1.42
cut_radius = 3.5
hop_scale = 12.0
twist_angle = 1.05 * math.pi / 180.0
root_three = math.sqrt(3.0)
cell_w = 4.0 * root_three
cell_h = 24.0
sigma_gain = v_sigma * math.exp((layer_gap - 1.0) / decay_len)
HI = lax.Precision.HIGHEST
MID = lax.Precision.HIGH
OFFSETS = [(a, b) for a in (-1, 0, 1) for b in (-1, 0, 1)]


def _base_np():
    orbital = np.arange(128)
    sub = orbital % 4
    cell = orbital // 4
    inner_x = np.where((sub == 1) | (sub == 2), root_three / 2.0, 0.0)
    inner_y = np.select([sub == 1, sub == 2, sub == 3], [0.5, 1.5, 2.0], 0.0)
    return np.stack([(cell // 8) * root_three + inner_x - cell_w / 2.0, (cell % 8) * 3.0 + inner_y - cell_h / 2.0])


def _reach_sets():
    base = _base_np()
    c, s = math.cos(twist_angle), math.sin(twist_angle)
    rot = np.array([[c, -s], [s, c]])
    margin = 0.5
    plane_r = cut_radius + margin
    inter_r = math.sqrt(cut_radius**2 - layer_gap**2) + margin
    twists = [
        np.array([[cell_w * (i - (PATCH_X - 1) / 2.0)], [cell_h * (j - (PATCH_Y - 1) / 2.0)]])
        for i in range(PATCH_X)
        for j in range(PATCH_Y)
    ]
    sets = {}
    for a, b in OFFSETS:
        shift = np.array([[a * cell_w], [b * cell_h]])
        gap = base[:, :, None] - base[:, None, :] - shift[:, :, None]
        mask = np.sqrt((gap**2).sum(0)) < plane_r
        for e in twists:
            turned = rot @ base + (rot - np.eye(2)) @ e
            for own, near in ((base, turned), (turned, base)):
                gap = own[:, :, None] - near[:, None, :] - shift[:, :, None]
                mask |= np.sqrt((gap**2).sum(0)) < inter_r
        sets[(a, b)] = (np.nonzero(mask.any(1))[0], np.nonzero(mask.any(0))[0])
    return sets


REACH = _reach_sets()


def _one_hot(idx):
    table = np.zeros((128, len(idx)), np.float32)
    table[idx, np.arange(len(idx))] = 1.0
    return table


def pick(x, idx):
    if len(idx) == x.shape[-1]:
        return x
    if np.all(np.diff(idx) == 1):
        return x[..., idx[0] : idx[0] + len(idx)]
    return jnp.einsum("...q,qk->...k", x, _one_hot(idx), precision=HI)


def extended_2(value, sides, width):
    for axis, dim in sides:
        devices, length = (lax.axis_size(axis), value.shape[dim])
        up = [(i, (i + 1) % devices) for i in range(devices)]
        down = [(j, i) for i, j in up]
        last = lax.slice_in_dim(value, length - width, length, axis=dim)
        first = lax.slice_in_dim(value, 0, width, axis=dim)
        if devices == 2:
            both = lax.ppermute(jnp.concatenate([last, first], axis=dim), axis, up)
            before = lax.slice_in_dim(both, 0, width, axis=dim)
            after = lax.slice_in_dim(both, width, 2 * width, axis=dim)
        else:
            before = lax.ppermute(last, axis, up)
            after = lax.ppermute(first, axis, down)
        value = jnp.concatenate([before, value, after], axis=dim)
    return value


def partner_2(value, axis, distance):
    return lax.ppermute(value, axis, [(i, i ^ 1 << distance) for i in range(lax.axis_size(axis))])


def lattice(cos_vals, sin_vals):
    base = jnp.asarray(_base_np(), jnp.float32)
    rot_x = cos_vals[:, None] * base[0] - sin_vals[:, None] * base[1]
    rot_y = sin_vals[:, None] * base[0] + cos_vals[:, None] * base[1]
    return jnp.stack([rot_x, rot_y], axis=1)


def twist_offsets(cos_vals, sin_vals, row_ids, col_ids):
    along_x = cell_w * ((row_ids % PATCH_X).astype(jnp.float32) - (PATCH_X - 1) / 2.0)
    along_y = cell_h * ((col_ids % PATCH_Y).astype(jnp.float32) - (PATCH_Y - 1) / 2.0)
    cos_less = (cos_vals - 1.0)[:, None, None]
    sin_cast = sin_vals[:, None, None]
    shift_x = cos_less * along_x[None, :, None] - sin_cast * along_y[None, None, :]
    shift_y = sin_cast * along_x[None, :, None] + cos_less * along_y[None, None, :]
    return jnp.stack([shift_x, shift_y], axis=-1)[..., None]


def taper(dist_sq):
    scaled = dist_sq / (cut_radius * cut_radius)
    return jnp.maximum(1.0 - scaled * scaled, 0.0)


def plane_block(own_pos, near_pos, shift_x, shift_y, self_rows):
    delta_x = own_pos[..., 0, :, None] - near_pos[..., 0, None, :] - shift_x
    delta_y = own_pos[..., 1, :, None] - near_pos[..., 1, None, :] - shift_y
    dist_sq = delta_x * delta_x + delta_y * delta_y
    spread = jnp.sqrt(dist_sq)
    hopping = v_pi * jnp.exp(-(spread - 1.0) / decay_len) * taper(dist_sq)
    if self_rows:
        orbital = jnp.arange(128, dtype=jnp.int32)
        hopping = jnp.where(orbital[:, None] == orbital[None, :], 0.0, hopping)
    return hopping


def inter_block(own_pos, near_pos, shift_x, shift_y):
    delta_x = own_pos[..., 0, :, None] - near_pos[..., 0, None, :] - shift_x
    delta_y = own_pos[..., 1, :, None] - near_pos[..., 1, None, :] - shift_y
    dist_sq = delta_x * delta_x + delta_y * delta_y + layer_gap * layer_gap
    spread = jnp.sqrt(dist_sq)
    cosine_sq = layer_gap * layer_gap / dist_sq
    decay = jnp.exp(-(spread - 1.0) / decay_len)
    bonds = decay * (v_pi * (1.0 - cosine_sq) + sigma_gain * cosine_sq)
    return bonds * taper(dist_sq)


def exchange(value):
    stacked = jnp.concatenate([value, partner_2(value, "layer", 0)], axis=0)
    rows = extended_2(stacked, (("gx", 1),), 1)
    return stacked, rows, extended_2(rows, (("gy", 2),), 1)


def near_view(stages, a, b):
    stacked, rows, full = stages
    tile_x, tile_y = stacked.shape[1], stacked.shape[2]
    if a == 0 and b == 0:
        return stacked
    if b == 0:
        return rows[:, 1 + a : 1 + a + tile_x]
    return full[:, 1 + a : 1 + a + tile_x, 1 + b : 1 + b + tile_y]


def body(prev_vec, cur_vec, displace, potential):
    layer_id = lax.axis_index("layer")
    tile_x = displace.shape[1]
    tile_y = displace.shape[2]
    cos_twist = math.cos(twist_angle)
    sin_twist = math.sin(twist_angle)
    width = cur_vec.shape[-2]
    packed = exchange(jnp.concatenate([cur_vec, displace], axis=-2))
    vec_stages = tuple(s[..., :width, :] for s in packed)
    disp_stages = tuple(s[..., width:, :] for s in packed)
    layer_up = layer_id == 1
    cos_vals = jnp.stack(
        [jnp.where(layer_up, cos_twist, 1.0), jnp.where(layer_up, 1.0, cos_twist)]
    ).astype(jnp.float32)
    sin_vals = jnp.stack(
        [jnp.where(layer_up, sin_twist, 0.0), jnp.where(layer_up, 0.0, sin_twist)]
    ).astype(jnp.float32)
    grid = lattice(cos_vals, sin_vals)[:, None, None]
    row_count = tile_x * lax.axis_size("gx")
    col_count = tile_y * lax.axis_size("gy")
    row_ids = (
        lax.axis_index("gx") * tile_x + jnp.arange(tile_x + 2, dtype=jnp.int32) - 1 + row_count
    ) % row_count
    col_ids = (
        lax.axis_index("gy") * tile_y + jnp.arange(tile_y + 2, dtype=jnp.int32) - 1 + col_count
    ) % col_count
    turn = twist_offsets(cos_vals, sin_vals, row_ids, col_ids)

    def own_view(value, a, b):
        return value[:, 1 + a : 1 + a + tile_x, 1 + b : 1 + b + tile_y]

    own_pos = disp_stages[0][0] + grid[0]
    own_shift = own_view(turn[:1], 0, 0)[0]
    cos_own = cos_vals[0]
    sin_own = sin_vals[0]
    narrow = [o for o in OFFSETS if len(REACH[o][0]) < 64]
    narrow_rows = np.concatenate([REACH[o][0] for o in narrow])
    picked = jnp.einsum("...q,qk->...k", own_pos, _one_hot(narrow_rows), precision=HI)
    blocks = {}
    columns = {}
    at = 0
    for a, b in OFFSETS:
        rows, cols = REACH[(a, b)]
        if len(rows) < 64:
            own_rows = picked[..., at : at + len(rows)]
            at += len(rows)
            cols = np.arange(128)
        else:
            own_rows = pick(own_pos, rows)
        shift_x = cos_own * (a * cell_w) - sin_own * (b * cell_h)
        shift_y = sin_own * (a * cell_w) + cos_own * (b * cell_h)
        near_places = near_view(disp_stages, a, b) + grid
        near_pos = pick(near_places[0], cols)
        near_twist = pick(near_places[1] + own_view(turn[1:], a, b)[0], cols)
        plane = plane_block(own_rows, near_pos, shift_x, shift_y, a == 0 and b == 0)
        inter = inter_block(own_rows + own_shift, near_twist, a * cell_w, b * cell_h)
        blocks[(a, b)] = lax.optimization_barrier((plane, inter))
        columns[(a, b)] = cols

    scatter = np.zeros((len(narrow_rows), 128), np.float32)
    scatter[np.arange(len(narrow_rows)), narrow_rows] = 1.0

    def hop_terms(vectors, stages):
        full = potential[0][..., None, :] * vectors[0]
        parts = {}
        for a, b in OFFSETS:
            plane, inter = blocks[(a, b)]
            near = pick(near_view(stages, a, b), columns[(a, b)])
            summed = jnp.einsum("xycq,xypq->xycp", near[0], plane, precision=MID)
            parts[(a, b)] = summed + jnp.einsum("xycq,xypq->xycp", near[1], inter, precision=MID)
        full = full + parts[(0, 0)]
        full = full + jnp.concatenate([parts[(-1, 0)], parts[(1, 0)]], axis=-1)
        full = full + jnp.einsum(
            "xycp,pn->xycn", jnp.concatenate([parts[o] for o in narrow], axis=-1), scatter, precision=MID
        )
        return (full / hop_scale)[None]

    first_term = 2.0 * hop_terms(cur_vec, vec_stages) - prev_vec
    second_term = 2.0 * hop_terms(first_term, exchange(first_term)) - cur_vec
    return (first_term, second_term)


def solution(mesh):
    in_specs = (
        P("layer", "gx", "gy", None, None),
        P("layer", "gx", "gy", None, None),
        P("layer", "gx", "gy", None, None),
        P("layer", "gx", "gy", None),
    )
    out_specs = (P("layer", "gx", "gy", None, None), P("layer", "gx", "gy", None, None))
    return jax.shard_map(body, mesh=mesh, in_specs=in_specs, out_specs=out_specs, check_vma=False)
```

```python
import math

import jax
import jax.numpy as jnp
import numpy as np
from jax import lax
from jax.sharding import PartitionSpec as P

PATCH_X = 14
PATCH_Y = 4


v_pi = -2.7
v_sigma = 0.48
decay_len = 0.319
layer_gap = 3.35 / 1.42
cut_radius = 3.5
hop_scale = 12.0
twist_angle = 1.05 * math.pi / 180.0
root_three = math.sqrt(3.0)
cell_w = 4.0 * root_three
cell_h = 24.0
sigma_gain = v_sigma * math.exp((layer_gap - 1.0) / decay_len)
HI = lax.Precision.HIGHEST
MID = lax.Precision.HIGH
OFFSETS = [(a, b) for a in (-1, 0, 1) for b in (-1, 0, 1)]


def _base_np():
    orbital = np.arange(128)
    sub = orbital % 4
    cell = orbital // 4
    inner_x = np.where((sub == 1) | (sub == 2), root_three / 2.0, 0.0)
    inner_y = np.select([sub == 1, sub == 2, sub == 3], [0.5, 1.5, 2.0], 0.0)
    return np.stack([(cell // 8) * root_three + inner_x - cell_w / 2.0, (cell % 8) * 3.0 + inner_y - cell_h / 2.0])


def _reach_sets():
    base = _base_np()
    c, s = math.cos(twist_angle), math.sin(twist_angle)
    rot = np.array([[c, -s], [s, c]])
    margin = 0.5
    plane_r = cut_radius + margin
    inter_r = math.sqrt(cut_radius**2 - layer_gap**2) + margin
    twists = [
        np.array([[cell_w * (i - (PATCH_X - 1) / 2.0)], [cell_h * (j - (PATCH_Y - 1) / 2.0)]])
        for i in range(PATCH_X)
        for j in range(PATCH_Y)
    ]
    sets = {}
    for a, b in OFFSETS:
        shift = np.array([[a * cell_w], [b * cell_h]])
        gap = base[:, :, None] - base[:, None, :] - shift[:, :, None]
        mask = np.sqrt((gap**2).sum(0)) < plane_r
        for e in twists:
            turned = rot @ base + (rot - np.eye(2)) @ e
            for own, near in ((base, turned), (turned, base)):
                gap = own[:, :, None] - near[:, None, :] - shift[:, :, None]
                mask |= np.sqrt((gap**2).sum(0)) < inter_r
        sets[(a, b)] = (np.nonzero(mask.any(1))[0], np.nonzero(mask.any(0))[0])
    return sets


REACH = _reach_sets()


def _one_hot(idx):
    table = np.zeros((128, len(idx)), np.float32)
    table[idx, np.arange(len(idx))] = 1.0
    return table


def pick(x, idx):
    if len(idx) == x.shape[-1]:
        return x
    if np.all(np.diff(idx) == 1):
        return x[..., idx[0] : idx[0] + len(idx)]
    return jnp.einsum("...q,qk->...k", x, _one_hot(idx), precision=HI)


def extended_2(value, sides, width):
    for axis, dim in sides:
        devices, length = (lax.axis_size(axis), value.shape[dim])
        up = [(i, (i + 1) % devices) for i in range(devices)]
        down = [(j, i) for i, j in up]
        last = lax.slice_in_dim(value, length - width, length, axis=dim)
        first = lax.slice_in_dim(value, 0, width, axis=dim)
        if devices == 2:
            both = lax.ppermute(jnp.concatenate([last, first], axis=dim), axis, up)
            before = lax.slice_in_dim(both, 0, width, axis=dim)
            after = lax.slice_in_dim(both, width, 2 * width, axis=dim)
        else:
            before = lax.ppermute(last, axis, up)
            after = lax.ppermute(first, axis, down)
        value = jnp.concatenate([before, value, after], axis=dim)
    return value


def partner_2(value, axis, distance):
    return lax.ppermute(value, axis, [(i, i ^ 1 << distance) for i in range(lax.axis_size(axis))])


def lattice(cos_vals, sin_vals):
    base = jnp.asarray(_base_np(), jnp.float32)
    rot_x = cos_vals[:, None] * base[0] - sin_vals[:, None] * base[1]
    rot_y = sin_vals[:, None] * base[0] + cos_vals[:, None] * base[1]
    return jnp.stack([rot_x, rot_y], axis=1)


def twist_offsets(cos_vals, sin_vals, row_ids, col_ids):
    along_x = cell_w * ((row_ids % PATCH_X).astype(jnp.float32) - (PATCH_X - 1) / 2.0)
    along_y = cell_h * ((col_ids % PATCH_Y).astype(jnp.float32) - (PATCH_Y - 1) / 2.0)
    cos_less = (cos_vals - 1.0)[:, None, None]
    sin_cast = sin_vals[:, None, None]
    shift_x = cos_less * along_x[None, :, None] - sin_cast * along_y[None, None, :]
    shift_y = sin_cast * along_x[None, :, None] + cos_less * along_y[None, None, :]
    return jnp.stack([shift_x, shift_y], axis=-1)[..., None]


def taper(dist_sq):
    scaled = dist_sq / (cut_radius * cut_radius)
    return jnp.maximum(1.0 - scaled * scaled, 0.0)


def plane_block(own_pos, near_pos, shift_x, shift_y, self_rows):
    delta_x = own_pos[..., 0, :, None] - near_pos[..., 0, None, :] - shift_x
    delta_y = own_pos[..., 1, :, None] - near_pos[..., 1, None, :] - shift_y
    dist_sq = delta_x * delta_x + delta_y * delta_y
    spread = jnp.sqrt(dist_sq)
    hopping = v_pi * jnp.exp(-(spread - 1.0) / decay_len) * taper(dist_sq)
    if self_rows:
        orbital = jnp.arange(128, dtype=jnp.int32)
        hopping = jnp.where(orbital[:, None] == orbital[None, :], 0.0, hopping)
    return hopping


def inter_block(own_pos, near_pos, shift_x, shift_y):
    delta_x = own_pos[..., 0, :, None] - near_pos[..., 0, None, :] - shift_x
    delta_y = own_pos[..., 1, :, None] - near_pos[..., 1, None, :] - shift_y
    dist_sq = delta_x * delta_x + delta_y * delta_y + layer_gap * layer_gap
    spread = jnp.sqrt(dist_sq)
    cosine_sq = layer_gap * layer_gap / dist_sq
    decay = jnp.exp(-(spread - 1.0) / decay_len)
    bonds = decay * (v_pi * (1.0 - cosine_sq) + sigma_gain * cosine_sq)
    return bonds * taper(dist_sq)


def _halo_options(n):
    if n == 1:
        return [(0, ("last", "all", "first"))]
    if n == 2:
        return [(0, ("all",)), (1, ("last", "first"))]
    return [(-1, ("last",)), (0, ("all",)), (1, ("first",))]


def _region(value, kind, axis):
    length = value.shape[axis]
    if kind == "last":
        return lax.slice_in_dim(value, length - 1, length, axis=axis)
    if kind == "first":
        return lax.slice_in_dim(value, 0, 1, axis=axis)
    return value


def exchange(value):
    stacked = jnp.concatenate([value, partner_2(value, "layer", 0)], axis=0)
    axes = ("gx", "gy")
    sizes = [lax.axis_size(a) for a in axes]
    tile = {1: stacked.shape[1], 2: stacked.shape[2]}
    pieces = {}
    for step_x, kinds_x in _halo_options(sizes[0]):
        along_x = jnp.concatenate([_region(stacked, r, 1) for r in kinds_x], axis=1)
        for step_y, kinds_y in _halo_options(sizes[1]):
            part = jnp.concatenate([_region(along_x, r, 2) for r in kinds_y], axis=2)
            if (step_x, step_y) != (0, 0):
                pairs = []
                for x in range(sizes[0]):
                    for y in range(sizes[1]):
                        dst = ((x - step_x) % sizes[0]) * sizes[1] + (y - step_y) % sizes[1]
                        pairs.append((x * sizes[1] + y, dst))
                part = lax.ppermute(part, axes, pairs)
            at_x = 0
            for rx in kinds_x:
                wide_x = tile[1] if rx == "all" else 1
                at_y = 0
                for ry in kinds_y:
                    wide_y = tile[2] if ry == "all" else 1
                    pieces[(rx, ry)] = part[:, at_x : at_x + wide_x, at_y : at_y + wide_y]
                    at_y += wide_y
                at_x += wide_x
    order = ("last", "all", "first")
    rows = [jnp.concatenate([pieces[(rx, ry)] for ry in order], axis=2) for rx in order]
    return jnp.concatenate(rows, axis=1)


def body(prev_vec, cur_vec, displace, potential):
    layer_id = lax.axis_index("layer")
    tile_x = displace.shape[1]
    tile_y = displace.shape[2]
    cos_twist = math.cos(twist_angle)
    sin_twist = math.sin(twist_angle)
    packed = exchange(jnp.concatenate([cur_vec, displace], axis=-2))
    vec_ext = packed[..., : cur_vec.shape[-2], :]
    ext_disp = packed[..., cur_vec.shape[-2] :, :]
    layer_up = layer_id == 1
    cos_vals = jnp.stack(
        [jnp.where(layer_up, cos_twist, 1.0), jnp.where(layer_up, 1.0, cos_twist)]
    ).astype(jnp.float32)
    sin_vals = jnp.stack(
        [jnp.where(layer_up, sin_twist, 0.0), jnp.where(layer_up, 0.0, sin_twist)]
    ).astype(jnp.float32)
    places = ext_disp + lattice(cos_vals, sin_vals)[:, None, None]
    row_count = tile_x * lax.axis_size("gx")
    col_count = tile_y * lax.axis_size("gy")
    row_ids = (
        lax.axis_index("gx") * tile_x + jnp.arange(tile_x + 2, dtype=jnp.int32) - 1 + row_count
    ) % row_count
    col_ids = (
        lax.axis_index("gy") * tile_y + jnp.arange(tile_y + 2, dtype=jnp.int32) - 1 + col_count
    ) % col_count
    turn = twist_offsets(cos_vals, sin_vals, row_ids, col_ids)
    twisted = places + turn

    def own_view(value, a, b):
        return value[:, 1 + a : 1 + a + tile_x, 1 + b : 1 + b + tile_y]

    own_pos = own_view(places[:1], 0, 0)[0]
    own_shift = own_view(turn[:1], 0, 0)[0]
    cos_own = cos_vals[0]
    sin_own = sin_vals[0]
    narrow = [o for o in OFFSETS if len(REACH[o][0]) < 64]
    narrow_rows = np.concatenate([REACH[o][0] for o in narrow])
    picked = jnp.einsum("...q,qk->...k", own_pos, _one_hot(narrow_rows), precision=HI)
    blocks = {}
    columns = {}
    at = 0
    for a, b in OFFSETS:
        rows, cols = REACH[(a, b)]
        if len(rows) < 64:
            own_rows = picked[..., at : at + len(rows)]
            at += len(rows)
            cols = np.arange(128)
        else:
            own_rows = pick(own_pos, rows)
        shift_x = cos_own * (a * cell_w) - sin_own * (b * cell_h)
        shift_y = sin_own * (a * cell_w) + cos_own * (b * cell_h)
        near_pos = pick(own_view(places[:1], a, b)[0], cols)
        near_twist = pick(own_view(twisted[1:], a, b)[0], cols)
        plane = plane_block(own_rows, near_pos, shift_x, shift_y, a == 0 and b == 0)
        inter = inter_block(own_rows + own_shift, near_twist, a * cell_w, b * cell_h)
        blocks[(a, b)] = (plane, inter)
        columns[(a, b)] = cols
    blocks = lax.optimization_barrier(blocks)

    scatter = np.zeros((len(narrow_rows), 128), np.float32)
    scatter[np.arange(len(narrow_rows)), narrow_rows] = 1.0

    def hop_terms(vectors, extended):
        full = potential[0][..., None, :] * vectors[0]
        parts = {}
        for a, b in OFFSETS:
            plane, inter = blocks[(a, b)]
            near = pick(own_view(extended, a, b), columns[(a, b)])
            summed = jnp.einsum("xycq,xypq->xycp", near[0], plane, precision=MID)
            parts[(a, b)] = summed + jnp.einsum("xycq,xypq->xycp", near[1], inter, precision=MID)
        full = full + parts[(0, 0)]
        full = full + jnp.concatenate([parts[(-1, 0)], parts[(1, 0)]], axis=-1)
        full = full + jnp.einsum(
            "xycp,pn->xycn", jnp.concatenate([parts[o] for o in narrow], axis=-1), scatter, precision=MID
        )
        return (full / hop_scale)[None]

    first_term = 2.0 * hop_terms(cur_vec, vec_ext) - prev_vec
    second_term = 2.0 * hop_terms(first_term, exchange(first_term)) - cur_vec
    return (first_term, second_term)


def solution(mesh):
    in_specs = (
        P("layer", "gx", "gy", None, None),
        P("layer", "gx", "gy", None, None),
        P("layer", "gx", "gy", None, None),
        P("layer", "gx", "gy", None),
    )
    out_specs = (P("layer", "gx", "gy", None, None), P("layer", "gx", "gy", None, None))
    return jax.shard_map(body, mesh=mesh, in_specs=in_specs, out_specs=out_specs, check_vma=False)
```

```python
import math

import jax
import jax.numpy as jnp
import numpy as np
from jax import lax
from jax.sharding import PartitionSpec as P

PATCH_X = 14
PATCH_Y = 4


v_pi = -2.7
v_sigma = 0.48
decay_len = 0.319
layer_gap = 3.35 / 1.42
cut_radius = 3.5
hop_scale = 12.0
twist_angle = 1.05 * math.pi / 180.0
root_three = math.sqrt(3.0)
cell_w = 4.0 * root_three
cell_h = 24.0
sigma_gain = v_sigma * math.exp((layer_gap - 1.0) / decay_len)
HI = lax.Precision.HIGHEST
MID = lax.Precision.HIGH
OFFSETS = [(a, b) for a in (-1, 0, 1) for b in (-1, 0, 1)]


def _base_np():
    orbital = np.arange(128)
    sub = orbital % 4
    cell = orbital // 4
    inner_x = np.where((sub == 1) | (sub == 2), root_three / 2.0, 0.0)
    inner_y = np.select([sub == 1, sub == 2, sub == 3], [0.5, 1.5, 2.0], 0.0)
    return np.stack([(cell // 8) * root_three + inner_x - cell_w / 2.0, (cell % 8) * 3.0 + inner_y - cell_h / 2.0])


def _reach_sets():
    base = _base_np()
    c, s = math.cos(twist_angle), math.sin(twist_angle)
    rot = np.array([[c, -s], [s, c]])
    margin = 0.5
    plane_r = cut_radius + margin
    inter_r = math.sqrt(cut_radius**2 - layer_gap**2) + margin
    twists = [
        np.array([[cell_w * (i - (PATCH_X - 1) / 2.0)], [cell_h * (j - (PATCH_Y - 1) / 2.0)]])
        for i in range(PATCH_X)
        for j in range(PATCH_Y)
    ]
    sets = {}
    for a, b in OFFSETS:
        shift = np.array([[a * cell_w], [b * cell_h]])
        gap = base[:, :, None] - base[:, None, :] - shift[:, :, None]
        mask = np.sqrt((gap**2).sum(0)) < plane_r
        for e in twists:
            turned = rot @ base + (rot - np.eye(2)) @ e
            for own, near in ((base, turned), (turned, base)):
                gap = own[:, :, None] - near[:, None, :] - shift[:, :, None]
                mask |= np.sqrt((gap**2).sum(0)) < inter_r
        sets[(a, b)] = (np.nonzero(mask.any(1))[0], np.nonzero(mask.any(0))[0])
    return sets


REACH = _reach_sets()


def _one_hot(idx):
    table = np.zeros((128, len(idx)), np.float32)
    table[idx, np.arange(len(idx))] = 1.0
    return table


def pick(x, idx):
    if len(idx) == x.shape[-1]:
        return x
    if np.all(np.diff(idx) == 1):
        return x[..., idx[0] : idx[0] + len(idx)]
    return jnp.einsum("...q,qk->...k", x, _one_hot(idx), precision=HI)


def extended_2(value, sides, width):
    for axis, dim in sides:
        devices, length = (lax.axis_size(axis), value.shape[dim])
        up = [(i, (i + 1) % devices) for i in range(devices)]
        down = [(j, i) for i, j in up]
        last = lax.slice_in_dim(value, length - width, length, axis=dim)
        first = lax.slice_in_dim(value, 0, width, axis=dim)
        if devices == 2:
            both = lax.ppermute(jnp.concatenate([last, first], axis=dim), axis, up)
            before = lax.slice_in_dim(both, 0, width, axis=dim)
            after = lax.slice_in_dim(both, width, 2 * width, axis=dim)
        else:
            before = lax.ppermute(last, axis, up)
            after = lax.ppermute(first, axis, down)
        value = jnp.concatenate([before, value, after], axis=dim)
    return value


def partner_2(value, axis, distance):
    return lax.ppermute(value, axis, [(i, i ^ 1 << distance) for i in range(lax.axis_size(axis))])


def lattice(cos_vals, sin_vals):
    base = jnp.asarray(_base_np(), jnp.float32)
    rot_x = cos_vals[:, None] * base[0] - sin_vals[:, None] * base[1]
    rot_y = sin_vals[:, None] * base[0] + cos_vals[:, None] * base[1]
    return jnp.stack([rot_x, rot_y], axis=1)


def twist_offsets(cos_vals, sin_vals, row_ids, col_ids):
    along_x = cell_w * ((row_ids % PATCH_X).astype(jnp.float32) - (PATCH_X - 1) / 2.0)
    along_y = cell_h * ((col_ids % PATCH_Y).astype(jnp.float32) - (PATCH_Y - 1) / 2.0)
    cos_less = (cos_vals - 1.0)[:, None, None]
    sin_cast = sin_vals[:, None, None]
    shift_x = cos_less * along_x[None, :, None] - sin_cast * along_y[None, None, :]
    shift_y = sin_cast * along_x[None, :, None] + cos_less * along_y[None, None, :]
    return jnp.stack([shift_x, shift_y], axis=-1)[..., None]


def taper(dist_sq):
    scaled = dist_sq / (cut_radius * cut_radius)
    return jnp.maximum(1.0 - scaled * scaled, 0.0)


def plane_block(own_pos, near_pos, shift_x, shift_y, self_rows):
    delta_x = own_pos[..., 0, :, None] - near_pos[..., 0, None, :] - shift_x
    delta_y = own_pos[..., 1, :, None] - near_pos[..., 1, None, :] - shift_y
    dist_sq = delta_x * delta_x + delta_y * delta_y
    spread = jnp.sqrt(dist_sq)
    hopping = v_pi * jnp.exp(-(spread - 1.0) / decay_len) * taper(dist_sq)
    if self_rows:
        orbital = jnp.arange(128, dtype=jnp.int32)
        hopping = jnp.where(orbital[:, None] == orbital[None, :], 0.0, hopping)
    return hopping


def inter_block(own_pos, near_pos, shift_x, shift_y):
    delta_x = own_pos[..., 0, :, None] - near_pos[..., 0, None, :] - shift_x
    delta_y = own_pos[..., 1, :, None] - near_pos[..., 1, None, :] - shift_y
    dist_sq = delta_x * delta_x + delta_y * delta_y + layer_gap * layer_gap
    spread = jnp.sqrt(dist_sq)
    cosine_sq = layer_gap * layer_gap / dist_sq
    decay = jnp.exp(-(spread - 1.0) / decay_len)
    bonds = decay * (v_pi * (1.0 - cosine_sq) + sigma_gain * cosine_sq)
    return bonds * taper(dist_sq)


def _halo_options(n):
    if n == 1:
        return [(0, ("last", "all", "first"))]
    if n == 2:
        return [(0, ("all",)), (1, ("last", "first"))]
    return [(-1, ("last",)), (0, ("all",)), (1, ("first",))]


def _region(value, kind, axis):
    length = value.shape[axis]
    if kind == "last":
        return lax.slice_in_dim(value, length - 1, length, axis=axis)
    if kind == "first":
        return lax.slice_in_dim(value, 0, 1, axis=axis)
    return value


def exchange(value):
    stacked = jnp.concatenate([value, partner_2(value, "layer", 0)], axis=0)
    axes = ("gx", "gy")
    sizes = [lax.axis_size(a) for a in axes]
    tile = {1: stacked.shape[1], 2: stacked.shape[2]}
    pieces = {}
    for step_x, kinds_x in _halo_options(sizes[0]):
        along_x = jnp.concatenate([_region(stacked, r, 1) for r in kinds_x], axis=1)
        for step_y, kinds_y in _halo_options(sizes[1]):
            part = jnp.concatenate([_region(along_x, r, 2) for r in kinds_y], axis=2)
            if (step_x, step_y) != (0, 0):
                pairs = []
                for x in range(sizes[0]):
                    for y in range(sizes[1]):
                        dst = ((x - step_x) % sizes[0]) * sizes[1] + (y - step_y) % sizes[1]
                        pairs.append((x * sizes[1] + y, dst))
                part = lax.ppermute(part, axes, pairs)
            at_x = 0
            for rx in kinds_x:
                wide_x = tile[1] if rx == "all" else 1
                at_y = 0
                for ry in kinds_y:
                    wide_y = tile[2] if ry == "all" else 1
                    pieces[(rx, ry)] = part[:, at_x : at_x + wide_x, at_y : at_y + wide_y]
                    at_y += wide_y
                at_x += wide_x
    order = ("last", "all", "first")
    rows = [jnp.concatenate([pieces[(rx, ry)] for ry in order], axis=2) for rx in order]
    return jnp.concatenate(rows, axis=1)


def body(prev_vec, cur_vec, displace, potential):
    layer_id = lax.axis_index("layer")
    tile_x = displace.shape[1]
    tile_y = displace.shape[2]
    cos_twist = math.cos(twist_angle)
    sin_twist = math.sin(twist_angle)
    packed = exchange(jnp.concatenate([cur_vec, displace], axis=-2))
    vec_ext = packed[..., : cur_vec.shape[-2], :]
    ext_disp = packed[..., cur_vec.shape[-2] :, :]
    layer_up = layer_id == 1
    cos_vals = jnp.stack(
        [jnp.where(layer_up, cos_twist, 1.0), jnp.where(layer_up, 1.0, cos_twist)]
    ).astype(jnp.float32)
    sin_vals = jnp.stack(
        [jnp.where(layer_up, sin_twist, 0.0), jnp.where(layer_up, 0.0, sin_twist)]
    ).astype(jnp.float32)
    places = ext_disp + lattice(cos_vals, sin_vals)[:, None, None]
    row_count = tile_x * lax.axis_size("gx")
    col_count = tile_y * lax.axis_size("gy")
    row_ids = (
        lax.axis_index("gx") * tile_x + jnp.arange(tile_x + 2, dtype=jnp.int32) - 1 + row_count
    ) % row_count
    col_ids = (
        lax.axis_index("gy") * tile_y + jnp.arange(tile_y + 2, dtype=jnp.int32) - 1 + col_count
    ) % col_count
    turn = twist_offsets(cos_vals, sin_vals, row_ids, col_ids)
    twisted = places + turn

    def own_view(value, a, b):
        return value[:, 1 + a : 1 + a + tile_x, 1 + b : 1 + b + tile_y]

    own_pos = own_view(places[:1], 0, 0)[0]
    own_shift = own_view(turn[:1], 0, 0)[0]
    cos_own = cos_vals[0]
    sin_own = sin_vals[0]
    narrow = [o for o in OFFSETS if len(REACH[o][0]) < 64]
    narrow_rows = np.concatenate([REACH[o][0] for o in narrow])
    picked = jnp.einsum("...q,qk->...k", own_pos, _one_hot(narrow_rows), precision=HI)
    blocks = {}
    columns = {}
    at = 0
    for a, b in OFFSETS:
        rows, cols = REACH[(a, b)]
        if len(rows) < 64:
            own_rows = picked[..., at : at + len(rows)]
            at += len(rows)
            cols = np.arange(128)
        else:
            own_rows = pick(own_pos, rows)
        shift_x = cos_own * (a * cell_w) - sin_own * (b * cell_h)
        shift_y = sin_own * (a * cell_w) + cos_own * (b * cell_h)
        near_pos = pick(own_view(places[:1], a, b)[0], cols)
        near_twist = pick(own_view(twisted[1:], a, b)[0], cols)
        plane = plane_block(own_rows, near_pos, shift_x, shift_y, a == 0 and b == 0)
        inter = inter_block(own_rows + own_shift, near_twist, a * cell_w, b * cell_h)
        blocks[(a, b)] = jnp.stack([plane, inter])
        columns[(a, b)] = cols

    def widen(block, at, total):
        pad = [(0, 0)] * (block.ndim - 1) + [(at, total - at - block.shape[-1])]
        return jnp.pad(block, pad)

    halves = ((-1, 0), (1, 0))
    side_cols = [columns[o] for o in halves]
    side = jnp.concatenate(
        [widen(blocks[o], 128 * n + int(c[0]), 256) for n, (o, c) in enumerate(zip(halves, side_cols))],
        axis=-2,
    )
    edge = jnp.concatenate([widen(blocks[o], 128 * n, 128 * len(narrow)) for n, o in enumerate(narrow)], axis=-2)
    centre, side, edge = lax.optimization_barrier((blocks[(0, 0)], side, edge))

    scatter = np.zeros((len(narrow_rows), 128), np.float32)
    scatter[np.arange(len(narrow_rows)), narrow_rows] = 1.0

    def hop_terms(vectors, extended):
        full = potential[0][..., None, :] * vectors[0]
        near = own_view(extended, 0, 0)
        full = full + jnp.einsum("kxycq,kxypq->xycp", near, centre, precision=MID)
        near = jnp.concatenate([own_view(extended, a, b) for a, b in halves], axis=-1)
        full = full + jnp.einsum("kxycq,kxypq->xycp", near, side, precision=MID)
        near = jnp.concatenate([own_view(extended, a, b) for a, b in narrow], axis=-1)
        parts = jnp.einsum("kxycq,kxypq->xycp", near, edge, precision=MID)
        full = full + jnp.einsum("xycp,pn->xycn", parts, scatter, precision=MID)
        return (full / hop_scale)[None]

    first_term = 2.0 * hop_terms(cur_vec, vec_ext) - prev_vec
    second_term = 2.0 * hop_terms(first_term, exchange(first_term)) - cur_vec
    return (first_term, second_term)


def solution(mesh):
    in_specs = (
        P("layer", "gx", "gy", None, None),
        P("layer", "gx", "gy", None, None),
        P("layer", "gx", "gy", None, None),
        P("layer", "gx", "gy", None),
    )
    out_specs = (P("layer", "gx", "gy", None, None), P("layer", "gx", "gy", None, None))
    return jax.shard_map(body, mesh=mesh, in_specs=in_specs, out_specs=out_specs, check_vma=False)
```

```python
import math

import jax
import jax.numpy as jnp
import numpy as np
from jax import lax
from jax.sharding import PartitionSpec as P

PATCH_X = 14
PATCH_Y = 4


v_pi = -2.7
v_sigma = 0.48
decay_len = 0.319
layer_gap = 3.35 / 1.42
cut_radius = 3.5
hop_scale = 12.0
twist_angle = 1.05 * math.pi / 180.0
root_three = math.sqrt(3.0)
cell_w = 4.0 * root_three
cell_h = 24.0
sigma_gain = v_sigma * math.exp((layer_gap - 1.0) / decay_len)
HI = lax.Precision.HIGHEST
MID = lax.Precision.HIGH
OFFSETS = [(a, b) for a in (-1, 0, 1) for b in (-1, 0, 1)]


def _base_np():
    orbital = np.arange(128)
    sub = orbital % 4
    cell = orbital // 4
    inner_x = np.where((sub == 1) | (sub == 2), root_three / 2.0, 0.0)
    inner_y = np.select([sub == 1, sub == 2, sub == 3], [0.5, 1.5, 2.0], 0.0)
    return np.stack([(cell // 8) * root_three + inner_x - cell_w / 2.0, (cell % 8) * 3.0 + inner_y - cell_h / 2.0])


def _reach_sets():
    base = _base_np()
    c, s = math.cos(twist_angle), math.sin(twist_angle)
    rot = np.array([[c, -s], [s, c]])
    margin = 0.5
    plane_r = cut_radius + margin
    inter_r = math.sqrt(cut_radius**2 - layer_gap**2) + margin
    twists = [
        np.array([[cell_w * (i - (PATCH_X - 1) / 2.0)], [cell_h * (j - (PATCH_Y - 1) / 2.0)]])
        for i in range(PATCH_X)
        for j in range(PATCH_Y)
    ]
    sets = {}
    for a, b in OFFSETS:
        shift = np.array([[a * cell_w], [b * cell_h]])
        gap = base[:, :, None] - base[:, None, :] - shift[:, :, None]
        mask = np.sqrt((gap**2).sum(0)) < plane_r
        for e in twists:
            turned = rot @ base + (rot - np.eye(2)) @ e
            for own, near in ((base, turned), (turned, base)):
                gap = own[:, :, None] - near[:, None, :] - shift[:, :, None]
                mask |= np.sqrt((gap**2).sum(0)) < inter_r
        sets[(a, b)] = (np.nonzero(mask.any(1))[0], np.nonzero(mask.any(0))[0])
    return sets


REACH = _reach_sets()


def _one_hot(idx):
    table = np.zeros((128, len(idx)), np.float32)
    table[idx, np.arange(len(idx))] = 1.0
    return table


def pick(x, idx):
    if len(idx) == x.shape[-1]:
        return x
    if np.all(np.diff(idx) == 1):
        return x[..., idx[0] : idx[0] + len(idx)]
    return jnp.einsum("...q,qk->...k", x, _one_hot(idx), precision=HI)


def extended_2(value, sides, width):
    for axis, dim in sides:
        devices, length = (lax.axis_size(axis), value.shape[dim])
        up = [(i, (i + 1) % devices) for i in range(devices)]
        down = [(j, i) for i, j in up]
        last = lax.slice_in_dim(value, length - width, length, axis=dim)
        first = lax.slice_in_dim(value, 0, width, axis=dim)
        if devices == 2:
            both = lax.ppermute(jnp.concatenate([last, first], axis=dim), axis, up)
            before = lax.slice_in_dim(both, 0, width, axis=dim)
            after = lax.slice_in_dim(both, width, 2 * width, axis=dim)
        else:
            before = lax.ppermute(last, axis, up)
            after = lax.ppermute(first, axis, down)
        value = jnp.concatenate([before, value, after], axis=dim)
    return value


def partner_2(value, axis, distance):
    return lax.ppermute(value, axis, [(i, i ^ 1 << distance) for i in range(lax.axis_size(axis))])


def lattice(cos_vals, sin_vals):
    base = jnp.asarray(_base_np(), jnp.float32)
    rot_x = cos_vals[:, None] * base[0] - sin_vals[:, None] * base[1]
    rot_y = sin_vals[:, None] * base[0] + cos_vals[:, None] * base[1]
    return jnp.stack([rot_x, rot_y], axis=1)


def twist_offsets(cos_vals, sin_vals, row_ids, col_ids):
    along_x = cell_w * ((row_ids % PATCH_X).astype(jnp.float32) - (PATCH_X - 1) / 2.0)
    along_y = cell_h * ((col_ids % PATCH_Y).astype(jnp.float32) - (PATCH_Y - 1) / 2.0)
    cos_less = (cos_vals - 1.0)[:, None, None]
    sin_cast = sin_vals[:, None, None]
    shift_x = cos_less * along_x[None, :, None] - sin_cast * along_y[None, None, :]
    shift_y = sin_cast * along_x[None, :, None] + cos_less * along_y[None, None, :]
    return jnp.stack([shift_x, shift_y], axis=-1)[..., None]


def taper(dist_sq):
    scaled = dist_sq / (cut_radius * cut_radius)
    return jnp.maximum(1.0 - scaled * scaled, 0.0)


def plane_block(own_pos, near_pos, shift_x, shift_y, self_rows):
    delta_x = own_pos[..., 0, :, None] - near_pos[..., 0, None, :] - shift_x
    delta_y = own_pos[..., 1, :, None] - near_pos[..., 1, None, :] - shift_y
    dist_sq = delta_x * delta_x + delta_y * delta_y
    spread = jnp.sqrt(dist_sq)
    hopping = v_pi * jnp.exp(-(spread - 1.0) / decay_len) * taper(dist_sq)
    if self_rows:
        orbital = jnp.arange(128, dtype=jnp.int32)
        hopping = jnp.where(orbital[:, None] == orbital[None, :], 0.0, hopping)
    return hopping


def inter_block(own_pos, near_pos, shift_x, shift_y):
    delta_x = own_pos[..., 0, :, None] - near_pos[..., 0, None, :] - shift_x
    delta_y = own_pos[..., 1, :, None] - near_pos[..., 1, None, :] - shift_y
    dist_sq = delta_x * delta_x + delta_y * delta_y + layer_gap * layer_gap
    spread = jnp.sqrt(dist_sq)
    cosine_sq = layer_gap * layer_gap / dist_sq
    decay = jnp.exp(-(spread - 1.0) / decay_len)
    bonds = decay * (v_pi * (1.0 - cosine_sq) + sigma_gain * cosine_sq)
    return bonds * taper(dist_sq)


def _halo_options(n):
    if n == 1:
        return [(0, ("last", "all", "first"))]
    if n == 2:
        return [(0, ("all",)), (1, ("last", "first"))]
    return [(-1, ("last",)), (0, ("all",)), (1, ("first",))]


def _region(value, kind, axis):
    length = value.shape[axis]
    if kind == "last":
        return lax.slice_in_dim(value, length - 1, length, axis=axis)
    if kind == "first":
        return lax.slice_in_dim(value, 0, 1, axis=axis)
    return value


def exchange(value):
    stacked = jnp.concatenate([value, partner_2(value, "layer", 0)], axis=0)
    axes = ("gx", "gy")
    sizes = [lax.axis_size(a) for a in axes]
    tile = {1: stacked.shape[1], 2: stacked.shape[2]}
    pieces = {}
    for step_x, kinds_x in _halo_options(sizes[0]):
        along_x = jnp.concatenate([_region(stacked, r, 1) for r in kinds_x], axis=1)
        for step_y, kinds_y in _halo_options(sizes[1]):
            part = jnp.concatenate([_region(along_x, r, 2) for r in kinds_y], axis=2)
            if (step_x, step_y) != (0, 0):
                pairs = []
                for x in range(sizes[0]):
                    for y in range(sizes[1]):
                        dst = ((x - step_x) % sizes[0]) * sizes[1] + (y - step_y) % sizes[1]
                        pairs.append((x * sizes[1] + y, dst))
                part = lax.ppermute(part, axes, pairs)
            at_x = 0
            for rx in kinds_x:
                wide_x = tile[1] if rx == "all" else 1
                at_y = 0
                for ry in kinds_y:
                    wide_y = tile[2] if ry == "all" else 1
                    pieces[(rx, ry)] = part[:, at_x : at_x + wide_x, at_y : at_y + wide_y]
                    at_y += wide_y
                at_x += wide_x
    order = ("last", "all", "first")
    rows = [jnp.concatenate([pieces[(rx, ry)] for ry in order], axis=2) for rx in order]
    return jnp.concatenate(rows, axis=1)


def body(prev_vec, cur_vec, displace, potential):
    layer_id = lax.axis_index("layer")
    tile_x = displace.shape[1]
    tile_y = displace.shape[2]
    cos_twist = math.cos(twist_angle)
    sin_twist = math.sin(twist_angle)
    packed = exchange(jnp.concatenate([cur_vec, displace], axis=-2))
    vec_ext = packed[..., : cur_vec.shape[-2], :]
    ext_disp = packed[..., cur_vec.shape[-2] :, :]
    layer_up = layer_id == 1
    cos_vals = jnp.stack(
        [jnp.where(layer_up, cos_twist, 1.0), jnp.where(layer_up, 1.0, cos_twist)]
    ).astype(jnp.float32)
    sin_vals = jnp.stack(
        [jnp.where(layer_up, sin_twist, 0.0), jnp.where(layer_up, 0.0, sin_twist)]
    ).astype(jnp.float32)
    places = ext_disp + lattice(cos_vals, sin_vals)[:, None, None]
    row_count = tile_x * lax.axis_size("gx")
    col_count = tile_y * lax.axis_size("gy")
    row_ids = (
        lax.axis_index("gx") * tile_x + jnp.arange(tile_x + 2, dtype=jnp.int32) - 1 + row_count
    ) % row_count
    col_ids = (
        lax.axis_index("gy") * tile_y + jnp.arange(tile_y + 2, dtype=jnp.int32) - 1 + col_count
    ) % col_count
    turn = twist_offsets(cos_vals, sin_vals, row_ids, col_ids)
    twisted = places + turn

    def own_view(value, a, b):
        return value[:, 1 + a : 1 + a + tile_x, 1 + b : 1 + b + tile_y]

    own_pos = own_view(places[:1], 0, 0)[0]
    own_shift = own_view(turn[:1], 0, 0)[0]
    cos_own = cos_vals[0]
    sin_own = sin_vals[0]
    narrow = [o for o in OFFSETS if len(REACH[o][0]) < 64]
    narrow_rows = np.concatenate([REACH[o][0] for o in narrow])
    picked = jnp.einsum("...q,qk->...k", own_pos, _one_hot(narrow_rows), precision=HI)
    blocks = {}
    columns = {}
    at = 0
    for a, b in OFFSETS:
        rows, cols = REACH[(a, b)]
        if len(rows) < 64:
            own_rows = picked[..., at : at + len(rows)]
            at += len(rows)
            cols = np.arange(128)
        else:
            own_rows = pick(own_pos, rows)
        shift_x = cos_own * (a * cell_w) - sin_own * (b * cell_h)
        shift_y = sin_own * (a * cell_w) + cos_own * (b * cell_h)
        near_pos = pick(own_view(places[:1], a, b)[0], cols)
        near_twist = pick(own_view(twisted[1:], a, b)[0], cols)
        plane = plane_block(own_rows, near_pos, shift_x, shift_y, a == 0 and b == 0)
        inter = inter_block(own_rows + own_shift, near_twist, a * cell_w, b * cell_h)
        blocks[(a, b)] = jnp.stack([plane, inter])
        columns[(a, b)] = cols
    blocks = lax.optimization_barrier(blocks)

    scatter = np.zeros((len(narrow_rows), 128), np.float32)
    scatter[np.arange(len(narrow_rows)), narrow_rows] = 1.0

    def hop_terms(vectors, extended):
        full = potential[0][..., None, :] * vectors[0]
        parts = {}
        for a, b in OFFSETS:
            near = pick(own_view(extended, a, b), columns[(a, b)])
            parts[(a, b)] = jnp.einsum("kxycq,kxypq->xycp", near, blocks[(a, b)], precision=MID)
        full = full + parts[(0, 0)]
        full = full + jnp.concatenate([parts[(-1, 0)], parts[(1, 0)]], axis=-1)
        full = full + jnp.einsum(
            "xycp,pn->xycn", jnp.concatenate([parts[o] for o in narrow], axis=-1), scatter, precision=MID
        )
        return (full / hop_scale)[None]

    first_term = 2.0 * hop_terms(cur_vec, vec_ext) - prev_vec
    second_term = 2.0 * hop_terms(first_term, exchange(first_term)) - cur_vec
    return (first_term, second_term)


def solution(mesh):
    in_specs = (
        P("layer", "gx", "gy", None, None),
        P("layer", "gx", "gy", None, None),
        P("layer", "gx", "gy", None, None),
        P("layer", "gx", "gy", None),
    )
    out_specs = (P("layer", "gx", "gy", None, None), P("layer", "gx", "gy", None, None))
    return jax.shard_map(body, mesh=mesh, in_specs=in_specs, out_specs=out_specs, check_vma=False)
```

```python
import math

import jax
import jax.numpy as jnp
import numpy as np
from jax import lax
from jax.sharding import PartitionSpec as P

PATCH_X = 14
PATCH_Y = 4


v_pi = -2.7
v_sigma = 0.48
decay_len = 0.319
layer_gap = 3.35 / 1.42
cut_radius = 3.5
hop_scale = 12.0
twist_angle = 1.05 * math.pi / 180.0
root_three = math.sqrt(3.0)
cell_w = 4.0 * root_three
cell_h = 24.0
sigma_gain = v_sigma * math.exp((layer_gap - 1.0) / decay_len)
HI = lax.Precision.HIGHEST
MID = lax.Precision.HIGH
OFFSETS = [(a, b) for a in (-1, 0, 1) for b in (-1, 0, 1)]


def _base_np():
    orbital = np.arange(128)
    sub = orbital % 4
    cell = orbital // 4
    inner_x = np.where((sub == 1) | (sub == 2), root_three / 2.0, 0.0)
    inner_y = np.select([sub == 1, sub == 2, sub == 3], [0.5, 1.5, 2.0], 0.0)
    return np.stack([(cell // 8) * root_three + inner_x - cell_w / 2.0, (cell % 8) * 3.0 + inner_y - cell_h / 2.0])


def _reach_sets():
    base = _base_np()
    c, s = math.cos(twist_angle), math.sin(twist_angle)
    rot = np.array([[c, -s], [s, c]])
    margin = 0.5
    plane_r = cut_radius + margin
    inter_r = math.sqrt(cut_radius**2 - layer_gap**2) + margin
    twists = [
        np.array([[cell_w * (i - (PATCH_X - 1) / 2.0)], [cell_h * (j - (PATCH_Y - 1) / 2.0)]])
        for i in range(PATCH_X)
        for j in range(PATCH_Y)
    ]
    sets = {}
    for a, b in OFFSETS:
        shift = np.array([[a * cell_w], [b * cell_h]])
        gap = base[:, :, None] - base[:, None, :] - shift[:, :, None]
        mask = np.sqrt((gap**2).sum(0)) < plane_r
        for e in twists:
            turned = rot @ base + (rot - np.eye(2)) @ e
            for own, near in ((base, turned), (turned, base)):
                gap = own[:, :, None] - near[:, None, :] - shift[:, :, None]
                mask |= np.sqrt((gap**2).sum(0)) < inter_r
        sets[(a, b)] = (np.nonzero(mask.any(1))[0], np.nonzero(mask.any(0))[0])
    return sets


REACH = _reach_sets()
assert all(REACH[(-1, b)][1].min() >= 64 and REACH[(1, b)][1].max() < 64 for b in (-1, 0, 1))


def _one_hot(idx):
    table = np.zeros((128, len(idx)), np.float32)
    table[idx, np.arange(len(idx))] = 1.0
    return table


def pick(x, idx):
    if len(idx) == x.shape[-1]:
        return x
    if np.all(np.diff(idx) == 1):
        return x[..., idx[0] : idx[0] + len(idx)]
    return jnp.einsum("...q,qk->...k", x, _one_hot(idx), precision=HI)


def extended_2(value, sides, width):
    for axis, dim in sides:
        devices, length = (lax.axis_size(axis), value.shape[dim])
        up = [(i, (i + 1) % devices) for i in range(devices)]
        down = [(j, i) for i, j in up]
        last = lax.slice_in_dim(value, length - width, length, axis=dim)
        first = lax.slice_in_dim(value, 0, width, axis=dim)
        if devices == 2:
            both = lax.ppermute(jnp.concatenate([last, first], axis=dim), axis, up)
            before = lax.slice_in_dim(both, 0, width, axis=dim)
            after = lax.slice_in_dim(both, width, 2 * width, axis=dim)
        else:
            before = lax.ppermute(last, axis, up)
            after = lax.ppermute(first, axis, down)
        value = jnp.concatenate([before, value, after], axis=dim)
    return value


def partner_2(value, axis, distance):
    return lax.ppermute(value, axis, [(i, i ^ 1 << distance) for i in range(lax.axis_size(axis))])


def lattice(cos_vals, sin_vals):
    base = jnp.asarray(_base_np(), jnp.float32)
    rot_x = cos_vals[:, None] * base[0] - sin_vals[:, None] * base[1]
    rot_y = sin_vals[:, None] * base[0] + cos_vals[:, None] * base[1]
    return jnp.stack([rot_x, rot_y], axis=1)


def twist_offsets(cos_vals, sin_vals, row_ids, col_ids):
    along_x = cell_w * ((row_ids % PATCH_X).astype(jnp.float32) - (PATCH_X - 1) / 2.0)
    along_y = cell_h * ((col_ids % PATCH_Y).astype(jnp.float32) - (PATCH_Y - 1) / 2.0)
    cos_less = (cos_vals - 1.0)[:, None, None]
    sin_cast = sin_vals[:, None, None]
    shift_x = cos_less * along_x[None, :, None] - sin_cast * along_y[None, None, :]
    shift_y = sin_cast * along_x[None, :, None] + cos_less * along_y[None, None, :]
    return jnp.stack([shift_x, shift_y], axis=-1)[..., None]


def taper(dist_sq):
    scaled = dist_sq / (cut_radius * cut_radius)
    return jnp.maximum(1.0 - scaled * scaled, 0.0)


def plane_block(own_pos, near_pos, shift_x, shift_y, self_rows):
    delta_x = own_pos[..., 0, :, None] - near_pos[..., 0, None, :] - shift_x
    delta_y = own_pos[..., 1, :, None] - near_pos[..., 1, None, :] - shift_y
    dist_sq = delta_x * delta_x + delta_y * delta_y
    spread = jnp.sqrt(dist_sq)
    hopping = v_pi * jnp.exp(-(spread - 1.0) / decay_len) * taper(dist_sq)
    if self_rows:
        orbital = jnp.arange(128, dtype=jnp.int32)
        hopping = jnp.where(orbital[:, None] == orbital[None, :], 0.0, hopping)
    return hopping


def inter_block(own_pos, near_pos, shift_x, shift_y):
    delta_x = own_pos[..., 0, :, None] - near_pos[..., 0, None, :] - shift_x
    delta_y = own_pos[..., 1, :, None] - near_pos[..., 1, None, :] - shift_y
    dist_sq = delta_x * delta_x + delta_y * delta_y + layer_gap * layer_gap
    spread = jnp.sqrt(dist_sq)
    cosine_sq = layer_gap * layer_gap / dist_sq
    decay = jnp.exp(-(spread - 1.0) / decay_len)
    bonds = decay * (v_pi * (1.0 - cosine_sq) + sigma_gain * cosine_sq)
    return bonds * taper(dist_sq)


def _halo_options(n):
    if n == 1:
        return [(0, ("last", "all", "first"))]
    if n == 2:
        return [(0, ("all",)), (1, ("last", "first"))]
    return [(-1, ("last",)), (0, ("all",)), (1, ("first",))]


def _region(value, kind, axis):
    length = value.shape[axis]
    if kind == "last":
        return lax.slice_in_dim(value, length - 1, length, axis=axis)
    if kind == "first":
        return lax.slice_in_dim(value, 0, 1, axis=axis)
    return value


def exchange(value):
    stacked = jnp.concatenate([value, partner_2(value, "layer", 0)], axis=0)
    axes = ("gx", "gy")
    sizes = [lax.axis_size(a) for a in axes]
    tile = {1: stacked.shape[1], 2: stacked.shape[2]}
    pieces = {}
    for step_x, kinds_x in _halo_options(sizes[0]):
        along_x = jnp.concatenate([_region(stacked, r, 1) for r in kinds_x], axis=1)
        for step_y, kinds_y in _halo_options(sizes[1]):
            part = jnp.concatenate([_region(along_x, r, 2) for r in kinds_y], axis=2)
            if (step_x, step_y) != (0, 0):
                pairs = []
                for x in range(sizes[0]):
                    for y in range(sizes[1]):
                        dst = ((x - step_x) % sizes[0]) * sizes[1] + (y - step_y) % sizes[1]
                        pairs.append((x * sizes[1] + y, dst))
                if len(kinds_x) == 1 and step_x != 0:
                    lo = 64 if step_x < 0 else 0
                    packed = jnp.concatenate([part[:1, ..., lo : lo + 64], part[1:, ..., lo : lo + 64]], axis=-1)
                    packed = lax.ppermute(packed, axes, pairs)
                    fill = [(0, 0)] * (part.ndim - 1) + [(lo, 64 - lo)]
                    part = jnp.concatenate(
                        [jnp.pad(packed[..., :64], fill), jnp.pad(packed[..., 64:], fill)], axis=0
                    )
                else:
                    part = lax.ppermute(part, axes, pairs)
            at_x = 0
            for rx in kinds_x:
                wide_x = tile[1] if rx == "all" else 1
                at_y = 0
                for ry in kinds_y:
                    wide_y = tile[2] if ry == "all" else 1
                    pieces[(rx, ry)] = part[:, at_x : at_x + wide_x, at_y : at_y + wide_y]
                    at_y += wide_y
                at_x += wide_x
    order = ("last", "all", "first")
    rows = [jnp.concatenate([pieces[(rx, ry)] for ry in order], axis=2) for rx in order]
    return jnp.concatenate(rows, axis=1)


def body(prev_vec, cur_vec, displace, potential):
    layer_id = lax.axis_index("layer")
    tile_x = displace.shape[1]
    tile_y = displace.shape[2]
    cos_twist = math.cos(twist_angle)
    sin_twist = math.sin(twist_angle)
    packed = exchange(jnp.concatenate([cur_vec, displace], axis=-2))
    vec_ext = packed[..., : cur_vec.shape[-2], :]
    ext_disp = packed[..., cur_vec.shape[-2] :, :]
    layer_up = layer_id == 1
    cos_vals = jnp.stack(
        [jnp.where(layer_up, cos_twist, 1.0), jnp.where(layer_up, 1.0, cos_twist)]
    ).astype(jnp.float32)
    sin_vals = jnp.stack(
        [jnp.where(layer_up, sin_twist, 0.0), jnp.where(layer_up, 0.0, sin_twist)]
    ).astype(jnp.float32)
    places = ext_disp + lattice(cos_vals, sin_vals)[:, None, None]
    row_count = tile_x * lax.axis_size("gx")
    col_count = tile_y * lax.axis_size("gy")
    row_ids = (
        lax.axis_index("gx") * tile_x + jnp.arange(tile_x + 2, dtype=jnp.int32) - 1 + row_count
    ) % row_count
    col_ids = (
        lax.axis_index("gy") * tile_y + jnp.arange(tile_y + 2, dtype=jnp.int32) - 1 + col_count
    ) % col_count
    turn = twist_offsets(cos_vals, sin_vals, row_ids, col_ids)
    twisted = places + turn

    def own_view(value, a, b):
        return value[:, 1 + a : 1 + a + tile_x, 1 + b : 1 + b + tile_y]

    own_pos = own_view(places[:1], 0, 0)[0]
    own_shift = own_view(turn[:1], 0, 0)[0]
    cos_own = cos_vals[0]
    sin_own = sin_vals[0]
    narrow = [o for o in OFFSETS if len(REACH[o][0]) < 64]
    narrow_rows = np.concatenate([REACH[o][0] for o in narrow])
    picked = jnp.einsum("...q,qk->...k", own_pos, _one_hot(narrow_rows), precision=HI)
    blocks = {}
    columns = {}
    at = 0
    for a, b in OFFSETS:
        rows, cols = REACH[(a, b)]
        if len(rows) < 64:
            own_rows = picked[..., at : at + len(rows)]
            at += len(rows)
            cols = np.arange(128)
        else:
            own_rows = pick(own_pos, rows)
        shift_x = cos_own * (a * cell_w) - sin_own * (b * cell_h)
        shift_y = sin_own * (a * cell_w) + cos_own * (b * cell_h)
        near_pos = pick(own_view(places[:1], a, b)[0], cols)
        near_twist = pick(own_view(twisted[1:], a, b)[0], cols)
        plane = plane_block(own_rows, near_pos, shift_x, shift_y, a == 0 and b == 0)
        inter = inter_block(own_rows + own_shift, near_twist, a * cell_w, b * cell_h)
        blocks[(a, b)] = jnp.stack([plane, inter])
        columns[(a, b)] = cols
    blocks = lax.optimization_barrier(blocks)

    scatter = np.zeros((len(narrow_rows), 128), np.float32)
    scatter[np.arange(len(narrow_rows)), narrow_rows] = 1.0

    def hop_terms(vectors, extended):
        full = potential[0][..., None, :] * vectors[0]
        parts = {}
        for a, b in OFFSETS:
            near = pick(own_view(extended, a, b), columns[(a, b)])
            parts[(a, b)] = jnp.einsum("kxycq,kxypq->xycp", near, blocks[(a, b)], precision=MID)
        full = full + parts[(0, 0)]
        full = full + jnp.concatenate([parts[(-1, 0)], parts[(1, 0)]], axis=-1)
        full = full + jnp.einsum(
            "xycp,pn->xycn", jnp.concatenate([parts[o] for o in narrow], axis=-1), scatter, precision=MID
        )
        return (full / hop_scale)[None]

    first_term = 2.0 * hop_terms(cur_vec, vec_ext) - prev_vec
    second_term = 2.0 * hop_terms(first_term, exchange(first_term)) - cur_vec
    return (first_term, second_term)


def solution(mesh):
    in_specs = (
        P("layer", "gx", "gy", None, None),
        P("layer", "gx", "gy", None, None),
        P("layer", "gx", "gy", None, None),
        P("layer", "gx", "gy", None),
    )
    out_specs = (P("layer", "gx", "gy", None, None), P("layer", "gx", "gy", None, None))
    return jax.shard_map(body, mesh=mesh, in_specs=in_specs, out_specs=out_specs, check_vma=False)
```

```python
import math

import jax
import jax.numpy as jnp
import numpy as np
from jax import lax
from jax.sharding import PartitionSpec as P

PATCH_X = 14
PATCH_Y = 4


v_pi = -2.7
v_sigma = 0.48
decay_len = 0.319
layer_gap = 3.35 / 1.42
cut_radius = 3.5
hop_scale = 12.0
twist_angle = 1.05 * math.pi / 180.0
root_three = math.sqrt(3.0)
cell_w = 4.0 * root_three
cell_h = 24.0
sigma_gain = v_sigma * math.exp((layer_gap - 1.0) / decay_len)
HI = lax.Precision.HIGHEST
MID = lax.Precision.HIGH
OFFSETS = [(a, b) for a in (-1, 0, 1) for b in (-1, 0, 1)]


def _base_np():
    orbital = np.arange(128)
    sub = orbital % 4
    cell = orbital // 4
    inner_x = np.where((sub == 1) | (sub == 2), root_three / 2.0, 0.0)
    inner_y = np.select([sub == 1, sub == 2, sub == 3], [0.5, 1.5, 2.0], 0.0)
    return np.stack([(cell // 8) * root_three + inner_x - cell_w / 2.0, (cell % 8) * 3.0 + inner_y - cell_h / 2.0])


def _reach_sets():
    base = _base_np()
    c, s = math.cos(twist_angle), math.sin(twist_angle)
    rot = np.array([[c, -s], [s, c]])
    margin = 0.5
    plane_r = cut_radius + margin
    inter_r = math.sqrt(cut_radius**2 - layer_gap**2) + margin
    twists = [
        np.array([[cell_w * (i - (PATCH_X - 1) / 2.0)], [cell_h * (j - (PATCH_Y - 1) / 2.0)]])
        for i in range(PATCH_X)
        for j in range(PATCH_Y)
    ]
    sets = {}
    for a, b in OFFSETS:
        shift = np.array([[a * cell_w], [b * cell_h]])
        gap = base[:, :, None] - base[:, None, :] - shift[:, :, None]
        mask = np.sqrt((gap**2).sum(0)) < plane_r
        for e in twists:
            turned = rot @ base + (rot - np.eye(2)) @ e
            for own, near in ((base, turned), (turned, base)):
                gap = own[:, :, None] - near[:, None, :] - shift[:, :, None]
                mask |= np.sqrt((gap**2).sum(0)) < inter_r
        sets[(a, b)] = (np.nonzero(mask.any(1))[0], np.nonzero(mask.any(0))[0])
    return sets


REACH = _reach_sets()


def _one_hot(idx):
    table = np.zeros((128, len(idx)), np.float32)
    table[idx, np.arange(len(idx))] = 1.0
    return table


def pick(x, idx):
    if len(idx) == x.shape[-1]:
        return x
    if np.all(np.diff(idx) == 1):
        return x[..., idx[0] : idx[0] + len(idx)]
    return jnp.einsum("...q,qk->...k", x, _one_hot(idx), precision=HI)


def extended_2(value, sides, width):
    for axis, dim in sides:
        devices, length = (lax.axis_size(axis), value.shape[dim])
        up = [(i, (i + 1) % devices) for i in range(devices)]
        down = [(j, i) for i, j in up]
        last = lax.slice_in_dim(value, length - width, length, axis=dim)
        first = lax.slice_in_dim(value, 0, width, axis=dim)
        if devices == 2:
            both = lax.ppermute(jnp.concatenate([last, first], axis=dim), axis, up)
            before = lax.slice_in_dim(both, 0, width, axis=dim)
            after = lax.slice_in_dim(both, width, 2 * width, axis=dim)
        else:
            before = lax.ppermute(last, axis, up)
            after = lax.ppermute(first, axis, down)
        value = jnp.concatenate([before, value, after], axis=dim)
    return value


def partner_2(value, axis, distance):
    return lax.ppermute(value, axis, [(i, i ^ 1 << distance) for i in range(lax.axis_size(axis))])


def lattice(cos_vals, sin_vals):
    base = jnp.asarray(_base_np(), jnp.float32)
    rot_x = cos_vals[:, None] * base[0] - sin_vals[:, None] * base[1]
    rot_y = sin_vals[:, None] * base[0] + cos_vals[:, None] * base[1]
    return jnp.stack([rot_x, rot_y], axis=1)


def twist_offsets(cos_vals, sin_vals, row_ids, col_ids):
    along_x = cell_w * ((row_ids % PATCH_X).astype(jnp.float32) - (PATCH_X - 1) / 2.0)
    along_y = cell_h * ((col_ids % PATCH_Y).astype(jnp.float32) - (PATCH_Y - 1) / 2.0)
    cos_less = (cos_vals - 1.0)[:, None, None]
    sin_cast = sin_vals[:, None, None]
    shift_x = cos_less * along_x[None, :, None] - sin_cast * along_y[None, None, :]
    shift_y = sin_cast * along_x[None, :, None] + cos_less * along_y[None, None, :]
    return jnp.stack([shift_x, shift_y], axis=-1)[..., None]


def taper(dist_sq):
    scaled = dist_sq / (cut_radius * cut_radius)
    return jnp.maximum(1.0 - scaled * scaled, 0.0)


def plane_block(own_pos, near_pos, shift_x, shift_y, self_rows):
    delta_x = own_pos[..., 0, :, None] - near_pos[..., 0, None, :] - shift_x
    delta_y = own_pos[..., 1, :, None] - near_pos[..., 1, None, :] - shift_y
    dist_sq = delta_x * delta_x + delta_y * delta_y
    spread = jnp.sqrt(dist_sq)
    hopping = v_pi * jnp.exp(-(spread - 1.0) / decay_len) * taper(dist_sq)
    if self_rows:
        orbital = jnp.arange(128, dtype=jnp.int32)
        hopping = jnp.where(orbital[:, None] == orbital[None, :], 0.0, hopping)
    return hopping


def inter_block(own_pos, near_pos, shift_x, shift_y):
    delta_x = own_pos[..., 0, :, None] - near_pos[..., 0, None, :] - shift_x
    delta_y = own_pos[..., 1, :, None] - near_pos[..., 1, None, :] - shift_y
    dist_sq = delta_x * delta_x + delta_y * delta_y + layer_gap * layer_gap
    spread = jnp.sqrt(dist_sq)
    cosine_sq = layer_gap * layer_gap / dist_sq
    decay = jnp.exp(-(spread - 1.0) / decay_len)
    bonds = decay * (v_pi * (1.0 - cosine_sq) + sigma_gain * cosine_sq)
    return bonds * taper(dist_sq)


def _halo_options(n):
    if n == 1:
        return [(0, ("last", "all", "first"))]
    if n == 2:
        return [(0, ("all",)), (1, ("last", "first"))]
    return [(-1, ("last",)), (0, ("all",)), (1, ("first",))]


def _region(value, kind, axis):
    length = value.shape[axis]
    if kind == "last":
        return lax.slice_in_dim(value, length - 1, length, axis=axis)
    if kind == "first":
        return lax.slice_in_dim(value, 0, 1, axis=axis)
    return value


def exchange(value):
    stacked = jnp.concatenate([value, partner_2(value, "layer", 0)], axis=0)
    axes = ("gx", "gy")
    sizes = [lax.axis_size(a) for a in axes]
    tile = {1: stacked.shape[1], 2: stacked.shape[2]}
    pieces = {}
    for step_x, kinds_x in _halo_options(sizes[0]):
        along_x = jnp.concatenate([_region(stacked, r, 1) for r in kinds_x], axis=1)
        for step_y, kinds_y in _halo_options(sizes[1]):
            part = jnp.concatenate([_region(along_x, r, 2) for r in kinds_y], axis=2)
            if (step_x, step_y) != (0, 0):
                pairs = []
                for x in range(sizes[0]):
                    for y in range(sizes[1]):
                        dst = ((x - step_x) % sizes[0]) * sizes[1] + (y - step_y) % sizes[1]
                        pairs.append((x * sizes[1] + y, dst))
                part = lax.ppermute(part, axes, pairs)
            at_x = 0
            for rx in kinds_x:
                wide_x = tile[1] if rx == "all" else 1
                at_y = 0
                for ry in kinds_y:
                    wide_y = tile[2] if ry == "all" else 1
                    pieces[(rx, ry)] = part[:, at_x : at_x + wide_x, at_y : at_y + wide_y]
                    at_y += wide_y
                at_x += wide_x
    order = ("last", "all", "first")
    rows = [jnp.concatenate([pieces[(rx, ry)] for ry in order], axis=2) for rx in order]
    return jnp.concatenate(rows, axis=1)


def body(prev_vec, cur_vec, displace, potential):
    layer_id = lax.axis_index("layer")
    tile_x = displace.shape[1]
    tile_y = displace.shape[2]
    cos_twist = math.cos(twist_angle)
    sin_twist = math.sin(twist_angle)
    packed = exchange(jnp.concatenate([cur_vec, displace], axis=-2))
    vec_ext = packed[..., : cur_vec.shape[-2], :]
    ext_disp = packed[..., cur_vec.shape[-2] :, :]
    layer_up = layer_id == 1
    cos_vals = jnp.stack(
        [jnp.where(layer_up, cos_twist, 1.0), jnp.where(layer_up, 1.0, cos_twist)]
    ).astype(jnp.float32)
    sin_vals = jnp.stack(
        [jnp.where(layer_up, sin_twist, 0.0), jnp.where(layer_up, 0.0, sin_twist)]
    ).astype(jnp.float32)
    places = ext_disp + lattice(cos_vals, sin_vals)[:, None, None]
    row_count = tile_x * lax.axis_size("gx")
    col_count = tile_y * lax.axis_size("gy")
    row_ids = (
        lax.axis_index("gx") * tile_x + jnp.arange(tile_x + 2, dtype=jnp.int32) - 1 + row_count
    ) % row_count
    col_ids = (
        lax.axis_index("gy") * tile_y + jnp.arange(tile_y + 2, dtype=jnp.int32) - 1 + col_count
    ) % col_count
    turn = twist_offsets(cos_vals, sin_vals, row_ids, col_ids)
    twisted = places + turn

    def own_view(value, a, b):
        return value[:, 1 + a : 1 + a + tile_x, 1 + b : 1 + b + tile_y]

    own_pos = own_view(places[:1], 0, 0)[0]
    own_shift = own_view(turn[:1], 0, 0)[0]
    cos_own = cos_vals[0]
    sin_own = sin_vals[0]
    narrow = [o for o in OFFSETS if len(REACH[o][0]) < 64]
    narrow_rows = np.concatenate([REACH[o][0] for o in narrow])
    picked = jnp.einsum("...q,qk->...k", own_pos, _one_hot(narrow_rows), precision=HI)
    blocks = {}
    columns = {}
    at = 0
    for a, b in OFFSETS:
        rows, cols = REACH[(a, b)]
        if len(rows) < 64:
            own_rows = picked[..., at : at + len(rows)]
            at += len(rows)
            cols = np.arange(128)
        else:
            own_rows = pick(own_pos, rows)
        shift_x = cos_own * (a * cell_w) - sin_own * (b * cell_h)
        shift_y = sin_own * (a * cell_w) + cos_own * (b * cell_h)
        near_pos = pick(own_view(places[:1], a, b)[0], cols)
        near_twist = pick(own_view(twisted[1:], a, b)[0], cols)
        plane = plane_block(own_rows, near_pos, shift_x, shift_y, a == 0 and b == 0)
        inter = inter_block(own_rows + own_shift, near_twist, a * cell_w, b * cell_h)
        blocks[(a, b)] = jnp.stack([plane, inter])
        columns[(a, b)] = cols
    assert list(REACH[(-1, 0)][0]) == list(range(64)) and list(REACH[(-1, 0)][1]) == list(range(64, 128))
    assert list(REACH[(1, 0)][0]) == list(range(64, 128)) and list(REACH[(1, 0)][1]) == list(range(64))
    fill = [(0, 0)] * (blocks[(0, 0)].ndim - 1)
    blocks[(9, 9)] = jnp.concatenate(
        [jnp.pad(blocks.pop((-1, 0)), fill + [(64, 0)]), jnp.pad(blocks.pop((1, 0)), fill + [(0, 64)])], axis=-2
    )
    blocks = lax.optimization_barrier(blocks)
    upper_lanes = jnp.arange(128) >= 64

    scatter = np.zeros((len(narrow_rows), 128), np.float32)
    scatter[np.arange(len(narrow_rows)), narrow_rows] = 1.0

    def hop_terms(vectors, extended):
        full = potential[0][..., None, :] * vectors[0]
        parts = {}
        for a, b in [(0, 0)] + narrow:
            near = pick(own_view(extended, a, b), columns[(a, b)])
            parts[(a, b)] = jnp.einsum("kxycq,kxypq->xycp", near, blocks[(a, b)], precision=MID)
        full = full + parts[(0, 0)]
        near = jnp.where(upper_lanes, own_view(extended, -1, 0), own_view(extended, 1, 0))
        full = full + jnp.einsum("kxycq,kxypq->xycp", near, blocks[(9, 9)], precision=MID)
        full = full + jnp.einsum(
            "xycp,pn->xycn", jnp.concatenate([parts[o] for o in narrow], axis=-1), scatter, precision=MID
        )
        return (full / hop_scale)[None]

    first_term = 2.0 * hop_terms(cur_vec, vec_ext) - prev_vec
    second_term = 2.0 * hop_terms(first_term, exchange(first_term)) - cur_vec
    return (first_term, second_term)


def solution(mesh):
    in_specs = (
        P("layer", "gx", "gy", None, None),
        P("layer", "gx", "gy", None, None),
        P("layer", "gx", "gy", None, None),
        P("layer", "gx", "gy", None),
    )
    out_specs = (P("layer", "gx", "gy", None, None), P("layer", "gx", "gy", None, None))
    return jax.shard_map(body, mesh=mesh, in_specs=in_specs, out_specs=out_specs, check_vma=False)
```

```python
import math

import jax
import jax.numpy as jnp
import numpy as np
from jax import lax
from jax.sharding import PartitionSpec as P

PATCH_X = 14
PATCH_Y = 4


v_pi = -2.7
v_sigma = 0.48
decay_len = 0.319
layer_gap = 3.35 / 1.42
cut_radius = 3.5
hop_scale = 12.0
twist_angle = 1.05 * math.pi / 180.0
root_three = math.sqrt(3.0)
cell_w = 4.0 * root_three
cell_h = 24.0
sigma_gain = v_sigma * math.exp((layer_gap - 1.0) / decay_len)
HI = lax.Precision.HIGHEST
MID = lax.Precision.HIGH
OFFSETS = [(a, b) for a in (-1, 0, 1) for b in (-1, 0, 1)]


def _base_np():
    orbital = np.arange(128)
    sub = orbital % 4
    cell = orbital // 4
    inner_x = np.where((sub == 1) | (sub == 2), root_three / 2.0, 0.0)
    inner_y = np.select([sub == 1, sub == 2, sub == 3], [0.5, 1.5, 2.0], 0.0)
    return np.stack([(cell // 8) * root_three + inner_x - cell_w / 2.0, (cell % 8) * 3.0 + inner_y - cell_h / 2.0])


def _reach_sets():
    base = _base_np()
    c, s = math.cos(twist_angle), math.sin(twist_angle)
    rot = np.array([[c, -s], [s, c]])
    margin = 0.5
    plane_r = cut_radius + margin
    inter_r = math.sqrt(cut_radius**2 - layer_gap**2) + margin
    twists = [
        np.array([[cell_w * (i - (PATCH_X - 1) / 2.0)], [cell_h * (j - (PATCH_Y - 1) / 2.0)]])
        for i in range(PATCH_X)
        for j in range(PATCH_Y)
    ]
    sets = {}
    for a, b in OFFSETS:
        shift = np.array([[a * cell_w], [b * cell_h]])
        gap = base[:, :, None] - base[:, None, :] - shift[:, :, None]
        mask = np.sqrt((gap**2).sum(0)) < plane_r
        for e in twists:
            turned = rot @ base + (rot - np.eye(2)) @ e
            for own, near in ((base, turned), (turned, base)):
                gap = own[:, :, None] - near[:, None, :] - shift[:, :, None]
                mask |= np.sqrt((gap**2).sum(0)) < inter_r
        sets[(a, b)] = (np.nonzero(mask.any(1))[0], np.nonzero(mask.any(0))[0])
    return sets


REACH = _reach_sets()


def _one_hot(idx):
    table = np.zeros((128, len(idx)), np.float32)
    table[idx, np.arange(len(idx))] = 1.0
    return table


def pick(x, idx):
    if len(idx) == x.shape[-1]:
        return x
    if np.all(np.diff(idx) == 1):
        return x[..., idx[0] : idx[0] + len(idx)]
    return jnp.einsum("...q,qk->...k", x, _one_hot(idx), precision=HI)


def extended_2(value, sides, width):
    for axis, dim in sides:
        devices, length = (lax.axis_size(axis), value.shape[dim])
        up = [(i, (i + 1) % devices) for i in range(devices)]
        down = [(j, i) for i, j in up]
        last = lax.slice_in_dim(value, length - width, length, axis=dim)
        first = lax.slice_in_dim(value, 0, width, axis=dim)
        if devices == 2:
            both = lax.ppermute(jnp.concatenate([last, first], axis=dim), axis, up)
            before = lax.slice_in_dim(both, 0, width, axis=dim)
            after = lax.slice_in_dim(both, width, 2 * width, axis=dim)
        else:
            before = lax.ppermute(last, axis, up)
            after = lax.ppermute(first, axis, down)
        value = jnp.concatenate([before, value, after], axis=dim)
    return value


def partner_2(value, axis, distance):
    return lax.ppermute(value, axis, [(i, i ^ 1 << distance) for i in range(lax.axis_size(axis))])


def lattice(cos_vals, sin_vals):
    base = jnp.asarray(_base_np(), jnp.float32)
    rot_x = cos_vals[:, None] * base[0] - sin_vals[:, None] * base[1]
    rot_y = sin_vals[:, None] * base[0] + cos_vals[:, None] * base[1]
    return jnp.stack([rot_x, rot_y], axis=1)


def twist_offsets(cos_vals, sin_vals, row_ids, col_ids):
    along_x = cell_w * ((row_ids % PATCH_X).astype(jnp.float32) - (PATCH_X - 1) / 2.0)
    along_y = cell_h * ((col_ids % PATCH_Y).astype(jnp.float32) - (PATCH_Y - 1) / 2.0)
    cos_less = (cos_vals - 1.0)[:, None, None]
    sin_cast = sin_vals[:, None, None]
    shift_x = cos_less * along_x[None, :, None] - sin_cast * along_y[None, None, :]
    shift_y = sin_cast * along_x[None, :, None] + cos_less * along_y[None, None, :]
    return jnp.stack([shift_x, shift_y], axis=-1)[..., None]


def taper(dist_sq):
    scaled = dist_sq / (cut_radius * cut_radius)
    return jnp.maximum(1.0 - scaled * scaled, 0.0)


def plane_block(own_pos, near_pos, shift_x, shift_y, self_rows):
    delta_x = own_pos[..., 0, :, None] - near_pos[..., 0, None, :] - shift_x
    delta_y = own_pos[..., 1, :, None] - near_pos[..., 1, None, :] - shift_y
    dist_sq = delta_x * delta_x + delta_y * delta_y
    spread = jnp.sqrt(dist_sq)
    hopping = v_pi * jnp.exp(-(spread - 1.0) / decay_len) * taper(dist_sq)
    if self_rows:
        orbital = jnp.arange(128, dtype=jnp.int32)
        hopping = jnp.where(orbital[:, None] == orbital[None, :], 0.0, hopping)
    return hopping


def inter_block(own_pos, near_pos, shift_x, shift_y):
    delta_x = own_pos[..., 0, :, None] - near_pos[..., 0, None, :] - shift_x
    delta_y = own_pos[..., 1, :, None] - near_pos[..., 1, None, :] - shift_y
    dist_sq = delta_x * delta_x + delta_y * delta_y + layer_gap * layer_gap
    spread = jnp.sqrt(dist_sq)
    cosine_sq = layer_gap * layer_gap / dist_sq
    decay = jnp.exp(-(spread - 1.0) / decay_len)
    bonds = decay * (v_pi * (1.0 - cosine_sq) + sigma_gain * cosine_sq)
    return bonds * taper(dist_sq)


def exchange(value):
    stacked = jnp.concatenate([value, partner_2(value, "layer", 0)], axis=0)
    return extended_2(stacked, (("gx", 1), ("gy", 2)), 1)


def body(prev_vec, cur_vec, displace, potential):
    layer_id = lax.axis_index("layer")
    tile_x = displace.shape[1]
    tile_y = displace.shape[2]
    cos_twist = math.cos(twist_angle)
    sin_twist = math.sin(twist_angle)
    packed = exchange(jnp.concatenate([cur_vec, displace], axis=-2))
    vec_ext = packed[..., : cur_vec.shape[-2], :]
    ext_disp = packed[..., cur_vec.shape[-2] :, :]
    layer_up = layer_id == 1
    cos_vals = jnp.stack(
        [jnp.where(layer_up, cos_twist, 1.0), jnp.where(layer_up, 1.0, cos_twist)]
    ).astype(jnp.float32)
    sin_vals = jnp.stack(
        [jnp.where(layer_up, sin_twist, 0.0), jnp.where(layer_up, 0.0, sin_twist)]
    ).astype(jnp.float32)
    places = ext_disp + lattice(cos_vals, sin_vals)[:, None, None]
    row_count = tile_x * lax.axis_size("gx")
    col_count = tile_y * lax.axis_size("gy")
    row_ids = (
        lax.axis_index("gx") * tile_x + jnp.arange(tile_x + 2, dtype=jnp.int32) - 1 + row_count
    ) % row_count
    col_ids = (
        lax.axis_index("gy") * tile_y + jnp.arange(tile_y + 2, dtype=jnp.int32) - 1 + col_count
    ) % col_count
    turn = twist_offsets(cos_vals, sin_vals, row_ids, col_ids)
    twisted = places + turn

    def own_view(value, a, b):
        return value[:, 1 + a : 1 + a + tile_x, 1 + b : 1 + b + tile_y]

    own_pos = own_view(places[:1], 0, 0)[0]
    own_shift = own_view(turn[:1], 0, 0)[0]
    cos_own = cos_vals[0]
    sin_own = sin_vals[0]
    narrow = [o for o in OFFSETS if len(REACH[o][0]) < 64]
    narrow_rows = np.concatenate([REACH[o][0] for o in narrow])
    picked = jnp.einsum("...q,qk->...k", own_pos, _one_hot(narrow_rows), precision=HI)
    blocks = {}
    columns = {}
    at = 0
    for a, b in OFFSETS:
        rows, cols = REACH[(a, b)]
        if len(rows) < 64:
            own_rows = picked[..., at : at + len(rows)]
            at += len(rows)
            cols = np.arange(128)
        else:
            own_rows = pick(own_pos, rows)
        shift_x = cos_own * (a * cell_w) - sin_own * (b * cell_h)
        shift_y = sin_own * (a * cell_w) + cos_own * (b * cell_h)
        near_pos = pick(own_view(places[:1], a, b)[0], cols)
        near_twist = pick(own_view(twisted[1:], a, b)[0], cols)
        plane = plane_block(own_rows, near_pos, shift_x, shift_y, a == 0 and b == 0)
        inter = inter_block(own_rows + own_shift, near_twist, a * cell_w, b * cell_h)
        blocks[(a, b)] = jnp.stack([plane, inter])
        columns[(a, b)] = cols
    blocks = lax.optimization_barrier(blocks)

    scatter = np.zeros((len(narrow_rows), 128), np.float32)
    scatter[np.arange(len(narrow_rows)), narrow_rows] = 1.0

    def hop_terms(vectors, extended):
        full = potential[0][..., None, :] * vectors[0]
        parts = {}
        for a, b in OFFSETS:
            near = pick(own_view(extended, a, b), columns[(a, b)])
            parts[(a, b)] = jnp.einsum("kxycq,kxypq->xycp", near, blocks[(a, b)], precision=MID)
        full = full + parts[(0, 0)]
        full = full + jnp.concatenate([parts[(-1, 0)], parts[(1, 0)]], axis=-1)
        full = full + jnp.einsum(
            "xycp,pn->xycn", jnp.concatenate([parts[o] for o in narrow], axis=-1), scatter, precision=MID
        )
        return (full / hop_scale)[None]

    first_term = 2.0 * hop_terms(cur_vec, vec_ext) - prev_vec
    second_term = 2.0 * hop_terms(first_term, exchange(first_term)) - cur_vec
    return (first_term, second_term)


def solution(mesh):
    in_specs = (
        P("layer", "gx", "gy", None, None),
        P("layer", "gx", "gy", None, None),
        P("layer", "gx", "gy", None, None),
        P("layer", "gx", "gy", None),
    )
    out_specs = (P("layer", "gx", "gy", None, None), P("layer", "gx", "gy", None, None))
    return jax.shard_map(body, mesh=mesh, in_specs=in_specs, out_specs=out_specs, check_vma=False)
```

```python
import math

import jax
import jax.numpy as jnp
import numpy as np
from jax import lax
from jax.sharding import PartitionSpec as P

PATCH_X = 14
PATCH_Y = 4


v_pi = -2.7
v_sigma = 0.48
decay_len = 0.319
layer_gap = 3.35 / 1.42
cut_radius = 3.5
hop_scale = 12.0
twist_angle = 1.05 * math.pi / 180.0
root_three = math.sqrt(3.0)
cell_w = 4.0 * root_three
cell_h = 24.0
sigma_gain = v_sigma * math.exp((layer_gap - 1.0) / decay_len)
HI = lax.Precision.HIGHEST
MID = lax.Precision.HIGH
OFFSETS = [(a, b) for a in (-1, 0, 1) for b in (-1, 0, 1)]


def _base_np():
    orbital = np.arange(128)
    sub = orbital % 4
    cell = orbital // 4
    inner_x = np.where((sub == 1) | (sub == 2), root_three / 2.0, 0.0)
    inner_y = np.select([sub == 1, sub == 2, sub == 3], [0.5, 1.5, 2.0], 0.0)
    return np.stack([(cell // 8) * root_three + inner_x - cell_w / 2.0, (cell % 8) * 3.0 + inner_y - cell_h / 2.0])


def _reach_sets():
    base = _base_np()
    c, s = math.cos(twist_angle), math.sin(twist_angle)
    rot = np.array([[c, -s], [s, c]])
    margin = 0.5
    plane_r = cut_radius + margin
    inter_r = math.sqrt(cut_radius**2 - layer_gap**2) + margin
    twists = [
        np.array([[cell_w * (i - (PATCH_X - 1) / 2.0)], [cell_h * (j - (PATCH_Y - 1) / 2.0)]])
        for i in range(PATCH_X)
        for j in range(PATCH_Y)
    ]
    sets = {}
    for a, b in OFFSETS:
        shift = np.array([[a * cell_w], [b * cell_h]])
        gap = base[:, :, None] - base[:, None, :] - shift[:, :, None]
        mask = np.sqrt((gap**2).sum(0)) < plane_r
        for e in twists:
            turned = rot @ base + (rot - np.eye(2)) @ e
            for own, near in ((base, turned), (turned, base)):
                gap = own[:, :, None] - near[:, None, :] - shift[:, :, None]
                mask |= np.sqrt((gap**2).sum(0)) < inter_r
        sets[(a, b)] = (np.nonzero(mask.any(1))[0], np.nonzero(mask.any(0))[0])
    return sets


REACH = _reach_sets()


def _one_hot(idx):
    table = np.zeros((128, len(idx)), np.float32)
    table[idx, np.arange(len(idx))] = 1.0
    return table


def pick(x, idx):
    if len(idx) == x.shape[-1]:
        return x
    if np.all(np.diff(idx) == 1):
        return x[..., idx[0] : idx[0] + len(idx)]
    return jnp.einsum("...q,qk->...k", x, _one_hot(idx), precision=HI)


def extended_2(value, sides, width):
    for axis, dim in sides:
        devices, length = (lax.axis_size(axis), value.shape[dim])
        up = [(i, (i + 1) % devices) for i in range(devices)]
        down = [(j, i) for i, j in up]
        last = lax.slice_in_dim(value, length - width, length, axis=dim)
        first = lax.slice_in_dim(value, 0, width, axis=dim)
        if devices == 2:
            both = lax.ppermute(jnp.concatenate([last, first], axis=dim), axis, up)
            before = lax.slice_in_dim(both, 0, width, axis=dim)
            after = lax.slice_in_dim(both, width, 2 * width, axis=dim)
        else:
            before = lax.ppermute(last, axis, up)
            after = lax.ppermute(first, axis, down)
        value = jnp.concatenate([before, value, after], axis=dim)
    return value


def partner_2(value, axis, distance):
    return lax.ppermute(value, axis, [(i, i ^ 1 << distance) for i in range(lax.axis_size(axis))])


def lattice(cos_vals, sin_vals):
    base = jnp.asarray(_base_np(), jnp.float32)
    rot_x = cos_vals[:, None] * base[0] - sin_vals[:, None] * base[1]
    rot_y = sin_vals[:, None] * base[0] + cos_vals[:, None] * base[1]
    return jnp.stack([rot_x, rot_y], axis=1)


def twist_offsets(cos_vals, sin_vals, row_ids, col_ids):
    along_x = cell_w * ((row_ids % PATCH_X).astype(jnp.float32) - (PATCH_X - 1) / 2.0)
    along_y = cell_h * ((col_ids % PATCH_Y).astype(jnp.float32) - (PATCH_Y - 1) / 2.0)
    cos_less = (cos_vals - 1.0)[:, None, None]
    sin_cast = sin_vals[:, None, None]
    shift_x = cos_less * along_x[None, :, None] - sin_cast * along_y[None, None, :]
    shift_y = sin_cast * along_x[None, :, None] + cos_less * along_y[None, None, :]
    return jnp.stack([shift_x, shift_y], axis=-1)[..., None]


def taper(dist_sq):
    scaled = dist_sq / (cut_radius * cut_radius)
    return jnp.maximum(1.0 - scaled * scaled, 0.0)


def plane_block(own_pos, near_pos, shift_x, shift_y, self_rows):
    delta_x = own_pos[..., 0, :, None] - near_pos[..., 0, None, :] - shift_x
    delta_y = own_pos[..., 1, :, None] - near_pos[..., 1, None, :] - shift_y
    dist_sq = delta_x * delta_x + delta_y * delta_y
    spread = jnp.sqrt(dist_sq)
    hopping = v_pi * jnp.exp(-(spread - 1.0) / decay_len) * taper(dist_sq)
    if self_rows:
        orbital = jnp.arange(128, dtype=jnp.int32)
        hopping = jnp.where(orbital[:, None] == orbital[None, :], 0.0, hopping)
    return hopping


def inter_block(own_pos, near_pos, shift_x, shift_y):
    delta_x = own_pos[..., 0, :, None] - near_pos[..., 0, None, :] - shift_x
    delta_y = own_pos[..., 1, :, None] - near_pos[..., 1, None, :] - shift_y
    dist_sq = delta_x * delta_x + delta_y * delta_y + layer_gap * layer_gap
    spread = jnp.sqrt(dist_sq)
    cosine_sq = layer_gap * layer_gap / dist_sq
    decay = jnp.exp(-(spread - 1.0) / decay_len)
    bonds = decay * (v_pi * (1.0 - cosine_sq) + sigma_gain * cosine_sq)
    return bonds * taper(dist_sq)


def _halo_options(n):
    if n == 1:
        return [(0, ("last", "all", "first"))]
    if n == 2:
        return [(0, ("all",)), (1, ("last", "first"))]
    return [(-1, ("last",)), (0, ("all",)), (1, ("first",))]


def _region(value, kind, axis):
    length = value.shape[axis]
    if kind == "last":
        return lax.slice_in_dim(value, length - 1, length, axis=axis)
    if kind == "first":
        return lax.slice_in_dim(value, 0, 1, axis=axis)
    return value


def exchange(value):
    stacked = jnp.concatenate([value, partner_2(value, "layer", 0)], axis=0)
    axes = ("gx", "gy")
    sizes = [lax.axis_size(a) for a in axes]
    tile = {1: stacked.shape[1], 2: stacked.shape[2]}
    pieces = {}
    for step_x, kinds_x in _halo_options(sizes[0]):
        along_x = jnp.concatenate([_region(stacked, r, 1) for r in kinds_x], axis=1)
        for step_y, kinds_y in _halo_options(sizes[1]):
            part = jnp.concatenate([_region(along_x, r, 2) for r in kinds_y], axis=2)
            if (step_x, step_y) != (0, 0):
                pairs = []
                for x in range(sizes[0]):
                    for y in range(sizes[1]):
                        dst = ((x - step_x) % sizes[0]) * sizes[1] + (y - step_y) % sizes[1]
                        pairs.append((x * sizes[1] + y, dst))
                part = lax.ppermute(part, axes, pairs)
            at_x = 0
            for rx in kinds_x:
                wide_x = tile[1] if rx == "all" else 1
                at_y = 0
                for ry in kinds_y:
                    wide_y = tile[2] if ry == "all" else 1
                    pieces[(rx, ry)] = part[:, at_x : at_x + wide_x, at_y : at_y + wide_y]
                    at_y += wide_y
                at_x += wide_x
    order = ("last", "all", "first")
    rows = [jnp.concatenate([pieces[(rx, ry)] for ry in order], axis=2) for rx in order]
    return stacked, jnp.concatenate(rows, axis=1)


def body(prev_vec, cur_vec, displace, potential):
    layer_id = lax.axis_index("layer")
    tile_x = displace.shape[1]
    tile_y = displace.shape[2]
    cos_twist = math.cos(twist_angle)
    sin_twist = math.sin(twist_angle)
    width = cur_vec.shape[-2]
    packed = exchange(jnp.concatenate([cur_vec, displace], axis=-2))
    vec_ext = tuple(s[..., :width, :] for s in packed)
    own_disp, ext_disp = (s[..., width:, :] for s in packed)
    layer_up = layer_id == 1
    cos_vals = jnp.stack(
        [jnp.where(layer_up, cos_twist, 1.0), jnp.where(layer_up, 1.0, cos_twist)]
    ).astype(jnp.float32)
    sin_vals = jnp.stack(
        [jnp.where(layer_up, sin_twist, 0.0), jnp.where(layer_up, 0.0, sin_twist)]
    ).astype(jnp.float32)
    grid = lattice(cos_vals, sin_vals)[:, None, None]
    places = ext_disp + grid
    centre = own_disp + grid
    row_count = tile_x * lax.axis_size("gx")
    col_count = tile_y * lax.axis_size("gy")
    row_ids = (
        lax.axis_index("gx") * tile_x + jnp.arange(tile_x + 2, dtype=jnp.int32) - 1 + row_count
    ) % row_count
    col_ids = (
        lax.axis_index("gy") * tile_y + jnp.arange(tile_y + 2, dtype=jnp.int32) - 1 + col_count
    ) % col_count
    turn = twist_offsets(cos_vals, sin_vals, row_ids, col_ids)
    twisted = places + turn

    def own_view(value, a, b):
        return value[:, 1 + a : 1 + a + tile_x, 1 + b : 1 + b + tile_y]

    own_pos = centre[0]
    own_shift = own_view(turn[:1], 0, 0)[0]
    cos_own = cos_vals[0]
    sin_own = sin_vals[0]
    narrow = [o for o in OFFSETS if len(REACH[o][0]) < 64]
    narrow_rows = np.concatenate([REACH[o][0] for o in narrow])
    picked = jnp.einsum("...q,qk->...k", own_pos, _one_hot(narrow_rows), precision=HI)
    blocks = {}
    columns = {}
    at = 0
    for a, b in OFFSETS:
        rows, cols = REACH[(a, b)]
        if len(rows) < 64:
            own_rows = picked[..., at : at + len(rows)]
            at += len(rows)
            cols = np.arange(128)
        else:
            own_rows = pick(own_pos, rows)
        shift_x = cos_own * (a * cell_w) - sin_own * (b * cell_h)
        shift_y = sin_own * (a * cell_w) + cos_own * (b * cell_h)
        if (a, b) == (0, 0):
            near_pos = centre[0]
            near_twist = centre[1] + own_view(turn[1:], 0, 0)[0]
        else:
            near_pos = pick(own_view(places[:1], a, b)[0], cols)
            near_twist = pick(own_view(twisted[1:], a, b)[0], cols)
        plane = plane_block(own_rows, near_pos, shift_x, shift_y, a == 0 and b == 0)
        inter = inter_block(own_rows + own_shift, near_twist, a * cell_w, b * cell_h)
        blocks[(a, b)] = jnp.stack([plane, inter])
        columns[(a, b)] = cols
    blocks = lax.optimization_barrier(blocks)

    scatter = np.zeros((len(narrow_rows), 128), np.float32)
    scatter[np.arange(len(narrow_rows)), narrow_rows] = 1.0

    def hop_terms(vectors, extended):
        full = potential[0][..., None, :] * vectors[0]
        parts = {}
        for a, b in OFFSETS:
            near = extended[0] if (a, b) == (0, 0) else pick(own_view(extended[1], a, b), columns[(a, b)])
            parts[(a, b)] = jnp.einsum("kxycq,kxypq->xycp", near, blocks[(a, b)], precision=MID)
        full = full + parts[(0, 0)]
        full = full + jnp.concatenate([parts[(-1, 0)], parts[(1, 0)]], axis=-1)
        full = full + jnp.einsum(
            "xycp,pn->xycn", jnp.concatenate([parts[o] for o in narrow], axis=-1), scatter, precision=MID
        )
        return (full / hop_scale)[None]

    first_term = 2.0 * hop_terms(cur_vec, vec_ext) - prev_vec
    second_term = 2.0 * hop_terms(first_term, exchange(first_term)) - cur_vec
    return (first_term, second_term)


def solution(mesh):
    in_specs = (
        P("layer", "gx", "gy", None, None),
        P("layer", "gx", "gy", None, None),
        P("layer", "gx", "gy", None, None),
        P("layer", "gx", "gy", None),
    )
    out_specs = (P("layer", "gx", "gy", None, None), P("layer", "gx", "gy", None, None))
    return jax.shard_map(body, mesh=mesh, in_specs=in_specs, out_specs=out_specs, check_vma=False)
```

```python
import math

import jax
import jax.numpy as jnp
import numpy as np
from jax import lax
from jax.sharding import PartitionSpec as P

PATCH_X = 14
PATCH_Y = 4


v_pi = -2.7
v_sigma = 0.48
decay_len = 0.319
layer_gap = 3.35 / 1.42
cut_radius = 3.5
hop_scale = 12.0
twist_angle = 1.05 * math.pi / 180.0
root_three = math.sqrt(3.0)
cell_w = 4.0 * root_three
cell_h = 24.0
sigma_gain = v_sigma * math.exp((layer_gap - 1.0) / decay_len)
HI = lax.Precision.HIGHEST
MID = lax.Precision.HIGH
OFFSETS = [(a, b) for a in (-1, 0, 1) for b in (-1, 0, 1)]


def _base_np():
    orbital = np.arange(128)
    sub = orbital % 4
    cell = orbital // 4
    inner_x = np.where((sub == 1) | (sub == 2), root_three / 2.0, 0.0)
    inner_y = np.select([sub == 1, sub == 2, sub == 3], [0.5, 1.5, 2.0], 0.0)
    return np.stack([(cell // 8) * root_three + inner_x - cell_w / 2.0, (cell % 8) * 3.0 + inner_y - cell_h / 2.0])


def _reach_sets():
    base = _base_np()
    c, s = math.cos(twist_angle), math.sin(twist_angle)
    rot = np.array([[c, -s], [s, c]])
    margin = 0.5
    plane_r = cut_radius + margin
    inter_r = math.sqrt(cut_radius**2 - layer_gap**2) + margin
    twists = [
        np.array([[cell_w * (i - (PATCH_X - 1) / 2.0)], [cell_h * (j - (PATCH_Y - 1) / 2.0)]])
        for i in range(PATCH_X)
        for j in range(PATCH_Y)
    ]
    sets = {}
    for a, b in OFFSETS:
        shift = np.array([[a * cell_w], [b * cell_h]])
        gap = base[:, :, None] - base[:, None, :] - shift[:, :, None]
        mask = np.sqrt((gap**2).sum(0)) < plane_r
        for e in twists:
            turned = rot @ base + (rot - np.eye(2)) @ e
            for own, near in ((base, turned), (turned, base)):
                gap = own[:, :, None] - near[:, None, :] - shift[:, :, None]
                mask |= np.sqrt((gap**2).sum(0)) < inter_r
        sets[(a, b)] = (np.nonzero(mask.any(1))[0], np.nonzero(mask.any(0))[0])
    return sets


REACH = _reach_sets()


def _one_hot(idx):
    table = np.zeros((128, len(idx)), np.float32)
    table[idx, np.arange(len(idx))] = 1.0
    return table


def pick(x, idx):
    if len(idx) == x.shape[-1]:
        return x
    if np.all(np.diff(idx) == 1):
        return x[..., idx[0] : idx[0] + len(idx)]
    return jnp.einsum("...q,qk->...k", x, _one_hot(idx), precision=HI)


def extended_2(value, sides, width):
    for axis, dim in sides:
        devices, length = (lax.axis_size(axis), value.shape[dim])
        up = [(i, (i + 1) % devices) for i in range(devices)]
        down = [(j, i) for i, j in up]
        last = lax.slice_in_dim(value, length - width, length, axis=dim)
        first = lax.slice_in_dim(value, 0, width, axis=dim)
        if devices == 2:
            both = lax.ppermute(jnp.concatenate([last, first], axis=dim), axis, up)
            before = lax.slice_in_dim(both, 0, width, axis=dim)
            after = lax.slice_in_dim(both, width, 2 * width, axis=dim)
        else:
            before = lax.ppermute(last, axis, up)
            after = lax.ppermute(first, axis, down)
        value = jnp.concatenate([before, value, after], axis=dim)
    return value


def partner_2(value, axis, distance):
    return lax.ppermute(value, axis, [(i, i ^ 1 << distance) for i in range(lax.axis_size(axis))])


def lattice(cos_vals, sin_vals):
    base = jnp.asarray(_base_np(), jnp.float32)
    rot_x = cos_vals[:, None] * base[0] - sin_vals[:, None] * base[1]
    rot_y = sin_vals[:, None] * base[0] + cos_vals[:, None] * base[1]
    return jnp.stack([rot_x, rot_y], axis=1)


def twist_offsets(cos_vals, sin_vals, row_ids, col_ids):
    along_x = cell_w * ((row_ids % PATCH_X).astype(jnp.float32) - (PATCH_X - 1) / 2.0)
    along_y = cell_h * ((col_ids % PATCH_Y).astype(jnp.float32) - (PATCH_Y - 1) / 2.0)
    cos_less = (cos_vals - 1.0)[:, None, None]
    sin_cast = sin_vals[:, None, None]
    shift_x = cos_less * along_x[None, :, None] - sin_cast * along_y[None, None, :]
    shift_y = sin_cast * along_x[None, :, None] + cos_less * along_y[None, None, :]
    return jnp.stack([shift_x, shift_y], axis=-1)[..., None]


def taper(dist_sq):
    scaled = dist_sq / (cut_radius * cut_radius)
    return jnp.maximum(1.0 - scaled * scaled, 0.0)


def plane_block(own_pos, near_pos, shift_x, shift_y, self_rows):
    delta_x = own_pos[..., 0, :, None] - near_pos[..., 0, None, :] - shift_x
    delta_y = own_pos[..., 1, :, None] - near_pos[..., 1, None, :] - shift_y
    dist_sq = delta_x * delta_x + delta_y * delta_y
    spread = jnp.sqrt(dist_sq)
    hopping = v_pi * jnp.exp(-(spread - 1.0) / decay_len) * taper(dist_sq)
    if self_rows:
        orbital = jnp.arange(128, dtype=jnp.int32)
        hopping = jnp.where(orbital[:, None] == orbital[None, :], 0.0, hopping)
    return hopping


def inter_block(own_pos, near_pos, shift_x, shift_y):
    delta_x = own_pos[..., 0, :, None] - near_pos[..., 0, None, :] - shift_x
    delta_y = own_pos[..., 1, :, None] - near_pos[..., 1, None, :] - shift_y
    dist_sq = delta_x * delta_x + delta_y * delta_y + layer_gap * layer_gap
    spread = jnp.sqrt(dist_sq)
    cosine_sq = layer_gap * layer_gap / dist_sq
    decay = jnp.exp(-(spread - 1.0) / decay_len)
    bonds = decay * (v_pi * (1.0 - cosine_sq) + sigma_gain * cosine_sq)
    return bonds * taper(dist_sq)


def _halo_options(n):
    if n == 1:
        return [(0, ("last", "all", "first"))]
    if n == 2:
        return [(0, ("all",)), (1, ("last", "first"))]
    return [(-1, ("last",)), (0, ("all",)), (1, ("first",))]


def _region(value, kind, axis):
    length = value.shape[axis]
    if kind == "last":
        return lax.slice_in_dim(value, length - 1, length, axis=axis)
    if kind == "first":
        return lax.slice_in_dim(value, 0, 1, axis=axis)
    return value


def exchange(value):
    axes = ("layer", "gx", "gy")
    sizes = [lax.axis_size(a) for a in axes]
    tile = {1: value.shape[1], 2: value.shape[2]}
    pieces = {}
    for layer_step in (0, 1):
        for step_x, kinds_x in _halo_options(sizes[1]):
            along_x = jnp.concatenate([_region(value, r, 1) for r in kinds_x], axis=1)
            for step_y, kinds_y in _halo_options(sizes[2]):
                part = jnp.concatenate([_region(along_x, r, 2) for r in kinds_y], axis=2)
                if (layer_step, step_x, step_y) != (0, 0, 0):
                    pairs = []
                    for l in range(sizes[0]):
                        for x in range(sizes[1]):
                            for y in range(sizes[2]):
                                src = (l * sizes[1] + x) * sizes[2] + y
                                dst_l = (l - layer_step) % sizes[0]
                                dst_x = (x - step_x) % sizes[1]
                                dst_y = (y - step_y) % sizes[2]
                                pairs.append((src, (dst_l * sizes[1] + dst_x) * sizes[2] + dst_y))
                    part = lax.ppermute(part, axes, pairs)
                at_x = 0
                for rx in kinds_x:
                    wide_x = tile[1] if rx == "all" else 1
                    at_y = 0
                    for ry in kinds_y:
                        wide_y = tile[2] if ry == "all" else 1
                        pieces[(layer_step, rx, ry)] = part[:, at_x : at_x + wide_x, at_y : at_y + wide_y]
                        at_y += wide_y
                    at_x += wide_x
    order = ("last", "all", "first")
    layers = []
    for layer_step in (0, 1):
        rows = [
            jnp.concatenate([pieces[(layer_step, rx, ry)] for ry in order], axis=2) for rx in order
        ]
        layers.append(jnp.concatenate(rows, axis=1))
    stacked = jnp.concatenate([pieces[(0, "all", "all")], pieces[(1, "all", "all")]], axis=0)
    return stacked, jnp.concatenate(layers, axis=0)


def body(prev_vec, cur_vec, displace, potential):
    layer_id = lax.axis_index("layer")
    tile_x = displace.shape[1]
    tile_y = displace.shape[2]
    cos_twist = math.cos(twist_angle)
    sin_twist = math.sin(twist_angle)
    width = cur_vec.shape[-2]
    packed = exchange(jnp.concatenate([cur_vec, displace], axis=-2))
    vec_ext = tuple(s[..., :width, :] for s in packed)
    own_disp, ext_disp = (s[..., width:, :] for s in packed)
    layer_up = layer_id == 1
    cos_vals = jnp.stack(
        [jnp.where(layer_up, cos_twist, 1.0), jnp.where(layer_up, 1.0, cos_twist)]
    ).astype(jnp.float32)
    sin_vals = jnp.stack(
        [jnp.where(layer_up, sin_twist, 0.0), jnp.where(layer_up, 0.0, sin_twist)]
    ).astype(jnp.float32)
    grid = lattice(cos_vals, sin_vals)[:, None, None]
    places = ext_disp + grid
    centre = own_disp + grid
    row_count = tile_x * lax.axis_size("gx")
    col_count = tile_y * lax.axis_size("gy")
    row_ids = (
        lax.axis_index("gx") * tile_x + jnp.arange(tile_x + 2, dtype=jnp.int32) - 1 + row_count
    ) % row_count
    col_ids = (
        lax.axis_index("gy") * tile_y + jnp.arange(tile_y + 2, dtype=jnp.int32) - 1 + col_count
    ) % col_count
    turn = twist_offsets(cos_vals, sin_vals, row_ids, col_ids)
    twisted = places + turn

    def own_view(value, a, b):
        return value[:, 1 + a : 1 + a + tile_x, 1 + b : 1 + b + tile_y]

    own_pos = centre[0]
    own_shift = own_view(turn[:1], 0, 0)[0]
    cos_own = cos_vals[0]
    sin_own = sin_vals[0]
    narrow = [o for o in OFFSETS if len(REACH[o][0]) < 64]
    narrow_rows = np.concatenate([REACH[o][0] for o in narrow])
    picked = jnp.einsum("...q,qk->...k", own_pos, _one_hot(narrow_rows), precision=HI)
    blocks = {}
    columns = {}
    at = 0
    for a, b in OFFSETS:
        rows, cols = REACH[(a, b)]
        if len(rows) < 64:
            own_rows = picked[..., at : at + len(rows)]
            at += len(rows)
            cols = np.arange(128)
        else:
            own_rows = pick(own_pos, rows)
        shift_x = cos_own * (a * cell_w) - sin_own * (b * cell_h)
        shift_y = sin_own * (a * cell_w) + cos_own * (b * cell_h)
        if (a, b) == (0, 0):
            near_pos = centre[0]
            near_twist = centre[1] + own_view(turn[1:], 0, 0)[0]
        else:
            near_pos = pick(own_view(places[:1], a, b)[0], cols)
            near_twist = pick(own_view(twisted[1:], a, b)[0], cols)
        plane = plane_block(own_rows, near_pos, shift_x, shift_y, a == 0 and b == 0)
        inter = inter_block(own_rows + own_shift, near_twist, a * cell_w, b * cell_h)
        blocks[(a, b)] = jnp.stack([plane, inter])
        columns[(a, b)] = cols
    blocks = lax.optimization_barrier(blocks)

    scatter = np.zeros((len(narrow_rows), 128), np.float32)
    scatter[np.arange(len(narrow_rows)), narrow_rows] = 1.0

    def hop_terms(vectors, extended):
        full = potential[0][..., None, :] * vectors[0]
        parts = {}
        for a, b in OFFSETS:
            near = extended[0] if (a, b) == (0, 0) else pick(own_view(extended[1], a, b), columns[(a, b)])
            parts[(a, b)] = jnp.einsum("kxycq,kxypq->xycp", near, blocks[(a, b)], precision=MID)
        full = full + parts[(0, 0)]
        full = full + jnp.concatenate([parts[(-1, 0)], parts[(1, 0)]], axis=-1)
        full = full + jnp.einsum(
            "xycp,pn->xycn", jnp.concatenate([parts[o] for o in narrow], axis=-1), scatter, precision=MID
        )
        return (full / hop_scale)[None]

    first_term = 2.0 * hop_terms(cur_vec, vec_ext) - prev_vec
    second_term = 2.0 * hop_terms(first_term, exchange(first_term)) - cur_vec
    return (first_term, second_term)


def solution(mesh):
    in_specs = (
        P("layer", "gx", "gy", None, None),
        P("layer", "gx", "gy", None, None),
        P("layer", "gx", "gy", None, None),
        P("layer", "gx", "gy", None),
    )
    out_specs = (P("layer", "gx", "gy", None, None), P("layer", "gx", "gy", None, None))
    return jax.shard_map(body, mesh=mesh, in_specs=in_specs, out_specs=out_specs, check_vma=False)
```

```python
import math

import jax
import jax.numpy as jnp
import numpy as np
from jax import lax
from jax.sharding import PartitionSpec as P

PATCH_X = 14
PATCH_Y = 4


v_pi = -2.7
v_sigma = 0.48
decay_len = 0.319
layer_gap = 3.35 / 1.42
cut_radius = 3.5
hop_scale = 12.0
twist_angle = 1.05 * math.pi / 180.0
root_three = math.sqrt(3.0)
cell_w = 4.0 * root_three
cell_h = 24.0
sigma_gain = v_sigma * math.exp((layer_gap - 1.0) / decay_len)
HI = lax.Precision.HIGHEST
MID = lax.Precision.HIGH
OFFSETS = [(a, b) for a in (-1, 0, 1) for b in (-1, 0, 1)]


def _base_np():
    orbital = np.arange(128)
    sub = orbital % 4
    cell = orbital // 4
    inner_x = np.where((sub == 1) | (sub == 2), root_three / 2.0, 0.0)
    inner_y = np.select([sub == 1, sub == 2, sub == 3], [0.5, 1.5, 2.0], 0.0)
    return np.stack([(cell // 8) * root_three + inner_x - cell_w / 2.0, (cell % 8) * 3.0 + inner_y - cell_h / 2.0])


def _reach_sets():
    base = _base_np()
    c, s = math.cos(twist_angle), math.sin(twist_angle)
    rot = np.array([[c, -s], [s, c]])
    margin = 0.5
    plane_r = cut_radius + margin
    inter_r = math.sqrt(cut_radius**2 - layer_gap**2) + margin
    twists = [
        np.array([[cell_w * (i - (PATCH_X - 1) / 2.0)], [cell_h * (j - (PATCH_Y - 1) / 2.0)]])
        for i in range(PATCH_X)
        for j in range(PATCH_Y)
    ]
    sets = {}
    for a, b in OFFSETS:
        shift = np.array([[a * cell_w], [b * cell_h]])
        gap = base[:, :, None] - base[:, None, :] - shift[:, :, None]
        mask = np.sqrt((gap**2).sum(0)) < plane_r
        for e in twists:
            turned = rot @ base + (rot - np.eye(2)) @ e
            for own, near in ((base, turned), (turned, base)):
                gap = own[:, :, None] - near[:, None, :] - shift[:, :, None]
                mask |= np.sqrt((gap**2).sum(0)) < inter_r
        sets[(a, b)] = (np.nonzero(mask.any(1))[0], np.nonzero(mask.any(0))[0])
    return sets


REACH = _reach_sets()


def _one_hot(idx):
    table = np.zeros((128, len(idx)), np.float32)
    table[idx, np.arange(len(idx))] = 1.0
    return table


def pick(x, idx):
    if len(idx) == x.shape[-1]:
        return x
    if np.all(np.diff(idx) == 1):
        return x[..., idx[0] : idx[0] + len(idx)]
    return jnp.einsum("...q,qk->...k", x, _one_hot(idx), precision=HI)


def extended_2(value, sides, width):
    for axis, dim in sides:
        devices, length = (lax.axis_size(axis), value.shape[dim])
        up = [(i, (i + 1) % devices) for i in range(devices)]
        down = [(j, i) for i, j in up]
        last = lax.slice_in_dim(value, length - width, length, axis=dim)
        first = lax.slice_in_dim(value, 0, width, axis=dim)
        if devices == 2:
            both = lax.ppermute(jnp.concatenate([last, first], axis=dim), axis, up)
            before = lax.slice_in_dim(both, 0, width, axis=dim)
            after = lax.slice_in_dim(both, width, 2 * width, axis=dim)
        else:
            before = lax.ppermute(last, axis, up)
            after = lax.ppermute(first, axis, down)
        value = jnp.concatenate([before, value, after], axis=dim)
    return value


def partner_2(value, axis, distance):
    return lax.ppermute(value, axis, [(i, i ^ 1 << distance) for i in range(lax.axis_size(axis))])


def lattice(cos_vals, sin_vals):
    base = jnp.asarray(_base_np(), jnp.float32)
    rot_x = cos_vals[:, None] * base[0] - sin_vals[:, None] * base[1]
    rot_y = sin_vals[:, None] * base[0] + cos_vals[:, None] * base[1]
    return jnp.stack([rot_x, rot_y], axis=1)


def twist_offsets(cos_vals, sin_vals, row_ids, col_ids):
    along_x = cell_w * ((row_ids % PATCH_X).astype(jnp.float32) - (PATCH_X - 1) / 2.0)
    along_y = cell_h * ((col_ids % PATCH_Y).astype(jnp.float32) - (PATCH_Y - 1) / 2.0)
    cos_less = (cos_vals - 1.0)[:, None, None]
    sin_cast = sin_vals[:, None, None]
    shift_x = cos_less * along_x[None, :, None] - sin_cast * along_y[None, None, :]
    shift_y = sin_cast * along_x[None, :, None] + cos_less * along_y[None, None, :]
    return jnp.stack([shift_x, shift_y], axis=-1)[..., None]


def taper(dist_sq):
    scaled = dist_sq / (cut_radius * cut_radius)
    return jnp.maximum(1.0 - scaled * scaled, 0.0)


def plane_block(own_pos, near_pos, shift_x, shift_y, self_rows):
    delta_x = own_pos[..., 0, :, None] - near_pos[..., 0, None, :] - shift_x
    delta_y = own_pos[..., 1, :, None] - near_pos[..., 1, None, :] - shift_y
    dist_sq = delta_x * delta_x + delta_y * delta_y
    spread = jnp.sqrt(dist_sq)
    hopping = v_pi * jnp.exp(-(spread - 1.0) / decay_len) * taper(dist_sq)
    if self_rows:
        orbital = jnp.arange(128, dtype=jnp.int32)
        hopping = jnp.where(orbital[:, None] == orbital[None, :], 0.0, hopping)
    return hopping


def inter_block(own_pos, near_pos, shift_x, shift_y):
    delta_x = own_pos[..., 0, :, None] - near_pos[..., 0, None, :] - shift_x
    delta_y = own_pos[..., 1, :, None] - near_pos[..., 1, None, :] - shift_y
    dist_sq = delta_x * delta_x + delta_y * delta_y + layer_gap * layer_gap
    spread = jnp.sqrt(dist_sq)
    cosine_sq = layer_gap * layer_gap / dist_sq
    decay = jnp.exp(-(spread - 1.0) / decay_len)
    bonds = decay * (v_pi * (1.0 - cosine_sq) + sigma_gain * cosine_sq)
    return bonds * taper(dist_sq)


def _halo_options(n):
    if n == 1:
        return [(0, ("last", "all", "first"))]
    if n == 2:
        return [(0, ("all",)), (1, ("last", "first"))]
    return [(-1, ("last",)), (0, ("all",)), (1, ("first",))]


def _region(value, kind, axis):
    length = value.shape[axis]
    if kind == "last":
        return lax.slice_in_dim(value, length - 1, length, axis=axis)
    if kind == "first":
        return lax.slice_in_dim(value, 0, 1, axis=axis)
    return value


def exchange(value):
    stacked = jnp.concatenate([value, partner_2(value, "layer", 0)], axis=0)
    axes = ("gx", "gy")
    sizes = [lax.axis_size(a) for a in axes]
    tile = {1: stacked.shape[1], 2: stacked.shape[2]}
    pieces = {}
    for step_x, kinds_x in _halo_options(sizes[0]):
        along_x = jnp.concatenate([_region(stacked, r, 1) for r in kinds_x], axis=1)
        for step_y, kinds_y in _halo_options(sizes[1]):
            part = jnp.concatenate([_region(along_x, r, 2) for r in kinds_y], axis=2)
            if (step_x, step_y) != (0, 0):
                pairs = []
                for x in range(sizes[0]):
                    for y in range(sizes[1]):
                        dst = ((x - step_x) % sizes[0]) * sizes[1] + (y - step_y) % sizes[1]
                        pairs.append((x * sizes[1] + y, dst))
                part = lax.ppermute(part, axes, pairs)
            at_x = 0
            for rx in kinds_x:
                wide_x = tile[1] if rx == "all" else 1
                at_y = 0
                for ry in kinds_y:
                    wide_y = tile[2] if ry == "all" else 1
                    pieces[(rx, ry)] = part[:, at_x : at_x + wide_x, at_y : at_y + wide_y]
                    at_y += wide_y
                at_x += wide_x
    order = ("last", "all", "first")
    rows = [jnp.concatenate([pieces[(rx, ry)] for ry in order], axis=2) for rx in order]
    return stacked, jnp.concatenate(rows, axis=1)


def body(prev_vec, cur_vec, displace, potential):
    layer_id = lax.axis_index("layer")
    tile_x = displace.shape[1]
    tile_y = displace.shape[2]
    cos_twist = math.cos(twist_angle)
    sin_twist = math.sin(twist_angle)
    width = cur_vec.shape[-2]
    packed = exchange(jnp.concatenate([cur_vec, displace], axis=-2))
    vec_ext = tuple(s[..., :width, :] for s in packed)
    own_disp, ext_disp = (s[..., width:, :] for s in packed)
    layer_up = layer_id == 1
    cos_vals = jnp.stack(
        [jnp.where(layer_up, cos_twist, 1.0), jnp.where(layer_up, 1.0, cos_twist)]
    ).astype(jnp.float32)
    sin_vals = jnp.stack(
        [jnp.where(layer_up, sin_twist, 0.0), jnp.where(layer_up, 0.0, sin_twist)]
    ).astype(jnp.float32)
    grid = lattice(cos_vals, sin_vals)[:, None, None]
    places = ext_disp + grid
    centre = own_disp + grid
    row_count = tile_x * lax.axis_size("gx")
    col_count = tile_y * lax.axis_size("gy")
    row_ids = (
        lax.axis_index("gx") * tile_x + jnp.arange(tile_x + 2, dtype=jnp.int32) - 1 + row_count
    ) % row_count
    col_ids = (
        lax.axis_index("gy") * tile_y + jnp.arange(tile_y + 2, dtype=jnp.int32) - 1 + col_count
    ) % col_count
    turn = twist_offsets(cos_vals, sin_vals, row_ids, col_ids)
    twisted = places + turn

    def own_view(value, a, b):
        return value[:, 1 + a : 1 + a + tile_x, 1 + b : 1 + b + tile_y]

    own_pos = centre[0]
    own_shift = own_view(turn[:1], 0, 0)[0]
    cos_own = cos_vals[0]
    sin_own = sin_vals[0]
    narrow = [o for o in OFFSETS if len(REACH[o][0]) < 64]
    narrow_rows = np.concatenate([REACH[o][0] for o in narrow])
    picked = jnp.einsum("...q,qk->...k", own_pos, _one_hot(narrow_rows), precision=HI)
    blocks = {}
    columns = {}
    at = 0
    for a, b in OFFSETS:
        rows, cols = REACH[(a, b)]
        if len(rows) < 64:
            own_rows = picked[..., at : at + len(rows)]
            at += len(rows)
            cols = np.arange(128)
        else:
            own_rows = pick(own_pos, rows)
        shift_x = cos_own * (a * cell_w) - sin_own * (b * cell_h)
        shift_y = sin_own * (a * cell_w) + cos_own * (b * cell_h)
        if (a, b) == (0, 0):
            near_pos = centre[0]
            near_twist = centre[1] + own_view(turn[1:], 0, 0)[0]
        else:
            near_pos = pick(own_view(places[:1], a, b)[0], cols)
            near_twist = pick(own_view(twisted[1:], a, b)[0], cols)
        plane = plane_block(own_rows, near_pos, shift_x, shift_y, a == 0 and b == 0)
        inter = inter_block(own_rows + own_shift, near_twist, a * cell_w, b * cell_h)
        blocks[(a, b)] = jnp.stack([plane, inter])
        columns[(a, b)] = cols
    blocks = lax.optimization_barrier(blocks)

    scatter = np.zeros((len(narrow_rows), 128), np.float32)
    scatter[np.arange(len(narrow_rows)), narrow_rows] = 1.0

    def hop_terms(vectors, extended):
        full = potential[0][..., None, :] * vectors[0]
        parts = {}
        centre = blocks[(0, 0)]
        full = full + jnp.einsum("xycq,xypq->xycp", vectors[0], centre[0], precision=MID)
        full = full + jnp.einsum("xycq,xypq->xycp", extended[0][1], centre[1], precision=MID)
        for a, b in OFFSETS:
            if (a, b) != (0, 0):
                near = pick(own_view(extended[1], a, b), columns[(a, b)])
                parts[(a, b)] = jnp.einsum("kxycq,kxypq->xycp", near, blocks[(a, b)], precision=MID)
        full = full + jnp.concatenate([parts[(-1, 0)], parts[(1, 0)]], axis=-1)
        full = full + jnp.einsum(
            "xycp,pn->xycn", jnp.concatenate([parts[o] for o in narrow], axis=-1), scatter, precision=MID
        )
        return (full / hop_scale)[None]

    first_term = 2.0 * hop_terms(cur_vec, vec_ext) - prev_vec
    second_term = 2.0 * hop_terms(first_term, exchange(first_term)) - cur_vec
    return (first_term, second_term)


def solution(mesh):
    in_specs = (
        P("layer", "gx", "gy", None, None),
        P("layer", "gx", "gy", None, None),
        P("layer", "gx", "gy", None, None),
        P("layer", "gx", "gy", None),
    )
    out_specs = (P("layer", "gx", "gy", None, None), P("layer", "gx", "gy", None, None))
    return jax.shard_map(body, mesh=mesh, in_specs=in_specs, out_specs=out_specs, check_vma=False)
```

```python
import math

import jax
import jax.numpy as jnp
import numpy as np
from jax import lax
from jax.sharding import PartitionSpec as P

PATCH_X = 14
PATCH_Y = 4


v_pi = -2.7
v_sigma = 0.48
decay_len = 0.319
layer_gap = 3.35 / 1.42
cut_radius = 3.5
hop_scale = 12.0
twist_angle = 1.05 * math.pi / 180.0
root_three = math.sqrt(3.0)
cell_w = 4.0 * root_three
cell_h = 24.0
sigma_gain = v_sigma * math.exp((layer_gap - 1.0) / decay_len)
HI = lax.Precision.HIGHEST
MID = lax.Precision.HIGH
OFFSETS = [(a, b) for a in (-1, 0, 1) for b in (-1, 0, 1)]


def _base_np():
    orbital = np.arange(128)
    sub = orbital % 4
    cell = orbital // 4
    inner_x = np.where((sub == 1) | (sub == 2), root_three / 2.0, 0.0)
    inner_y = np.select([sub == 1, sub == 2, sub == 3], [0.5, 1.5, 2.0], 0.0)
    return np.stack([(cell // 8) * root_three + inner_x - cell_w / 2.0, (cell % 8) * 3.0 + inner_y - cell_h / 2.0])


def _reach_sets():
    base = _base_np()
    c, s = math.cos(twist_angle), math.sin(twist_angle)
    rot = np.array([[c, -s], [s, c]])
    margin = 0.5
    plane_r = cut_radius + margin
    inter_r = math.sqrt(cut_radius**2 - layer_gap**2) + margin
    twists = [
        np.array([[cell_w * (i - (PATCH_X - 1) / 2.0)], [cell_h * (j - (PATCH_Y - 1) / 2.0)]])
        for i in range(PATCH_X)
        for j in range(PATCH_Y)
    ]
    sets = {}
    for a, b in OFFSETS:
        shift = np.array([[a * cell_w], [b * cell_h]])
        gap = base[:, :, None] - base[:, None, :] - shift[:, :, None]
        mask = np.sqrt((gap**2).sum(0)) < plane_r
        for e in twists:
            turned = rot @ base + (rot - np.eye(2)) @ e
            for own, near in ((base, turned), (turned, base)):
                gap = own[:, :, None] - near[:, None, :] - shift[:, :, None]
                mask |= np.sqrt((gap**2).sum(0)) < inter_r
        sets[(a, b)] = (np.nonzero(mask.any(1))[0], np.nonzero(mask.any(0))[0])
    return sets


REACH = _reach_sets()


def _one_hot(idx):
    table = np.zeros((128, len(idx)), np.float32)
    table[idx, np.arange(len(idx))] = 1.0
    return table


def pick(x, idx):
    if len(idx) == x.shape[-1]:
        return x
    if np.all(np.diff(idx) == 1):
        return x[..., idx[0] : idx[0] + len(idx)]
    return jnp.einsum("...q,qk->...k", x, _one_hot(idx), precision=HI)


def extended_2(value, sides, width):
    for axis, dim in sides:
        devices, length = (lax.axis_size(axis), value.shape[dim])
        up = [(i, (i + 1) % devices) for i in range(devices)]
        down = [(j, i) for i, j in up]
        last = lax.slice_in_dim(value, length - width, length, axis=dim)
        first = lax.slice_in_dim(value, 0, width, axis=dim)
        if devices == 2:
            both = lax.ppermute(jnp.concatenate([last, first], axis=dim), axis, up)
            before = lax.slice_in_dim(both, 0, width, axis=dim)
            after = lax.slice_in_dim(both, width, 2 * width, axis=dim)
        else:
            before = lax.ppermute(last, axis, up)
            after = lax.ppermute(first, axis, down)
        value = jnp.concatenate([before, value, after], axis=dim)
    return value


def partner_2(value, axis, distance):
    return lax.ppermute(value, axis, [(i, i ^ 1 << distance) for i in range(lax.axis_size(axis))])


def lattice(cos_vals, sin_vals):
    base = jnp.asarray(_base_np(), jnp.float32)
    rot_x = cos_vals[:, None] * base[0] - sin_vals[:, None] * base[1]
    rot_y = sin_vals[:, None] * base[0] + cos_vals[:, None] * base[1]
    return jnp.stack([rot_x, rot_y], axis=1)


def twist_offsets(cos_vals, sin_vals, row_ids, col_ids):
    along_x = cell_w * ((row_ids % PATCH_X).astype(jnp.float32) - (PATCH_X - 1) / 2.0)
    along_y = cell_h * ((col_ids % PATCH_Y).astype(jnp.float32) - (PATCH_Y - 1) / 2.0)
    cos_less = (cos_vals - 1.0)[:, None, None]
    sin_cast = sin_vals[:, None, None]
    shift_x = cos_less * along_x[None, :, None] - sin_cast * along_y[None, None, :]
    shift_y = sin_cast * along_x[None, :, None] + cos_less * along_y[None, None, :]
    return jnp.stack([shift_x, shift_y], axis=-1)[..., None]


def taper(dist_sq):
    scaled = dist_sq / (cut_radius * cut_radius)
    return jnp.maximum(1.0 - scaled * scaled, 0.0)


def plane_block(own_pos, near_pos, shift_x, shift_y, self_rows):
    delta_x = own_pos[..., 0, :, None] - near_pos[..., 0, None, :] - shift_x
    delta_y = own_pos[..., 1, :, None] - near_pos[..., 1, None, :] - shift_y
    dist_sq = delta_x * delta_x + delta_y * delta_y
    spread = jnp.sqrt(dist_sq)
    hopping = v_pi * jnp.exp(-(spread - 1.0) / decay_len) * taper(dist_sq)
    if self_rows:
        orbital = jnp.arange(128, dtype=jnp.int32)
        hopping = jnp.where(orbital[:, None] == orbital[None, :], 0.0, hopping)
    return hopping


def inter_block(own_pos, near_pos, shift_x, shift_y):
    delta_x = own_pos[..., 0, :, None] - near_pos[..., 0, None, :] - shift_x
    delta_y = own_pos[..., 1, :, None] - near_pos[..., 1, None, :] - shift_y
    dist_sq = delta_x * delta_x + delta_y * delta_y + layer_gap * layer_gap
    spread = jnp.sqrt(dist_sq)
    cosine_sq = layer_gap * layer_gap / dist_sq
    decay = jnp.exp(-(spread - 1.0) / decay_len)
    bonds = decay * (v_pi * (1.0 - cosine_sq) + sigma_gain * cosine_sq)
    return bonds * taper(dist_sq)


def _halo_options(n):
    if n == 1:
        return [(0, ("last", "all", "first"))]
    if n == 2:
        return [(0, ("all",)), (1, ("last", "first"))]
    return [(-1, ("last",)), (0, ("all",)), (1, ("first",))]


def _region(value, kind, axis):
    length = value.shape[axis]
    if kind == "last":
        return lax.slice_in_dim(value, length - 1, length, axis=axis)
    if kind == "first":
        return lax.slice_in_dim(value, 0, 1, axis=axis)
    return value


def exchange(value):
    stacked = jnp.concatenate([value, partner_2(value, "layer", 0)], axis=0)
    axes = ("gx", "gy")
    sizes = [lax.axis_size(a) for a in axes]
    tile = {1: stacked.shape[1], 2: stacked.shape[2]}
    pieces = {}
    for step_x, kinds_x in _halo_options(sizes[0]):
        along_x = jnp.concatenate([_region(stacked, r, 1) for r in kinds_x], axis=1)
        for step_y, kinds_y in _halo_options(sizes[1]):
            part = jnp.concatenate([_region(along_x, r, 2) for r in kinds_y], axis=2)
            if (step_x, step_y) != (0, 0):
                pairs = []
                for x in range(sizes[0]):
                    for y in range(sizes[1]):
                        dst = ((x - step_x) % sizes[0]) * sizes[1] + (y - step_y) % sizes[1]
                        pairs.append((x * sizes[1] + y, dst))
                part = lax.ppermute(part, axes, pairs)
            at_x = 0
            for rx in kinds_x:
                wide_x = tile[1] if rx == "all" else 1
                at_y = 0
                for ry in kinds_y:
                    wide_y = tile[2] if ry == "all" else 1
                    pieces[(rx, ry)] = part[:, at_x : at_x + wide_x, at_y : at_y + wide_y]
                    at_y += wide_y
                at_x += wide_x
    order = ("last", "all", "first")
    rows = [jnp.concatenate([pieces[(rx, ry)] for ry in order], axis=2) for rx in order]
    return stacked, jnp.concatenate(rows, axis=1)


def body(prev_vec, cur_vec, displace, potential):
    layer_id = lax.axis_index("layer")
    tile_x = displace.shape[1]
    tile_y = displace.shape[2]
    cos_twist = math.cos(twist_angle)
    sin_twist = math.sin(twist_angle)
    width = cur_vec.shape[-2]
    packed = exchange(jnp.concatenate([cur_vec, displace], axis=-2))
    vec_ext = tuple(s[..., :width, :] for s in packed)
    own_disp, ext_disp = (s[..., width:, :] for s in packed)
    layer_up = layer_id == 1
    cos_vals = jnp.stack(
        [jnp.where(layer_up, cos_twist, 1.0), jnp.where(layer_up, 1.0, cos_twist)]
    ).astype(jnp.float32)
    sin_vals = jnp.stack(
        [jnp.where(layer_up, sin_twist, 0.0), jnp.where(layer_up, 0.0, sin_twist)]
    ).astype(jnp.float32)
    grid = lattice(cos_vals, sin_vals)[:, None, None]
    places = ext_disp + grid
    centre = own_disp + grid
    row_count = tile_x * lax.axis_size("gx")
    col_count = tile_y * lax.axis_size("gy")
    row_ids = (
        lax.axis_index("gx") * tile_x + jnp.arange(tile_x + 2, dtype=jnp.int32) - 1 + row_count
    ) % row_count
    col_ids = (
        lax.axis_index("gy") * tile_y + jnp.arange(tile_y + 2, dtype=jnp.int32) - 1 + col_count
    ) % col_count
    turn = twist_offsets(cos_vals, sin_vals, row_ids, col_ids)
    twisted = places + turn

    def own_view(value, a, b):
        return value[:, 1 + a : 1 + a + tile_x, 1 + b : 1 + b + tile_y]

    own_pos = centre[0]
    own_shift = own_view(turn[:1], 0, 0)[0]
    cos_own = cos_vals[0]
    sin_own = sin_vals[0]
    narrow = [o for o in OFFSETS if len(REACH[o][0]) < 64]
    narrow_rows = np.concatenate([REACH[o][0] for o in narrow])
    picked = jnp.einsum("...q,qk->...k", own_pos, _one_hot(narrow_rows), precision=HI)
    blocks = {}
    columns = {}
    at = 0
    for a, b in OFFSETS:
        rows, cols = REACH[(a, b)]
        if len(rows) < 64:
            own_rows = picked[..., at : at + len(rows)]
            at += len(rows)
            cols = np.arange(128)
        else:
            own_rows = pick(own_pos, rows)
        shift_x = cos_own * (a * cell_w) - sin_own * (b * cell_h)
        shift_y = sin_own * (a * cell_w) + cos_own * (b * cell_h)
        if (a, b) == (0, 0):
            near_pos = centre[0]
            near_twist = centre[1] + own_view(turn[1:], 0, 0)[0]
        else:
            near_pos = pick(own_view(places[:1], a, b)[0], cols)
            near_twist = pick(own_view(twisted[1:], a, b)[0], cols)
        plane = plane_block(own_rows, near_pos, shift_x, shift_y, a == 0 and b == 0)
        inter = inter_block(own_rows + own_shift, near_twist, a * cell_w, b * cell_h)
        if (a, b) == (0, 0):
            own_centre = lax.optimization_barrier(plane)
            blocks[(a, b)] = inter
        else:
            blocks[(a, b)] = jnp.stack([plane, inter])
        columns[(a, b)] = cols
    blocks = lax.optimization_barrier(blocks)

    scatter = np.zeros((len(narrow_rows), 128), np.float32)
    scatter[np.arange(len(narrow_rows)), narrow_rows] = 1.0

    def hop_terms(vectors, extended):
        full = potential[0][..., None, :] * vectors[0]
        parts = {}
        centre = blocks[(0, 0)]
        full = full + jnp.einsum("xycq,xypq->xycp", vectors[0], own_centre, precision=MID)
        full = full + jnp.einsum("xycq,xypq->xycp", extended[0][1], centre, precision=MID)
        for a, b in OFFSETS:
            if (a, b) != (0, 0):
                near = pick(own_view(extended[1], a, b), columns[(a, b)])
                parts[(a, b)] = jnp.einsum("kxycq,kxypq->xycp", near, blocks[(a, b)], precision=MID)
        full = full + jnp.concatenate([parts[(-1, 0)], parts[(1, 0)]], axis=-1)
        full = full + jnp.einsum(
            "xycp,pn->xycn", jnp.concatenate([parts[o] for o in narrow], axis=-1), scatter, precision=MID
        )
        return (full / hop_scale)[None]

    first_term = 2.0 * hop_terms(cur_vec, vec_ext) - prev_vec
    second_term = 2.0 * hop_terms(first_term, exchange(first_term)) - cur_vec
    return (first_term, second_term)


def solution(mesh):
    in_specs = (
        P("layer", "gx", "gy", None, None),
        P("layer", "gx", "gy", None, None),
        P("layer", "gx", "gy", None, None),
        P("layer", "gx", "gy", None),
    )
    out_specs = (P("layer", "gx", "gy", None, None), P("layer", "gx", "gy", None, None))
    return jax.shard_map(body, mesh=mesh, in_specs=in_specs, out_specs=out_specs, check_vma=False)
```

```python
import math

import jax
import jax.numpy as jnp
import numpy as np
from jax import lax
from jax.sharding import PartitionSpec as P

PATCH_X = 14
PATCH_Y = 4


v_pi = -2.7
v_sigma = 0.48
decay_len = 0.319
layer_gap = 3.35 / 1.42
cut_radius = 3.5
hop_scale = 12.0
twist_angle = 1.05 * math.pi / 180.0
root_three = math.sqrt(3.0)
cell_w = 4.0 * root_three
cell_h = 24.0
sigma_gain = v_sigma * math.exp((layer_gap - 1.0) / decay_len)
HI = lax.Precision.HIGHEST
MID = lax.Precision.HIGH
OFFSETS = [(a, b) for a in (-1, 0, 1) for b in (-1, 0, 1)]


def _base_np():
    orbital = np.arange(128)
    sub = orbital % 4
    cell = orbital // 4
    inner_x = np.where((sub == 1) | (sub == 2), root_three / 2.0, 0.0)
    inner_y = np.select([sub == 1, sub == 2, sub == 3], [0.5, 1.5, 2.0], 0.0)
    return np.stack([(cell // 8) * root_three + inner_x - cell_w / 2.0, (cell % 8) * 3.0 + inner_y - cell_h / 2.0])


def _reach_sets():
    base = _base_np()
    c, s = math.cos(twist_angle), math.sin(twist_angle)
    rot = np.array([[c, -s], [s, c]])
    margin = 0.5
    plane_r = cut_radius + margin
    inter_r = math.sqrt(cut_radius**2 - layer_gap**2) + margin
    twists = [
        np.array([[cell_w * (i - (PATCH_X - 1) / 2.0)], [cell_h * (j - (PATCH_Y - 1) / 2.0)]])
        for i in range(PATCH_X)
        for j in range(PATCH_Y)
    ]
    sets = {}
    for a, b in OFFSETS:
        shift = np.array([[a * cell_w], [b * cell_h]])
        gap = base[:, :, None] - base[:, None, :] - shift[:, :, None]
        mask = np.sqrt((gap**2).sum(0)) < plane_r
        for e in twists:
            turned = rot @ base + (rot - np.eye(2)) @ e
            for own, near in ((base, turned), (turned, base)):
                gap = own[:, :, None] - near[:, None, :] - shift[:, :, None]
                mask |= np.sqrt((gap**2).sum(0)) < inter_r
        sets[(a, b)] = (np.nonzero(mask.any(1))[0], np.nonzero(mask.any(0))[0])
    return sets


REACH = _reach_sets()


def _one_hot(idx):
    table = np.zeros((128, len(idx)), np.float32)
    table[idx, np.arange(len(idx))] = 1.0
    return table


def pick(x, idx):
    if len(idx) == x.shape[-1]:
        return x
    if np.all(np.diff(idx) == 1):
        return x[..., idx[0] : idx[0] + len(idx)]
    return jnp.einsum("...q,qk->...k", x, _one_hot(idx), precision=HI)


def extended_2(value, sides, width):
    for axis, dim in sides:
        devices, length = (lax.axis_size(axis), value.shape[dim])
        up = [(i, (i + 1) % devices) for i in range(devices)]
        down = [(j, i) for i, j in up]
        last = lax.slice_in_dim(value, length - width, length, axis=dim)
        first = lax.slice_in_dim(value, 0, width, axis=dim)
        if devices == 2:
            both = lax.ppermute(jnp.concatenate([last, first], axis=dim), axis, up)
            before = lax.slice_in_dim(both, 0, width, axis=dim)
            after = lax.slice_in_dim(both, width, 2 * width, axis=dim)
        else:
            before = lax.ppermute(last, axis, up)
            after = lax.ppermute(first, axis, down)
        value = jnp.concatenate([before, value, after], axis=dim)
    return value


def partner_2(value, axis, distance):
    return lax.ppermute(value, axis, [(i, i ^ 1 << distance) for i in range(lax.axis_size(axis))])


def lattice(cos_vals, sin_vals):
    base = jnp.asarray(_base_np(), jnp.float32)
    rot_x = cos_vals[:, None] * base[0] - sin_vals[:, None] * base[1]
    rot_y = sin_vals[:, None] * base[0] + cos_vals[:, None] * base[1]
    return jnp.stack([rot_x, rot_y], axis=1)


def twist_offsets(cos_vals, sin_vals, row_ids, col_ids):
    along_x = cell_w * ((row_ids % PATCH_X).astype(jnp.float32) - (PATCH_X - 1) / 2.0)
    along_y = cell_h * ((col_ids % PATCH_Y).astype(jnp.float32) - (PATCH_Y - 1) / 2.0)
    cos_less = (cos_vals - 1.0)[:, None, None]
    sin_cast = sin_vals[:, None, None]
    shift_x = cos_less * along_x[None, :, None] - sin_cast * along_y[None, None, :]
    shift_y = sin_cast * along_x[None, :, None] + cos_less * along_y[None, None, :]
    return jnp.stack([shift_x, shift_y], axis=-1)[..., None]


def taper(dist_sq):
    scaled = dist_sq / (cut_radius * cut_radius)
    return jnp.maximum(1.0 - scaled * scaled, 0.0)


def plane_block(own_pos, near_pos, shift_x, shift_y, self_rows):
    delta_x = own_pos[..., 0, :, None] - near_pos[..., 0, None, :] - shift_x
    delta_y = own_pos[..., 1, :, None] - near_pos[..., 1, None, :] - shift_y
    dist_sq = delta_x * delta_x + delta_y * delta_y
    spread = jnp.sqrt(dist_sq)
    hopping = v_pi * jnp.exp(-(spread - 1.0) / decay_len) * taper(dist_sq)
    if self_rows:
        orbital = jnp.arange(128, dtype=jnp.int32)
        hopping = jnp.where(orbital[:, None] == orbital[None, :], 0.0, hopping)
    return hopping


def inter_block(own_pos, near_pos, shift_x, shift_y):
    delta_x = own_pos[..., 0, :, None] - near_pos[..., 0, None, :] - shift_x
    delta_y = own_pos[..., 1, :, None] - near_pos[..., 1, None, :] - shift_y
    dist_sq = delta_x * delta_x + delta_y * delta_y + layer_gap * layer_gap
    spread = jnp.sqrt(dist_sq)
    cosine_sq = layer_gap * layer_gap / dist_sq
    decay = jnp.exp(-(spread - 1.0) / decay_len)
    bonds = decay * (v_pi * (1.0 - cosine_sq) + sigma_gain * cosine_sq)
    return bonds * taper(dist_sq)


def _halo_options(n):
    if n == 1:
        return [(0, ("last", "all", "first"))]
    if n == 2:
        return [(0, ("all",)), (1, ("last", "first"))]
    return [(-1, ("last",)), (0, ("all",)), (1, ("first",))]


def _region(value, kind, axis):
    length = value.shape[axis]
    if kind == "last":
        return lax.slice_in_dim(value, length - 1, length, axis=axis)
    if kind == "first":
        return lax.slice_in_dim(value, 0, 1, axis=axis)
    return value


def exchange(value):
    stacked = jnp.concatenate([value, partner_2(value, "layer", 0)], axis=0)
    axes = ("gx", "gy")
    sizes = [lax.axis_size(a) for a in axes]
    tile = {1: stacked.shape[1], 2: stacked.shape[2]}
    pieces = {}
    for step_x, kinds_x in _halo_options(sizes[0]):
        along_x = jnp.concatenate([_region(stacked, r, 1) for r in kinds_x], axis=1)
        for step_y, kinds_y in _halo_options(sizes[1]):
            part = jnp.concatenate([_region(along_x, r, 2) for r in kinds_y], axis=2)
            if (step_x, step_y) != (0, 0):
                pairs = []
                for x in range(sizes[0]):
                    for y in range(sizes[1]):
                        dst = ((x - step_x) % sizes[0]) * sizes[1] + (y - step_y) % sizes[1]
                        pairs.append((x * sizes[1] + y, dst))
                part = lax.ppermute(part, axes, pairs)
            at_x = 0
            for rx in kinds_x:
                wide_x = tile[1] if rx == "all" else 1
                at_y = 0
                for ry in kinds_y:
                    wide_y = tile[2] if ry == "all" else 1
                    pieces[(rx, ry)] = part[:, at_x : at_x + wide_x, at_y : at_y + wide_y]
                    at_y += wide_y
                at_x += wide_x
    order = ("last", "all", "first")
    rows = [jnp.concatenate([pieces[(rx, ry)] for ry in order], axis=2) for rx in order]
    return stacked, jnp.concatenate(rows, axis=1)


def body(prev_vec, cur_vec, displace, potential):
    layer_id = lax.axis_index("layer")
    tile_x = displace.shape[1]
    tile_y = displace.shape[2]
    cos_twist = math.cos(twist_angle)
    sin_twist = math.sin(twist_angle)
    width = cur_vec.shape[-2]
    packed = exchange(jnp.concatenate([cur_vec, displace], axis=-2))
    vec_ext = tuple(s[..., :width, :] for s in packed)
    own_disp, ext_disp = (s[..., width:, :] for s in packed)
    layer_up = layer_id == 1
    cos_vals = jnp.stack(
        [jnp.where(layer_up, cos_twist, 1.0), jnp.where(layer_up, 1.0, cos_twist)]
    ).astype(jnp.float32)
    sin_vals = jnp.stack(
        [jnp.where(layer_up, sin_twist, 0.0), jnp.where(layer_up, 0.0, sin_twist)]
    ).astype(jnp.float32)
    grid = lattice(cos_vals, sin_vals)[:, None, None]
    places = ext_disp + grid
    centre = own_disp + grid
    row_count = tile_x * lax.axis_size("gx")
    col_count = tile_y * lax.axis_size("gy")
    row_ids = (
        lax.axis_index("gx") * tile_x + jnp.arange(tile_x + 2, dtype=jnp.int32) - 1 + row_count
    ) % row_count
    col_ids = (
        lax.axis_index("gy") * tile_y + jnp.arange(tile_y + 2, dtype=jnp.int32) - 1 + col_count
    ) % col_count
    turn = twist_offsets(cos_vals, sin_vals, row_ids, col_ids)
    twisted = places + turn

    def own_view(value, a, b):
        return value[:, 1 + a : 1 + a + tile_x, 1 + b : 1 + b + tile_y]

    own_pos = centre[0]
    own_shift = own_view(turn[:1], 0, 0)[0]
    cos_own = cos_vals[0]
    sin_own = sin_vals[0]
    narrow = [o for o in OFFSETS if len(REACH[o][0]) < 64]
    narrow_rows = np.concatenate([REACH[o][0] for o in narrow])
    picked = jnp.einsum("...q,qk->...k", own_pos, _one_hot(narrow_rows), precision=HI)
    blocks = {}
    columns = {}
    at = 0
    for a, b in OFFSETS:
        rows, cols = REACH[(a, b)]
        if len(rows) < 64:
            own_rows = picked[..., at : at + len(rows)]
            at += len(rows)
            cols = np.arange(128)
        else:
            own_rows = pick(own_pos, rows)
        shift_x = cos_own * (a * cell_w) - sin_own * (b * cell_h)
        shift_y = sin_own * (a * cell_w) + cos_own * (b * cell_h)
        if (a, b) == (0, 0):
            near_pos = centre[0]
            near_twist = centre[1] + own_view(turn[1:], 0, 0)[0]
        else:
            near_pos = pick(own_view(places[:1], a, b)[0], cols)
            near_twist = pick(own_view(twisted[1:], a, b)[0], cols)
        plane = plane_block(own_rows, near_pos, shift_x, shift_y, a == 0 and b == 0)
        inter = inter_block(own_rows + own_shift, near_twist, a * cell_w, b * cell_h)
        blocks[(a, b)] = jnp.stack([plane, inter])
        columns[(a, b)] = cols
    blocks = lax.optimization_barrier(blocks)

    scatter = np.zeros((len(narrow_rows), 128), np.float32)
    scatter[np.arange(len(narrow_rows)), narrow_rows] = 1.0

    def hop_terms(vectors, extended):
        full = potential[0][..., None, :] * vectors[0]
        parts = {}
        centre = blocks[(0, 0)]
        full = full + jnp.einsum("xycq,xypq->xycp", vectors[0], centre[0], precision=MID)
        full = full + jnp.einsum("xycq,xypq->xycp", extended[0][1], centre[1], precision=MID)
        for a, b in OFFSETS:
            if (a, b) != (0, 0):
                near = pick(own_view(extended[1], a, b), columns[(a, b)])
                parts[(a, b)] = jnp.einsum("kxycq,kxypq->xycp", near, blocks[(a, b)], precision=MID)
        full = full + jnp.concatenate([parts[(-1, 0)], parts[(1, 0)]], axis=-1)
        at = 0
        for o in narrow:
            width = parts[o].shape[-1]
            full = full + jnp.einsum("xycp,pn->xycn", parts[o], scatter[at : at + width], precision=MID)
            at += width
        return (full / hop_scale)[None]

    first_term = 2.0 * hop_terms(cur_vec, vec_ext) - prev_vec
    second_term = 2.0 * hop_terms(first_term, exchange(first_term)) - cur_vec
    return (first_term, second_term)


def solution(mesh):
    in_specs = (
        P("layer", "gx", "gy", None, None),
        P("layer", "gx", "gy", None, None),
        P("layer", "gx", "gy", None, None),
        P("layer", "gx", "gy", None),
    )
    out_specs = (P("layer", "gx", "gy", None, None), P("layer", "gx", "gy", None, None))
    return jax.shard_map(body, mesh=mesh, in_specs=in_specs, out_specs=out_specs, check_vma=False)
```

```python
import math

import jax
import jax.numpy as jnp
import numpy as np
from jax import lax
from jax.sharding import PartitionSpec as P

PATCH_X = 14
PATCH_Y = 4


v_pi = -2.7
v_sigma = 0.48
decay_len = 0.319
layer_gap = 3.35 / 1.42
cut_radius = 3.5
hop_scale = 12.0
twist_angle = 1.05 * math.pi / 180.0
root_three = math.sqrt(3.0)
cell_w = 4.0 * root_three
cell_h = 24.0
sigma_gain = v_sigma * math.exp((layer_gap - 1.0) / decay_len)
HI = lax.Precision.HIGHEST
MID = lax.Precision.HIGH
OFFSETS = [(a, b) for a in (-1, 0, 1) for b in (-1, 0, 1)]


def _base_np():
    orbital = np.arange(128)
    sub = orbital % 4
    cell = orbital // 4
    inner_x = np.where((sub == 1) | (sub == 2), root_three / 2.0, 0.0)
    inner_y = np.select([sub == 1, sub == 2, sub == 3], [0.5, 1.5, 2.0], 0.0)
    return np.stack([(cell // 8) * root_three + inner_x - cell_w / 2.0, (cell % 8) * 3.0 + inner_y - cell_h / 2.0])


def _reach_sets():
    base = _base_np()
    c, s = math.cos(twist_angle), math.sin(twist_angle)
    rot = np.array([[c, -s], [s, c]])
    margin = 0.5
    plane_r = cut_radius + margin
    inter_r = math.sqrt(cut_radius**2 - layer_gap**2) + margin
    twists = [
        np.array([[cell_w * (i - (PATCH_X - 1) / 2.0)], [cell_h * (j - (PATCH_Y - 1) / 2.0)]])
        for i in range(PATCH_X)
        for j in range(PATCH_Y)
    ]
    sets = {}
    for a, b in OFFSETS:
        shift = np.array([[a * cell_w], [b * cell_h]])
        gap = base[:, :, None] - base[:, None, :] - shift[:, :, None]
        mask = np.sqrt((gap**2).sum(0)) < plane_r
        for e in twists:
            turned = rot @ base + (rot - np.eye(2)) @ e
            for own, near in ((base, turned), (turned, base)):
                gap = own[:, :, None] - near[:, None, :] - shift[:, :, None]
                mask |= np.sqrt((gap**2).sum(0)) < inter_r
        sets[(a, b)] = (np.nonzero(mask.any(1))[0], np.nonzero(mask.any(0))[0])
    return sets


REACH = _reach_sets()


def _one_hot(idx):
    table = np.zeros((128, len(idx)), np.float32)
    table[idx, np.arange(len(idx))] = 1.0
    return table


def pick(x, idx):
    if len(idx) == x.shape[-1]:
        return x
    if np.all(np.diff(idx) == 1):
        return x[..., idx[0] : idx[0] + len(idx)]
    return jnp.einsum("...q,qk->...k", x, _one_hot(idx), precision=HI)


def extended_2(value, sides, width):
    for axis, dim in sides:
        devices, length = (lax.axis_size(axis), value.shape[dim])
        up = [(i, (i + 1) % devices) for i in range(devices)]
        down = [(j, i) for i, j in up]
        last = lax.slice_in_dim(value, length - width, length, axis=dim)
        first = lax.slice_in_dim(value, 0, width, axis=dim)
        if devices == 2:
            both = lax.ppermute(jnp.concatenate([last, first], axis=dim), axis, up)
            before = lax.slice_in_dim(both, 0, width, axis=dim)
            after = lax.slice_in_dim(both, width, 2 * width, axis=dim)
        else:
            before = lax.ppermute(last, axis, up)
            after = lax.ppermute(first, axis, down)
        value = jnp.concatenate([before, value, after], axis=dim)
    return value


def partner_2(value, axis, distance):
    return lax.ppermute(value, axis, [(i, i ^ 1 << distance) for i in range(lax.axis_size(axis))])


def lattice(cos_vals, sin_vals):
    base = jnp.asarray(_base_np(), jnp.float32)
    rot_x = cos_vals[:, None] * base[0] - sin_vals[:, None] * base[1]
    rot_y = sin_vals[:, None] * base[0] + cos_vals[:, None] * base[1]
    return jnp.stack([rot_x, rot_y], axis=1)


def twist_offsets(cos_vals, sin_vals, row_ids, col_ids):
    along_x = cell_w * ((row_ids % PATCH_X).astype(jnp.float32) - (PATCH_X - 1) / 2.0)
    along_y = cell_h * ((col_ids % PATCH_Y).astype(jnp.float32) - (PATCH_Y - 1) / 2.0)
    cos_less = (cos_vals - 1.0)[:, None, None]
    sin_cast = sin_vals[:, None, None]
    shift_x = cos_less * along_x[None, :, None] - sin_cast * along_y[None, None, :]
    shift_y = sin_cast * along_x[None, :, None] + cos_less * along_y[None, None, :]
    return jnp.stack([shift_x, shift_y], axis=-1)[..., None]


def taper(dist_sq):
    scaled = dist_sq / (cut_radius * cut_radius)
    return jnp.maximum(1.0 - scaled * scaled, 0.0)


def plane_block(own_pos, near_pos, shift_x, shift_y, self_rows):
    delta_x = own_pos[..., 0, :, None] - near_pos[..., 0, None, :] - shift_x
    delta_y = own_pos[..., 1, :, None] - near_pos[..., 1, None, :] - shift_y
    dist_sq = delta_x * delta_x + delta_y * delta_y
    spread = jnp.sqrt(dist_sq)
    hopping = v_pi * jnp.exp(-(spread - 1.0) / decay_len) * taper(dist_sq)
    if self_rows:
        orbital = jnp.arange(128, dtype=jnp.int32)
        hopping = jnp.where(orbital[:, None] == orbital[None, :], 0.0, hopping)
    return hopping


def inter_block(own_pos, near_pos, shift_x, shift_y):
    delta_x = own_pos[..., 0, :, None] - near_pos[..., 0, None, :] - shift_x
    delta_y = own_pos[..., 1, :, None] - near_pos[..., 1, None, :] - shift_y
    dist_sq = delta_x * delta_x + delta_y * delta_y + layer_gap * layer_gap
    spread = jnp.sqrt(dist_sq)
    cosine_sq = layer_gap * layer_gap / dist_sq
    decay = jnp.exp(-(spread - 1.0) / decay_len)
    bonds = decay * (v_pi * (1.0 - cosine_sq) + sigma_gain * cosine_sq)
    return bonds * taper(dist_sq)


def _halo_options(n):
    if n == 1:
        return [(0, ("last", "all", "first"))]
    if n == 2:
        return [(0, ("all",)), (1, ("last", "first"))]
    return [(-1, ("last",)), (0, ("all",)), (1, ("first",))]


def _region(value, kind, axis):
    length = value.shape[axis]
    if kind == "last":
        return lax.slice_in_dim(value, length - 1, length, axis=axis)
    if kind == "first":
        return lax.slice_in_dim(value, 0, 1, axis=axis)
    return value


def exchange(value):
    stacked = jnp.concatenate([value, partner_2(value, "layer", 0)], axis=0)
    axes = ("gx", "gy")
    sizes = [lax.axis_size(a) for a in axes]
    tile = {1: stacked.shape[1], 2: stacked.shape[2]}
    pieces = {}
    for step_x, kinds_x in _halo_options(sizes[0]):
        along_x = jnp.concatenate([_region(stacked, r, 1) for r in kinds_x], axis=1)
        for step_y, kinds_y in _halo_options(sizes[1]):
            part = jnp.concatenate([_region(along_x, r, 2) for r in kinds_y], axis=2)
            if (step_x, step_y) != (0, 0):
                pairs = []
                for x in range(sizes[0]):
                    for y in range(sizes[1]):
                        dst = ((x - step_x) % sizes[0]) * sizes[1] + (y - step_y) % sizes[1]
                        pairs.append((x * sizes[1] + y, dst))
                part = lax.ppermute(part, axes, pairs)
            at_x = 0
            for rx in kinds_x:
                wide_x = tile[1] if rx == "all" else 1
                at_y = 0
                for ry in kinds_y:
                    wide_y = tile[2] if ry == "all" else 1
                    pieces[(rx, ry)] = part[:, at_x : at_x + wide_x, at_y : at_y + wide_y]
                    at_y += wide_y
                at_x += wide_x
    order = ("last", "all", "first")
    rows = [jnp.concatenate([pieces[(rx, ry)] for ry in order], axis=2) for rx in order]
    return stacked, jnp.concatenate(rows, axis=1)


def body(prev_vec, cur_vec, displace, potential):
    layer_id = lax.axis_index("layer")
    tile_x = displace.shape[1]
    tile_y = displace.shape[2]
    cos_twist = math.cos(twist_angle)
    sin_twist = math.sin(twist_angle)
    width = cur_vec.shape[-2]
    spare = jnp.zeros(displace.shape[:-2] + (8 - displace.shape[-2] % 8, 128), jnp.float32)
    packed = exchange(jnp.concatenate([cur_vec, displace, spare], axis=-2))
    vec_ext = tuple(s[..., :width, :] for s in packed)
    own_disp, ext_disp = (s[..., width : width + displace.shape[-2], :] for s in packed)
    layer_up = layer_id == 1
    cos_vals = jnp.stack(
        [jnp.where(layer_up, cos_twist, 1.0), jnp.where(layer_up, 1.0, cos_twist)]
    ).astype(jnp.float32)
    sin_vals = jnp.stack(
        [jnp.where(layer_up, sin_twist, 0.0), jnp.where(layer_up, 0.0, sin_twist)]
    ).astype(jnp.float32)
    grid = lattice(cos_vals, sin_vals)[:, None, None]
    places = ext_disp + grid
    centre = own_disp + grid
    row_count = tile_x * lax.axis_size("gx")
    col_count = tile_y * lax.axis_size("gy")
    row_ids = (
        lax.axis_index("gx") * tile_x + jnp.arange(tile_x + 2, dtype=jnp.int32) - 1 + row_count
    ) % row_count
    col_ids = (
        lax.axis_index("gy") * tile_y + jnp.arange(tile_y + 2, dtype=jnp.int32) - 1 + col_count
    ) % col_count
    turn = twist_offsets(cos_vals, sin_vals, row_ids, col_ids)
    twisted = places + turn

    def own_view(value, a, b):
        return value[:, 1 + a : 1 + a + tile_x, 1 + b : 1 + b + tile_y]

    own_pos = centre[0]
    own_shift = own_view(turn[:1], 0, 0)[0]
    cos_own = cos_vals[0]
    sin_own = sin_vals[0]
    narrow = [o for o in OFFSETS if len(REACH[o][0]) < 64]
    narrow_rows = np.concatenate([REACH[o][0] for o in narrow])
    picked = jnp.einsum("...q,qk->...k", own_pos, _one_hot(narrow_rows), precision=HI)
    blocks = {}
    columns = {}
    at = 0
    for a, b in OFFSETS:
        rows, cols = REACH[(a, b)]
        if len(rows) < 64:
            own_rows = picked[..., at : at + len(rows)]
            at += len(rows)
            cols = np.arange(128)
        else:
            own_rows = pick(own_pos, rows)
        shift_x = cos_own * (a * cell_w) - sin_own * (b * cell_h)
        shift_y = sin_own * (a * cell_w) + cos_own * (b * cell_h)
        if (a, b) == (0, 0):
            near_pos = centre[0]
            near_twist = centre[1] + own_view(turn[1:], 0, 0)[0]
        else:
            near_pos = pick(own_view(places[:1], a, b)[0], cols)
            near_twist = pick(own_view(twisted[1:], a, b)[0], cols)
        plane = plane_block(own_rows, near_pos, shift_x, shift_y, a == 0 and b == 0)
        inter = inter_block(own_rows + own_shift, near_twist, a * cell_w, b * cell_h)
        blocks[(a, b)] = jnp.stack([plane, inter])
        columns[(a, b)] = cols
    blocks = lax.optimization_barrier(blocks)

    scatter = np.zeros((len(narrow_rows), 128), np.float32)
    scatter[np.arange(len(narrow_rows)), narrow_rows] = 1.0

    def hop_terms(vectors, extended):
        full = potential[0][..., None, :] * vectors[0]
        parts = {}
        centre = blocks[(0, 0)]
        full = full + jnp.einsum("xycq,xypq->xycp", vectors[0], centre[0], precision=MID)
        full = full + jnp.einsum("xycq,xypq->xycp", extended[0][1], centre[1], precision=MID)
        for a, b in OFFSETS:
            if (a, b) != (0, 0):
                near = pick(own_view(extended[1], a, b), columns[(a, b)])
                parts[(a, b)] = jnp.einsum("kxycq,kxypq->xycp", near, blocks[(a, b)], precision=MID)
        full = full + jnp.concatenate([parts[(-1, 0)], parts[(1, 0)]], axis=-1)
        full = full + jnp.einsum(
            "xycp,pn->xycn", jnp.concatenate([parts[o] for o in narrow], axis=-1), scatter, precision=MID
        )
        return (full / hop_scale)[None]

    first_term = 2.0 * hop_terms(cur_vec, vec_ext) - prev_vec
    second_term = 2.0 * hop_terms(first_term, exchange(first_term)) - cur_vec
    return (first_term, second_term)


def solution(mesh):
    in_specs = (
        P("layer", "gx", "gy", None, None),
        P("layer", "gx", "gy", None, None),
        P("layer", "gx", "gy", None, None),
        P("layer", "gx", "gy", None),
    )
    out_specs = (P("layer", "gx", "gy", None, None), P("layer", "gx", "gy", None, None))
    return jax.shard_map(body, mesh=mesh, in_specs=in_specs, out_specs=out_specs, check_vma=False)
```

```python
import math

import jax
import jax.numpy as jnp
import numpy as np
from jax import lax
from jax.sharding import PartitionSpec as P

PATCH_X = 14
PATCH_Y = 4


v_pi = -2.7
v_sigma = 0.48
decay_len = 0.319
layer_gap = 3.35 / 1.42
cut_radius = 3.5
hop_scale = 12.0
twist_angle = 1.05 * math.pi / 180.0
root_three = math.sqrt(3.0)
cell_w = 4.0 * root_three
cell_h = 24.0
sigma_gain = v_sigma * math.exp((layer_gap - 1.0) / decay_len)
HI = lax.Precision.HIGHEST
MID = lax.Precision.HIGH
OFFSETS = [(a, b) for a in (-1, 0, 1) for b in (-1, 0, 1)]


def _base_np():
    orbital = np.arange(128)
    sub = orbital % 4
    cell = orbital // 4
    inner_x = np.where((sub == 1) | (sub == 2), root_three / 2.0, 0.0)
    inner_y = np.select([sub == 1, sub == 2, sub == 3], [0.5, 1.5, 2.0], 0.0)
    return np.stack([(cell // 8) * root_three + inner_x - cell_w / 2.0, (cell % 8) * 3.0 + inner_y - cell_h / 2.0])


def _reach_sets():
    base = _base_np()
    c, s = math.cos(twist_angle), math.sin(twist_angle)
    rot = np.array([[c, -s], [s, c]])
    margin = 0.5
    plane_r = cut_radius + margin
    inter_r = math.sqrt(cut_radius**2 - layer_gap**2) + margin
    twists = [
        np.array([[cell_w * (i - (PATCH_X - 1) / 2.0)], [cell_h * (j - (PATCH_Y - 1) / 2.0)]])
        for i in range(PATCH_X)
        for j in range(PATCH_Y)
    ]
    sets = {}
    for a, b in OFFSETS:
        shift = np.array([[a * cell_w], [b * cell_h]])
        gap = base[:, :, None] - base[:, None, :] - shift[:, :, None]
        mask = np.sqrt((gap**2).sum(0)) < plane_r
        for e in twists:
            turned = rot @ base + (rot - np.eye(2)) @ e
            for own, near in ((base, turned), (turned, base)):
                gap = own[:, :, None] - near[:, None, :] - shift[:, :, None]
                mask |= np.sqrt((gap**2).sum(0)) < inter_r
        sets[(a, b)] = (np.nonzero(mask.any(1))[0], np.nonzero(mask.any(0))[0])
    return sets


REACH = _reach_sets()


def _one_hot(idx):
    table = np.zeros((128, len(idx)), np.float32)
    table[idx, np.arange(len(idx))] = 1.0
    return table


def pick(x, idx):
    if len(idx) == x.shape[-1]:
        return x
    if np.all(np.diff(idx) == 1):
        return x[..., idx[0] : idx[0] + len(idx)]
    return jnp.einsum("...q,qk->...k", x, _one_hot(idx), precision=HI)


def extended_2(value, sides, width):
    for axis, dim in sides:
        devices, length = (lax.axis_size(axis), value.shape[dim])
        up = [(i, (i + 1) % devices) for i in range(devices)]
        down = [(j, i) for i, j in up]
        last = lax.slice_in_dim(value, length - width, length, axis=dim)
        first = lax.slice_in_dim(value, 0, width, axis=dim)
        if devices == 2:
            both = lax.ppermute(jnp.concatenate([last, first], axis=dim), axis, up)
            before = lax.slice_in_dim(both, 0, width, axis=dim)
            after = lax.slice_in_dim(both, width, 2 * width, axis=dim)
        else:
            before = lax.ppermute(last, axis, up)
            after = lax.ppermute(first, axis, down)
        value = jnp.concatenate([before, value, after], axis=dim)
    return value


def partner_2(value, axis, distance):
    return lax.ppermute(value, axis, [(i, i ^ 1 << distance) for i in range(lax.axis_size(axis))])


def lattice(cos_vals, sin_vals):
    base = jnp.asarray(_base_np(), jnp.float32)
    rot_x = cos_vals[:, None] * base[0] - sin_vals[:, None] * base[1]
    rot_y = sin_vals[:, None] * base[0] + cos_vals[:, None] * base[1]
    return jnp.stack([rot_x, rot_y], axis=1)


def twist_offsets(cos_vals, sin_vals, row_ids, col_ids):
    along_x = cell_w * ((row_ids % PATCH_X).astype(jnp.float32) - (PATCH_X - 1) / 2.0)
    along_y = cell_h * ((col_ids % PATCH_Y).astype(jnp.float32) - (PATCH_Y - 1) / 2.0)
    cos_less = (cos_vals - 1.0)[:, None, None]
    sin_cast = sin_vals[:, None, None]
    shift_x = cos_less * along_x[None, :, None] - sin_cast * along_y[None, None, :]
    shift_y = sin_cast * along_x[None, :, None] + cos_less * along_y[None, None, :]
    return jnp.stack([shift_x, shift_y], axis=-1)[..., None]


def taper(dist_sq):
    scaled = dist_sq / (cut_radius * cut_radius)
    return jnp.maximum(1.0 - scaled * scaled, 0.0)


def plane_block(own_pos, near_pos, shift_x, shift_y, self_rows):
    delta_x = own_pos[..., 0, :, None] - near_pos[..., 0, None, :] - shift_x
    delta_y = own_pos[..., 1, :, None] - near_pos[..., 1, None, :] - shift_y
    dist_sq = delta_x * delta_x + delta_y * delta_y
    spread = jnp.sqrt(dist_sq)
    hopping = v_pi * jnp.exp(-(spread - 1.0) / decay_len) * taper(dist_sq)
    if self_rows:
        orbital = jnp.arange(128, dtype=jnp.int32)
        hopping = jnp.where(orbital[:, None] == orbital[None, :], 0.0, hopping)
    return hopping


def inter_block(own_pos, near_pos, shift_x, shift_y):
    delta_x = own_pos[..., 0, :, None] - near_pos[..., 0, None, :] - shift_x
    delta_y = own_pos[..., 1, :, None] - near_pos[..., 1, None, :] - shift_y
    dist_sq = delta_x * delta_x + delta_y * delta_y + layer_gap * layer_gap
    spread = jnp.sqrt(dist_sq)
    cosine_sq = layer_gap * layer_gap / dist_sq
    decay = jnp.exp(-(spread - 1.0) / decay_len)
    bonds = decay * (v_pi * (1.0 - cosine_sq) + sigma_gain * cosine_sq)
    return bonds * taper(dist_sq)


def _halo_options(n):
    if n == 1:
        return [(0, ("last", "all", "first"))]
    if n == 2:
        return [(0, ("all",)), (1, ("last", "first"))]
    return [(-1, ("last",)), (0, ("all",)), (1, ("first",))]


def _region(value, kind, axis):
    length = value.shape[axis]
    if kind == "last":
        return lax.slice_in_dim(value, length - 1, length, axis=axis)
    if kind == "first":
        return lax.slice_in_dim(value, 0, 1, axis=axis)
    return value


def exchange(value):
    stacked = jnp.concatenate([value, partner_2(value, "layer", 0)], axis=0)
    axes = ("gx", "gy")
    sizes = [lax.axis_size(a) for a in axes]
    tile = {1: stacked.shape[1], 2: stacked.shape[2]}
    pieces = {}
    for step_x, kinds_x in _halo_options(sizes[0]):
        along_x = jnp.concatenate([_region(stacked, r, 1) for r in kinds_x], axis=1)
        for step_y, kinds_y in _halo_options(sizes[1]):
            part = jnp.concatenate([_region(along_x, r, 2) for r in kinds_y], axis=2)
            if (step_x, step_y) != (0, 0):
                pairs = []
                for x in range(sizes[0]):
                    for y in range(sizes[1]):
                        dst = ((x - step_x) % sizes[0]) * sizes[1] + (y - step_y) % sizes[1]
                        pairs.append((x * sizes[1] + y, dst))
                part = lax.ppermute(part, axes, pairs)
            at_x = 0
            for rx in kinds_x:
                wide_x = tile[1] if rx == "all" else 1
                at_y = 0
                for ry in kinds_y:
                    wide_y = tile[2] if ry == "all" else 1
                    pieces[(rx, ry)] = part[:, at_x : at_x + wide_x, at_y : at_y + wide_y]
                    at_y += wide_y
                at_x += wide_x
    order = ("last", "all", "first")
    rows = [jnp.concatenate([pieces[(rx, ry)] for ry in order], axis=2) for rx in order]
    return stacked, jnp.concatenate(rows, axis=1)


def body(prev_vec, cur_vec, displace, potential):
    layer_id = lax.axis_index("layer")
    tile_x = displace.shape[1]
    tile_y = displace.shape[2]
    cos_twist = math.cos(twist_angle)
    sin_twist = math.sin(twist_angle)
    width = cur_vec.shape[-2]
    packed = exchange(jnp.concatenate([cur_vec, displace], axis=-2))
    vec_ext = tuple(s[..., :width, :] for s in packed)
    own_disp, ext_disp = (s[..., width:, :] for s in packed)
    layer_up = layer_id == 1
    cos_vals = jnp.stack(
        [jnp.where(layer_up, cos_twist, 1.0), jnp.where(layer_up, 1.0, cos_twist)]
    ).astype(jnp.float32)
    sin_vals = jnp.stack(
        [jnp.where(layer_up, sin_twist, 0.0), jnp.where(layer_up, 0.0, sin_twist)]
    ).astype(jnp.float32)
    grid = lattice(cos_vals, sin_vals)[:, None, None]
    places = ext_disp + grid
    centre = own_disp + grid
    row_count = tile_x * lax.axis_size("gx")
    col_count = tile_y * lax.axis_size("gy")
    row_ids = (
        lax.axis_index("gx") * tile_x + jnp.arange(tile_x + 2, dtype=jnp.int32) - 1 + row_count
    ) % row_count
    col_ids = (
        lax.axis_index("gy") * tile_y + jnp.arange(tile_y + 2, dtype=jnp.int32) - 1 + col_count
    ) % col_count
    turn = twist_offsets(cos_vals, sin_vals, row_ids, col_ids)
    twisted = places + turn

    def own_view(value, a, b):
        return value[:, 1 + a : 1 + a + tile_x, 1 + b : 1 + b + tile_y]

    own_pos = centre[0]
    own_shift = own_view(turn[:1], 0, 0)[0]
    cos_own = cos_vals[0]
    sin_own = sin_vals[0]
    narrow = [o for o in OFFSETS if len(REACH[o][0]) < 64]
    narrow_rows = np.concatenate([REACH[o][0] for o in narrow])
    base_rows = jnp.asarray(_base_np()[:, narrow_rows], jnp.float32)
    grid_rows = jnp.stack(
        [cos_own * base_rows[0] - sin_own * base_rows[1], sin_own * base_rows[0] + cos_own * base_rows[1]]
    )
    picked = jnp.einsum("...q,qk->...k", own_disp[0], _one_hot(narrow_rows), precision=MID) + grid_rows
    blocks = {}
    columns = {}
    at = 0
    for a, b in OFFSETS:
        rows, cols = REACH[(a, b)]
        if len(rows) < 64:
            own_rows = picked[..., at : at + len(rows)]
            at += len(rows)
            cols = np.arange(128)
        else:
            own_rows = pick(own_pos, rows)
        shift_x = cos_own * (a * cell_w) - sin_own * (b * cell_h)
        shift_y = sin_own * (a * cell_w) + cos_own * (b * cell_h)
        if (a, b) == (0, 0):
            near_pos = centre[0]
            near_twist = centre[1] + own_view(turn[1:], 0, 0)[0]
        else:
            near_pos = pick(own_view(places[:1], a, b)[0], cols)
            near_twist = pick(own_view(twisted[1:], a, b)[0], cols)
        plane = plane_block(own_rows, near_pos, shift_x, shift_y, a == 0 and b == 0)
        inter = inter_block(own_rows + own_shift, near_twist, a * cell_w, b * cell_h)
        blocks[(a, b)] = jnp.stack([plane, inter])
        columns[(a, b)] = cols
    blocks = lax.optimization_barrier(blocks)

    scatter = np.zeros((len(narrow_rows), 128), np.float32)
    scatter[np.arange(len(narrow_rows)), narrow_rows] = 1.0

    def hop_terms(vectors, extended):
        full = potential[0][..., None, :] * vectors[0]
        parts = {}
        centre = blocks[(0, 0)]
        full = full + jnp.einsum("xycq,xypq->xycp", vectors[0], centre[0], precision=MID)
        full = full + jnp.einsum("xycq,xypq->xycp", extended[0][1], centre[1], precision=MID)
        for a, b in OFFSETS:
            if (a, b) != (0, 0):
                near = pick(own_view(extended[1], a, b), columns[(a, b)])
                parts[(a, b)] = jnp.einsum("kxycq,kxypq->xycp", near, blocks[(a, b)], precision=MID)
        full = full + jnp.concatenate([parts[(-1, 0)], parts[(1, 0)]], axis=-1)
        full = full + jnp.einsum(
            "xycp,pn->xycn", jnp.concatenate([parts[o] for o in narrow], axis=-1), scatter, precision=MID
        )
        return (full / hop_scale)[None]

    first_term = 2.0 * hop_terms(cur_vec, vec_ext) - prev_vec
    second_term = 2.0 * hop_terms(first_term, exchange(first_term)) - cur_vec
    return (first_term, second_term)


def solution(mesh):
    in_specs = (
        P("layer", "gx", "gy", None, None),
        P("layer", "gx", "gy", None, None),
        P("layer", "gx", "gy", None, None),
        P("layer", "gx", "gy", None),
    )
    out_specs = (P("layer", "gx", "gy", None, None), P("layer", "gx", "gy", None, None))
    return jax.shard_map(body, mesh=mesh, in_specs=in_specs, out_specs=out_specs, check_vma=False)
```

```python
import math

import jax
import jax.numpy as jnp
import numpy as np
from jax import lax
from jax.sharding import PartitionSpec as P

PATCH_X = 14
PATCH_Y = 4


v_pi = -2.7
v_sigma = 0.48
decay_len = 0.319
layer_gap = 3.35 / 1.42
cut_radius = 3.5
hop_scale = 12.0
twist_angle = 1.05 * math.pi / 180.0
root_three = math.sqrt(3.0)
cell_w = 4.0 * root_three
cell_h = 24.0
sigma_gain = v_sigma * math.exp((layer_gap - 1.0) / decay_len)
HI = lax.Precision.HIGHEST
MID = lax.Precision.HIGH
OFFSETS = [(a, b) for a in (-1, 0, 1) for b in (-1, 0, 1)]


def _base_np():
    orbital = np.arange(128)
    sub = orbital % 4
    cell = orbital // 4
    inner_x = np.where((sub == 1) | (sub == 2), root_three / 2.0, 0.0)
    inner_y = np.select([sub == 1, sub == 2, sub == 3], [0.5, 1.5, 2.0], 0.0)
    return np.stack([(cell // 8) * root_three + inner_x - cell_w / 2.0, (cell % 8) * 3.0 + inner_y - cell_h / 2.0])


def _reach_sets():
    base = _base_np()
    c, s = math.cos(twist_angle), math.sin(twist_angle)
    rot = np.array([[c, -s], [s, c]])
    margin = 0.5
    plane_r = cut_radius + margin
    inter_r = math.sqrt(cut_radius**2 - layer_gap**2) + margin
    twists = [
        np.array([[cell_w * (i - (PATCH_X - 1) / 2.0)], [cell_h * (j - (PATCH_Y - 1) / 2.0)]])
        for i in range(PATCH_X)
        for j in range(PATCH_Y)
    ]
    sets = {}
    for a, b in OFFSETS:
        shift = np.array([[a * cell_w], [b * cell_h]])
        gap = base[:, :, None] - base[:, None, :] - shift[:, :, None]
        mask = np.sqrt((gap**2).sum(0)) < plane_r
        for e in twists:
            turned = rot @ base + (rot - np.eye(2)) @ e
            for own, near in ((base, turned), (turned, base)):
                gap = own[:, :, None] - near[:, None, :] - shift[:, :, None]
                mask |= np.sqrt((gap**2).sum(0)) < inter_r
        sets[(a, b)] = (np.nonzero(mask.any(1))[0], np.nonzero(mask.any(0))[0])
    return sets


REACH = _reach_sets()


def _one_hot(idx):
    table = np.zeros((128, len(idx)), np.float32)
    table[idx, np.arange(len(idx))] = 1.0
    return table


def pick(x, idx):
    if len(idx) == x.shape[-1]:
        return x
    if np.all(np.diff(idx) == 1):
        return x[..., idx[0] : idx[0] + len(idx)]
    return jnp.einsum("...q,qk->...k", x, _one_hot(idx), precision=HI)


def extended_2(value, sides, width):
    for axis, dim in sides:
        devices, length = (lax.axis_size(axis), value.shape[dim])
        up = [(i, (i + 1) % devices) for i in range(devices)]
        down = [(j, i) for i, j in up]
        last = lax.slice_in_dim(value, length - width, length, axis=dim)
        first = lax.slice_in_dim(value, 0, width, axis=dim)
        if devices == 2:
            both = lax.ppermute(jnp.concatenate([last, first], axis=dim), axis, up)
            before = lax.slice_in_dim(both, 0, width, axis=dim)
            after = lax.slice_in_dim(both, width, 2 * width, axis=dim)
        else:
            before = lax.ppermute(last, axis, up)
            after = lax.ppermute(first, axis, down)
        value = jnp.concatenate([before, value, after], axis=dim)
    return value


def partner_2(value, axis, distance):
    return lax.ppermute(value, axis, [(i, i ^ 1 << distance) for i in range(lax.axis_size(axis))])


def lattice(cos_vals, sin_vals):
    base = jnp.asarray(_base_np(), jnp.float32)
    rot_x = cos_vals[:, None] * base[0] - sin_vals[:, None] * base[1]
    rot_y = sin_vals[:, None] * base[0] + cos_vals[:, None] * base[1]
    return jnp.stack([rot_x, rot_y], axis=1)


def twist_offsets(cos_vals, sin_vals, row_ids, col_ids):
    along_x = cell_w * ((row_ids % PATCH_X).astype(jnp.float32) - (PATCH_X - 1) / 2.0)
    along_y = cell_h * ((col_ids % PATCH_Y).astype(jnp.float32) - (PATCH_Y - 1) / 2.0)
    cos_less = (cos_vals - 1.0)[:, None, None]
    sin_cast = sin_vals[:, None, None]
    shift_x = cos_less * along_x[None, :, None] - sin_cast * along_y[None, None, :]
    shift_y = sin_cast * along_x[None, :, None] + cos_less * along_y[None, None, :]
    return jnp.stack([shift_x, shift_y], axis=-1)[..., None]


def taper(dist_sq):
    scaled = dist_sq / (cut_radius * cut_radius)
    return jnp.maximum(1.0 - scaled * scaled, 0.0)


def plane_block(own_pos, near_pos, shift_x, shift_y, self_rows):
    delta_x = own_pos[..., 0, :, None] - near_pos[..., 0, None, :] - shift_x
    delta_y = own_pos[..., 1, :, None] - near_pos[..., 1, None, :] - shift_y
    dist_sq = delta_x * delta_x + delta_y * delta_y
    spread = jnp.sqrt(dist_sq)
    hopping = v_pi * jnp.exp(-(spread - 1.0) / decay_len) * taper(dist_sq)
    if self_rows:
        orbital = jnp.arange(128, dtype=jnp.int32)
        hopping = jnp.where(orbital[:, None] == orbital[None, :], 0.0, hopping)
    return hopping


def inter_block(own_pos, near_pos, shift_x, shift_y):
    delta_x = own_pos[..., 0, :, None] - near_pos[..., 0, None, :] - shift_x
    delta_y = own_pos[..., 1, :, None] - near_pos[..., 1, None, :] - shift_y
    dist_sq = delta_x * delta_x + delta_y * delta_y + layer_gap * layer_gap
    spread = jnp.sqrt(dist_sq)
    cosine_sq = layer_gap * layer_gap / dist_sq
    decay = jnp.exp(-(spread - 1.0) / decay_len)
    bonds = decay * (v_pi * (1.0 - cosine_sq) + sigma_gain * cosine_sq)
    return bonds * taper(dist_sq)


def _halo_options(n):
    if n == 1:
        return [(0, ("last", "all", "first"))]
    if n == 2:
        return [(0, ("all",)), (1, ("last", "first"))]
    return [(-1, ("last",)), (0, ("all",)), (1, ("first",))]


def _region(value, kind, axis):
    length = value.shape[axis]
    if kind == "last":
        return lax.slice_in_dim(value, length - 1, length, axis=axis)
    if kind == "first":
        return lax.slice_in_dim(value, 0, 1, axis=axis)
    return value


def exchange(value):
    stacked = jnp.concatenate([value, partner_2(value, "layer", 0)], axis=0)
    axes = ("gx", "gy")
    sizes = [lax.axis_size(a) for a in axes]
    tile = {1: stacked.shape[1], 2: stacked.shape[2]}
    pieces = {}
    for step_x, kinds_x in _halo_options(sizes[0]):
        along_x = jnp.concatenate([_region(stacked, r, 1) for r in kinds_x], axis=1)
        for step_y, kinds_y in _halo_options(sizes[1]):
            part = jnp.concatenate([_region(along_x, r, 2) for r in kinds_y], axis=2)
            if (step_x, step_y) != (0, 0):
                pairs = []
                for x in range(sizes[0]):
                    for y in range(sizes[1]):
                        dst = ((x - step_x) % sizes[0]) * sizes[1] + (y - step_y) % sizes[1]
                        pairs.append((x * sizes[1] + y, dst))
                part = lax.ppermute(part, axes, pairs)
            at_x = 0
            for rx in kinds_x:
                wide_x = tile[1] if rx == "all" else 1
                at_y = 0
                for ry in kinds_y:
                    wide_y = tile[2] if ry == "all" else 1
                    pieces[(rx, ry)] = part[:, at_x : at_x + wide_x, at_y : at_y + wide_y]
                    at_y += wide_y
                at_x += wide_x
    order = ("last", "all", "first")
    rows = [jnp.concatenate([pieces[(rx, ry)] for ry in order], axis=2) for rx in order]
    return stacked, jnp.concatenate(rows, axis=1)


def body(prev_vec, cur_vec, displace, potential):
    layer_id = lax.axis_index("layer")
    tile_x = displace.shape[1]
    tile_y = displace.shape[2]
    cos_twist = math.cos(twist_angle)
    sin_twist = math.sin(twist_angle)
    width = cur_vec.shape[-2]
    packed = exchange(jnp.concatenate([cur_vec, displace], axis=-2))
    vec_ext = tuple(s[..., :width, :] for s in packed)
    own_disp, ext_disp = (s[..., width:, :] for s in packed)
    layer_up = layer_id == 1
    cos_vals = jnp.stack(
        [jnp.where(layer_up, cos_twist, 1.0), jnp.where(layer_up, 1.0, cos_twist)]
    ).astype(jnp.float32)
    sin_vals = jnp.stack(
        [jnp.where(layer_up, sin_twist, 0.0), jnp.where(layer_up, 0.0, sin_twist)]
    ).astype(jnp.float32)
    grid = lattice(cos_vals, sin_vals)[:, None, None]
    places = ext_disp + grid
    centre = own_disp + grid
    row_count = tile_x * lax.axis_size("gx")
    col_count = tile_y * lax.axis_size("gy")
    row_ids = (
        lax.axis_index("gx") * tile_x + jnp.arange(tile_x + 2, dtype=jnp.int32) - 1 + row_count
    ) % row_count
    col_ids = (
        lax.axis_index("gy") * tile_y + jnp.arange(tile_y + 2, dtype=jnp.int32) - 1 + col_count
    ) % col_count
    turn = twist_offsets(cos_vals, sin_vals, row_ids, col_ids)
    twisted = places + turn

    def own_view(value, a, b):
        return value[:, 1 + a : 1 + a + tile_x, 1 + b : 1 + b + tile_y]

    own_pos = centre[0]
    own_shift = own_view(turn[:1], 0, 0)[0]
    cos_own = cos_vals[0]
    sin_own = sin_vals[0]
    narrow = [o for o in OFFSETS if len(REACH[o][0]) < 64]
    narrow_rows = np.concatenate([REACH[o][0] for o in narrow])
    picked = jnp.einsum("...q,qk->...k", own_pos, _one_hot(narrow_rows), precision=HI)
    blocks = {}
    columns = {}
    at = 0
    for a, b in OFFSETS:
        rows, cols = REACH[(a, b)]
        if len(rows) < 64:
            own_rows = picked[..., at : at + len(rows)]
            at += len(rows)
            cols = np.arange(128)
        else:
            own_rows = pick(own_pos, rows)
        shift_x = cos_own * (a * cell_w) - sin_own * (b * cell_h)
        shift_y = sin_own * (a * cell_w) + cos_own * (b * cell_h)
        if (a, b) == (0, 0):
            near_pos = centre[0]
            near_twist = centre[1] + own_view(turn[1:], 0, 0)[0]
        else:
            near_pos = pick(own_view(places[:1], a, b)[0], cols)
            near_twist = pick(own_view(twisted[1:], a, b)[0], cols)
        plane = plane_block(own_rows, near_pos, shift_x, shift_y, a == 0 and b == 0)
        inter = inter_block(own_rows + own_shift, near_twist, a * cell_w, b * cell_h)
        blocks[(a, b)] = jnp.stack([plane, inter])
        columns[(a, b)] = cols
    pairs = (((0, -1), (0, 1)), ((-1, -1), (-1, 1)), ((1, -1), (1, 1)))
    for first, second in pairs:
        assert len(REACH[first][0]) == len(REACH[second][0])
        blocks[first] = jnp.stack([blocks[first], blocks.pop(second)])
    blocks = lax.optimization_barrier(blocks)

    scatter = np.zeros((len(narrow_rows), 128), np.float32)
    scatter[np.arange(len(narrow_rows)), narrow_rows] = 1.0

    def hop_terms(vectors, extended):
        full = potential[0][..., None, :] * vectors[0]
        parts = {}
        centre = blocks[(0, 0)]
        full = full + jnp.einsum("xycq,xypq->xycp", vectors[0], centre[0], precision=MID)
        full = full + jnp.einsum("xycq,xypq->xycp", extended[0][1], centre[1], precision=MID)
        for a, b in ((-1, 0), (1, 0)):
            near = pick(own_view(extended[1], a, b), columns[(a, b)])
            parts[(a, b)] = jnp.einsum("kxycq,kxypq->xycp", near, blocks[(a, b)], precision=MID)
        for first, second in pairs:
            near = jnp.stack([own_view(extended[1], *first), own_view(extended[1], *second)])
            both = jnp.einsum("okxycq,okxypq->oxycp", near, blocks[first], precision=MID)
            parts[first], parts[second] = both[0], both[1]
        full = full + jnp.concatenate([parts[(-1, 0)], parts[(1, 0)]], axis=-1)
        full = full + jnp.einsum(
            "xycp,pn->xycn", jnp.concatenate([parts[o] for o in narrow], axis=-1), scatter, precision=MID
        )
        return (full / hop_scale)[None]

    first_term = 2.0 * hop_terms(cur_vec, vec_ext) - prev_vec
    second_term = 2.0 * hop_terms(first_term, exchange(first_term)) - cur_vec
    return (first_term, second_term)


def solution(mesh):
    in_specs = (
        P("layer", "gx", "gy", None, None),
        P("layer", "gx", "gy", None, None),
        P("layer", "gx", "gy", None, None),
        P("layer", "gx", "gy", None),
    )
    out_specs = (P("layer", "gx", "gy", None, None), P("layer", "gx", "gy", None, None))
    return jax.shard_map(body, mesh=mesh, in_specs=in_specs, out_specs=out_specs, check_vma=False)
```

```python
import math

import jax
import jax.numpy as jnp
import numpy as np
from jax import lax
from jax.sharding import PartitionSpec as P

PATCH_X = 14
PATCH_Y = 4


v_pi = -2.7
v_sigma = 0.48
decay_len = 0.319
layer_gap = 3.35 / 1.42
cut_radius = 3.5
hop_scale = 12.0
twist_angle = 1.05 * math.pi / 180.0
root_three = math.sqrt(3.0)
cell_w = 4.0 * root_three
cell_h = 24.0
sigma_gain = v_sigma * math.exp((layer_gap - 1.0) / decay_len)
HI = lax.Precision.HIGHEST
MID = lax.Precision.HIGH
OFFSETS = [(a, b) for a in (-1, 0, 1) for b in (-1, 0, 1)]


def _base_np():
    orbital = np.arange(128)
    sub = orbital % 4
    cell = orbital // 4
    inner_x = np.where((sub == 1) | (sub == 2), root_three / 2.0, 0.0)
    inner_y = np.select([sub == 1, sub == 2, sub == 3], [0.5, 1.5, 2.0], 0.0)
    return np.stack([(cell // 8) * root_three + inner_x - cell_w / 2.0, (cell % 8) * 3.0 + inner_y - cell_h / 2.0])


def _reach_sets():
    base = _base_np()
    c, s = math.cos(twist_angle), math.sin(twist_angle)
    rot = np.array([[c, -s], [s, c]])
    margin = 0.5
    plane_r = cut_radius + margin
    inter_r = math.sqrt(cut_radius**2 - layer_gap**2) + margin
    twists = [
        np.array([[cell_w * (i - (PATCH_X - 1) / 2.0)], [cell_h * (j - (PATCH_Y - 1) / 2.0)]])
        for i in range(PATCH_X)
        for j in range(PATCH_Y)
    ]
    sets = {}
    for a, b in OFFSETS:
        shift = np.array([[a * cell_w], [b * cell_h]])
        gap = base[:, :, None] - base[:, None, :] - shift[:, :, None]
        mask = np.sqrt((gap**2).sum(0)) < plane_r
        for e in twists:
            turned = rot @ base + (rot - np.eye(2)) @ e
            for own, near in ((base, turned), (turned, base)):
                gap = own[:, :, None] - near[:, None, :] - shift[:, :, None]
                mask |= np.sqrt((gap**2).sum(0)) < inter_r
        sets[(a, b)] = (np.nonzero(mask.any(1))[0], np.nonzero(mask.any(0))[0])
    return sets


REACH = _reach_sets()


def _one_hot(idx):
    table = np.zeros((128, len(idx)), np.float32)
    table[idx, np.arange(len(idx))] = 1.0
    return table


def pick(x, idx):
    if len(idx) == x.shape[-1]:
        return x
    if np.all(np.diff(idx) == 1):
        return x[..., idx[0] : idx[0] + len(idx)]
    return jnp.einsum("...q,qk->...k", x, _one_hot(idx), precision=HI)


def extended_2(value, sides, width):
    for axis, dim in sides:
        devices, length = (lax.axis_size(axis), value.shape[dim])
        up = [(i, (i + 1) % devices) for i in range(devices)]
        down = [(j, i) for i, j in up]
        last = lax.slice_in_dim(value, length - width, length, axis=dim)
        first = lax.slice_in_dim(value, 0, width, axis=dim)
        if devices == 2:
            both = lax.ppermute(jnp.concatenate([last, first], axis=dim), axis, up)
            before = lax.slice_in_dim(both, 0, width, axis=dim)
            after = lax.slice_in_dim(both, width, 2 * width, axis=dim)
        else:
            before = lax.ppermute(last, axis, up)
            after = lax.ppermute(first, axis, down)
        value = jnp.concatenate([before, value, after], axis=dim)
    return value


def partner_2(value, axis, distance):
    return lax.ppermute(value, axis, [(i, i ^ 1 << distance) for i in range(lax.axis_size(axis))])


def lattice(cos_vals, sin_vals):
    base = jnp.asarray(_base_np(), jnp.float32)
    rot_x = cos_vals[:, None] * base[0] - sin_vals[:, None] * base[1]
    rot_y = sin_vals[:, None] * base[0] + cos_vals[:, None] * base[1]
    return jnp.stack([rot_x, rot_y], axis=1)


def twist_offsets(cos_vals, sin_vals, row_ids, col_ids):
    along_x = cell_w * ((row_ids % PATCH_X).astype(jnp.float32) - (PATCH_X - 1) / 2.0)
    along_y = cell_h * ((col_ids % PATCH_Y).astype(jnp.float32) - (PATCH_Y - 1) / 2.0)
    cos_less = (cos_vals - 1.0)[:, None, None]
    sin_cast = sin_vals[:, None, None]
    shift_x = cos_less * along_x[None, :, None] - sin_cast * along_y[None, None, :]
    shift_y = sin_cast * along_x[None, :, None] + cos_less * along_y[None, None, :]
    return jnp.stack([shift_x, shift_y], axis=-1)[..., None]


def taper(dist_sq):
    scaled = dist_sq / (cut_radius * cut_radius)
    return jnp.maximum(1.0 - scaled * scaled, 0.0)


def plane_block(own_pos, near_pos, shift_x, shift_y, self_rows):
    delta_x = own_pos[..., 0, :, None] - near_pos[..., 0, None, :] - shift_x
    delta_y = own_pos[..., 1, :, None] - near_pos[..., 1, None, :] - shift_y
    dist_sq = delta_x * delta_x + delta_y * delta_y
    spread = jnp.sqrt(dist_sq)
    hopping = v_pi * jnp.exp(-(spread - 1.0) / decay_len) * taper(dist_sq)
    if self_rows:
        orbital = jnp.arange(128, dtype=jnp.int32)
        hopping = jnp.where(orbital[:, None] == orbital[None, :], 0.0, hopping)
    return hopping


def inter_block(own_pos, near_pos, shift_x, shift_y):
    delta_x = own_pos[..., 0, :, None] - near_pos[..., 0, None, :] - shift_x
    delta_y = own_pos[..., 1, :, None] - near_pos[..., 1, None, :] - shift_y
    dist_sq = delta_x * delta_x + delta_y * delta_y + layer_gap * layer_gap
    spread = jnp.sqrt(dist_sq)
    cosine_sq = layer_gap * layer_gap / dist_sq
    decay = jnp.exp(-(spread - 1.0) / decay_len)
    bonds = decay * (v_pi * (1.0 - cosine_sq) + sigma_gain * cosine_sq)
    return bonds * taper(dist_sq)


def _halo_options(n):
    if n == 1:
        return [(0, ("last", "all", "first"))]
    if n == 2:
        return [(0, ("all",)), (1, ("last", "first"))]
    return [(-1, ("last",)), (0, ("all",)), (1, ("first",))]


def _region(value, kind, axis):
    length = value.shape[axis]
    if kind == "last":
        return lax.slice_in_dim(value, length - 1, length, axis=axis)
    if kind == "first":
        return lax.slice_in_dim(value, 0, 1, axis=axis)
    return value


def exchange(value):
    stacked = jnp.concatenate([value, partner_2(value, "layer", 0)], axis=0)
    axes = ("gx", "gy")
    sizes = [lax.axis_size(a) for a in axes]
    tile = {1: stacked.shape[1], 2: stacked.shape[2]}
    pieces = {}
    for step_x, kinds_x in _halo_options(sizes[0]):
        along_x = jnp.concatenate([_region(stacked, r, 1) for r in kinds_x], axis=1)
        for step_y, kinds_y in _halo_options(sizes[1]):
            part = jnp.concatenate([_region(along_x, r, 2) for r in kinds_y], axis=2)
            if (step_x, step_y) != (0, 0):
                pairs = []
                for x in range(sizes[0]):
                    for y in range(sizes[1]):
                        dst = ((x - step_x) % sizes[0]) * sizes[1] + (y - step_y) % sizes[1]
                        pairs.append((x * sizes[1] + y, dst))
                part = lax.ppermute(part, axes, pairs)
            at_x = 0
            for rx in kinds_x:
                wide_x = tile[1] if rx == "all" else 1
                at_y = 0
                for ry in kinds_y:
                    wide_y = tile[2] if ry == "all" else 1
                    pieces[(rx, ry)] = part[:, at_x : at_x + wide_x, at_y : at_y + wide_y]
                    at_y += wide_y
                at_x += wide_x
    order = ("last", "all", "first")
    rows = [jnp.concatenate([pieces[(rx, ry)] for ry in order], axis=2) for rx in order]
    return stacked, jnp.concatenate(rows, axis=1)


def body(prev_vec, cur_vec, displace, potential):
    layer_id = lax.axis_index("layer")
    tile_x = displace.shape[1]
    tile_y = displace.shape[2]
    cos_twist = math.cos(twist_angle)
    sin_twist = math.sin(twist_angle)
    width = cur_vec.shape[-2]
    packed = exchange(jnp.concatenate([cur_vec, displace], axis=-2))
    vec_ext = tuple(s[..., :width, :] for s in packed)
    own_disp, ext_disp = (s[..., width:, :] for s in packed)
    layer_up = layer_id == 1
    cos_vals = jnp.stack(
        [jnp.where(layer_up, cos_twist, 1.0), jnp.where(layer_up, 1.0, cos_twist)]
    ).astype(jnp.float32)
    sin_vals = jnp.stack(
        [jnp.where(layer_up, sin_twist, 0.0), jnp.where(layer_up, 0.0, sin_twist)]
    ).astype(jnp.float32)
    grid = lattice(cos_vals, sin_vals)[:, None, None]
    places = ext_disp + grid
    centre = own_disp + grid
    row_count = tile_x * lax.axis_size("gx")
    col_count = tile_y * lax.axis_size("gy")
    row_ids = (
        lax.axis_index("gx") * tile_x + jnp.arange(tile_x + 2, dtype=jnp.int32) - 1 + row_count
    ) % row_count
    col_ids = (
        lax.axis_index("gy") * tile_y + jnp.arange(tile_y + 2, dtype=jnp.int32) - 1 + col_count
    ) % col_count
    turn = twist_offsets(cos_vals, sin_vals, row_ids, col_ids)
    twisted = places + turn

    def own_view(value, a, b):
        return value[:, 1 + a : 1 + a + tile_x, 1 + b : 1 + b + tile_y]

    own_pos = centre[0]
    own_shift = own_view(turn[:1], 0, 0)[0]
    cos_own = cos_vals[0]
    sin_own = sin_vals[0]
    narrow = [o for o in OFFSETS if len(REACH[o][0]) < 64]
    narrow_rows = np.concatenate([REACH[o][0] for o in narrow])
    picked = jnp.einsum("...q,qk->...k", own_pos, _one_hot(narrow_rows), precision=HI)
    blocks = {}
    columns = {}
    at = 0
    for a, b in OFFSETS:
        rows, cols = REACH[(a, b)]
        if len(rows) < 64:
            own_rows = picked[..., at : at + len(rows)]
            at += len(rows)
            cols = np.arange(128)
        else:
            own_rows = pick(own_pos, rows)
        shift_x = cos_own * (a * cell_w) - sin_own * (b * cell_h)
        shift_y = sin_own * (a * cell_w) + cos_own * (b * cell_h)
        if (a, b) == (0, 0):
            near_pos = centre[0]
            near_twist = centre[1] + own_view(turn[1:], 0, 0)[0]
        else:
            near_pos = pick(own_view(places[:1], a, b)[0], cols)
            near_twist = pick(own_view(twisted[1:], a, b)[0], cols)
        plane = plane_block(own_rows, near_pos, shift_x, shift_y, a == 0 and b == 0)
        inter = inter_block(own_rows + own_shift, near_twist, a * cell_w, b * cell_h)
        blocks[(a, b)] = jnp.stack([plane, inter])
        columns[(a, b)] = cols
    for o in ((-1, 0), (1, 0)):
        lo = int(columns[o][0])
        assert list(columns[o]) == list(range(lo, lo + 64))
        fill = [(0, 0)] * (blocks[o].ndim - 1) + [(lo, 128 - 64 - lo)]
        blocks[o] = jnp.pad(blocks[o], fill)
        columns[o] = np.arange(128)
    blocks = lax.optimization_barrier(blocks)

    scatter = np.zeros((len(narrow_rows), 128), np.float32)
    scatter[np.arange(len(narrow_rows)), narrow_rows] = 1.0

    def hop_terms(vectors, extended):
        full = potential[0][..., None, :] * vectors[0]
        parts = {}
        centre = blocks[(0, 0)]
        full = full + jnp.einsum("xycq,xypq->xycp", vectors[0], centre[0], precision=MID)
        full = full + jnp.einsum("xycq,xypq->xycp", extended[0][1], centre[1], precision=MID)
        for a, b in OFFSETS:
            if (a, b) != (0, 0):
                near = pick(own_view(extended[1], a, b), columns[(a, b)])
                parts[(a, b)] = jnp.einsum("kxycq,kxypq->xycp", near, blocks[(a, b)], precision=MID)
        full = full + jnp.concatenate([parts[(-1, 0)], parts[(1, 0)]], axis=-1)
        full = full + jnp.einsum(
            "xycp,pn->xycn", jnp.concatenate([parts[o] for o in narrow], axis=-1), scatter, precision=MID
        )
        return (full / hop_scale)[None]

    first_term = 2.0 * hop_terms(cur_vec, vec_ext) - prev_vec
    second_term = 2.0 * hop_terms(first_term, exchange(first_term)) - cur_vec
    return (first_term, second_term)


def solution(mesh):
    in_specs = (
        P("layer", "gx", "gy", None, None),
        P("layer", "gx", "gy", None, None),
        P("layer", "gx", "gy", None, None),
        P("layer", "gx", "gy", None),
    )
    out_specs = (P("layer", "gx", "gy", None, None), P("layer", "gx", "gy", None, None))
    return jax.shard_map(body, mesh=mesh, in_specs=in_specs, out_specs=out_specs, check_vma=False)
```
